256 devices in a mesh: lat: 16 (over y_hi, x, core), lon: 16 (over z, y_lo).
Axes of the slice: x: 4, y: 4 (y_hi: 2, y_lo: 2; y = y_hi * 2 + y_lo), z: 8, core: 2. Of those that a mesh axis runs over, the one named last changes fastest.
Arguments:
- queries: bfloat16 [256, 256, 1024], P('lat', 'lon'), may hold values from -80 to 80
- keys: bfloat16 [256, 256, 1024], P('lat', 'lon'), may hold values from -6 to 6
- values: bfloat16 [256, 256, 1024], P('lat', 'lon'), may hold values from -6 to 6
- grad_out: bfloat16 [256, 256, 1024], P('lat', 'lon'), may hold values from -6 to 6
- fold_cols: int32 [2, 256], replicated, may hold values from 0 to 255, as said below
Outputs:
- grad_queries: bfloat16 [256, 256, 1024], P('lat', 'lon')
- grad_keys: bfloat16 [256, 256, 1024], P('lat', 'lon')
- grad_values: bfloat16 [256, 256, 1024], P('lat', 'lon')
The draws below stay inside these ranges and needn't reach their ends.
Inputs may be any that keep to these rules, and one draw needn't show every extreme that they name: Each row of fold_cols maps, for every block b of 16 columns, the runs [b * 16, b * 16 + 4), [b * 16 + 4, (b + 1) * 16 - 4) and [(b + 1) * 16 - 4, (b + 1) * 16) one to one onto the same runs of the block 8 blocks further on the loop.
All inputs are finite; a program needn't handle non-finite values.
Results may differ from the reference program's by a relative error of at most 0.0075.
Values may be sent and summed in bfloat16 or wider, within the bound.
No kernel may reach another device: no remote copies, remote signals or barrier semaphores. Data moves between devices by JAX's collectives and lax.ppermute only.
A program may use at most 128 MiB of HBM per device.

```python
import jax
import jax.numpy as jnp
from jax import lax

HEADS = 16
HEAD_DIM = 64
WIDTH = 1024
RADIUS = 4
TW = 16
NLAT = 256
NLON = 256


def query_key_pair(key):
    grid_shape = (NLAT, NLON, WIDTH)
    base_keys = jax.random.truncated_normal(jax.random.fold_in(key, 101), -6.0, 6.0, grid_shape, jnp.float32)
    base_queries = jax.random.truncated_normal(jax.random.fold_in(key, 102), -6.0, 6.0, grid_shape, jnp.float32)
    return (base_queries, base_keys)


def draw_queries(key, part):
    return query_key_pair(key)[0].astype(jnp.bfloat16)


def draw_keys(key, part):
    return query_key_pair(key)[1].astype(jnp.bfloat16)


def draw_fold_cols(key, part):
    columns = jnp.arange(NLON, dtype=jnp.int32)
    block_index = columns // TW
    within = columns % TW
    segment = block_index * 3 + (within >= 4).astype(jnp.int32) + (within >= TW - 4).astype(jnp.int32)
    offset_start = jnp.where(within < 4, 0, jnp.where(within < TW - 4, 4, TW - 4))
    block_count = NLON // TW
    target_block = (block_index + block_count // 2) % block_count
    same_segment = segment[:, None] == segment[None, :]
    result_rows = []
    for pole_side in range(2):
        ranking = jax.random.randint(jax.random.fold_in(key, 201 + pole_side), (NLON,), 0, 1 << 16) * NLON + columns
        position = jnp.sum(same_segment & (ranking[None, :] < ranking[:, None]), axis=1).astype(jnp.int32)
        result_rows.append(target_block * TW + offset_start + position)
    return jnp.stack(result_rows).astype(jnp.int32)


def level_of(rng, shape, cuts, least, top_value):
    def one(axis_at, blocks):
        draws = jax.random.uniform(jax.random.fold_in(jax.random.fold_in(rng, 6), axis_at), (blocks,), jnp.float32, least / len(cuts), top_value / len(cuts))
        return jnp.repeat(jnp.exp(draws), shape[axis_at] // blocks).reshape((-1,) + (1,) * (len(shape) - axis_at - 1))

    factor_of = one(*cuts[0])
    for cut in cuts[1:]:
        factor_of = factor_of * one(*cut)
    return factor_of


def centred(key, dims, scale, most, cuts=(), kind=jnp.bfloat16):
    values = scale * jax.random.normal(key, dims, jnp.float32)
    if cuts:
        values = values * level_of(key, dims, cuts, -0.22, 0.18)
    return jnp.clip(values, -most, most).astype(kind)


def setup_inputs(seed: int = 0) -> dict:
    arg_keys = jax.random.split(jax.random.key(seed), 6)
    return {
        "queries": draw_queries(jax.random.fold_in(arg_keys[5], 71), 0),
        "keys": draw_keys(jax.random.fold_in(arg_keys[5], 71), 0),
        "values": centred(arg_keys[2], (NLAT, NLON, WIDTH), 1.0, 6.0, ((0, 16), (1, 16))),
        "grad_out": centred(arg_keys[3], (NLAT, NLON, WIDTH), 1.0, 6.0, ((0, 16), (1, 16))),
        "fold_cols": draw_fold_cols(jax.random.fold_in(arg_keys[5], 71), 0),
    }


band_rows = 8

def pad_grid(source, fold_cols):
    lat_rows = source.shape[0]
    lon_cols = source.shape[1]
    columns = ((jnp.arange(lon_cols + 2 * RADIUS) - RADIUS) % lon_cols).astype(jnp.int32)
    middle = jnp.take(source, columns, axis=1)
    north_cols = jnp.take(fold_cols[0], columns).astype(jnp.int32)
    south_cols = jnp.take(fold_cols[1], columns).astype(jnp.int32)
    north_rows = jnp.take(source[:RADIUS][::-1], north_cols, axis=1)
    south_rows = jnp.take(source[lat_rows - RADIUS:][::-1], south_cols, axis=1)
    return jnp.concatenate([north_rows, middle, south_rows], axis=0)

def reference(queries, keys, values, grad_out, fold_cols):
    score_scale = HEAD_DIM ** (-0.5)
    lat_rows, lon_cols, features = queries.shape
    key_pad = pad_grid(keys, fold_cols)
    value_pad = pad_grid(values, fold_cols)
    span = 2 * RADIUS + 1
    offsets = [(shift_row, shift_col) for shift_row in range(span) for shift_col in range(span)]
    halo_rows = band_rows + 2 * RADIUS

    def split_heads(array_block):
        return array_block.astype(jnp.float32).reshape(array_block.shape[0], array_block.shape[1], HEADS, HEAD_DIM)

    def nearby(array_block, shift_row, shift_col):
        return array_block[shift_row:shift_row + band_rows, shift_col:shift_col + lon_cols]

    def band_step(running, band_index):
        key_grad, value_grad = running
        first_row = (band_index * band_rows).astype(jnp.int32)
        query_band = split_heads(lax.dynamic_slice_in_dim(queries, first_row, band_rows, 0))
        grad_band = split_heads(lax.dynamic_slice_in_dim(grad_out, first_row, band_rows, 0))
        key_band = split_heads(lax.dynamic_slice_in_dim(key_pad, first_row, halo_rows, 0))
        value_band = split_heads(lax.dynamic_slice_in_dim(value_pad, first_row, halo_rows, 0))
        scores = jnp.stack([lax.optimization_barrier(jnp.sum(query_band * nearby(key_band, shift_row, shift_col), axis=-1)) for shift_row, shift_col in offsets]) * score_scale
        row_max = lax.optimization_barrier(jnp.max(scores, axis=0))
        log_total = row_max + jnp.log(lax.optimization_barrier(jnp.sum(jnp.exp(scores - row_max), axis=0)))
        weights = jnp.exp(scores - log_total)
        dweights = jnp.stack([lax.optimization_barrier(jnp.sum(grad_band * nearby(value_band, shift_row, shift_col), axis=-1)) for shift_row, shift_col in offsets])
        correction = lax.optimization_barrier(jnp.sum(weights * dweights, axis=0))
        dscores = lax.optimization_barrier((weights * (dweights - correction)).astype(jnp.bfloat16)).astype(jnp.float32)
        weights_low = lax.optimization_barrier(weights.astype(jnp.bfloat16)).astype(jnp.float32)
        query_grad = jnp.zeros((band_rows, lon_cols, HEADS, HEAD_DIM), jnp.float32)
        key_part = jnp.zeros((halo_rows, lon_cols + 2 * RADIUS, HEADS, HEAD_DIM), jnp.float32)
        value_part = jnp.zeros((halo_rows, lon_cols + 2 * RADIUS, HEADS, HEAD_DIM), jnp.float32)
        for position, (shift_row, shift_col) in enumerate(offsets):
            query_grad = query_grad + dscores[position][..., None] * nearby(key_band, shift_row, shift_col)
            key_part = key_part.at[shift_row:shift_row + band_rows, shift_col:shift_col + lon_cols].add(dscores[position][..., None] * query_band)
            value_part = value_part.at[shift_row:shift_row + band_rows, shift_col:shift_col + lon_cols].add(weights_low[position][..., None] * grad_band)
        key_slab = lax.dynamic_slice_in_dim(key_grad, first_row, halo_rows, 0) + score_scale * key_part.reshape(halo_rows, lon_cols + 2 * RADIUS, features)
        value_slab = lax.dynamic_slice_in_dim(value_grad, first_row, halo_rows, 0) + value_part.reshape(halo_rows, lon_cols + 2 * RADIUS, features)
        key_grad = lax.dynamic_update_slice_in_dim(key_grad, key_slab, first_row, 0)
        value_grad = lax.dynamic_update_slice_in_dim(value_grad, value_slab, first_row, 0)
        return ((key_grad, value_grad), (score_scale * query_grad).reshape(band_rows, lon_cols, features))
    pad_shape = (lat_rows + 2 * RADIUS, lon_cols + 2 * RADIUS, features)
    start_grads = (jnp.zeros(pad_shape, jnp.float32), jnp.zeros(pad_shape, jnp.float32))
    (key_grad, value_grad), query_grads = lax.scan(band_step, start_grads, jnp.arange(lat_rows // band_rows))
    _, pull_back = jax.vjp(lambda source: pad_grid(source, fold_cols), jnp.zeros((lat_rows, lon_cols, features), jnp.float32))
    grad_keys = pull_back(key_grad)[0]
    grad_values = pull_back(value_grad)[0]
    grad_queries = query_grads.reshape(lat_rows, lon_cols, features)
    return (grad_queries.astype(jnp.bfloat16), grad_keys.astype(jnp.bfloat16), grad_values.astype(jnp.bfloat16))
```

```python
import jax
import jax.numpy as jnp
from jax import lax
from jax.experimental import pallas as pl
from jax.experimental.pallas import tpu as pltpu
from jax.sharding import PartitionSpec as P

HEADS = 16
HEAD_DIM = 64
RADIUS = 4

SPAN = 2 * RADIUS + 1
TILE_ROWS = 8
LANES = 128


def attention_kernel(width, q_ref, g_ref, k_ref, v_ref, dq_ref, dk_ref, dv_ref, bias_ref):
    scale = HEAD_DIM ** (-0.5)
    ext_w = width + 2 * RADIUS
    tq = TILE_ROWS * width
    tk = (TILE_ROWS + 2 * RADIUS) * ext_w
    step_k = TILE_ROWS * ext_w
    tiles = q_ref.shape[0] // tq
    pairs = q_ref.shape[1] // LANES

    qi = lax.broadcasted_iota(jnp.int32, (tq, tk), 0).astype(jnp.float32)
    ki = lax.broadcasted_iota(jnp.int32, (tq, tk), 1).astype(jnp.float32)
    qr = jnp.floor((qi + 0.5) * (1.0 / width))
    qc = qi - width * qr
    kr = jnp.floor((ki + 0.5) * (1.0 / ext_w))
    kc = ki - ext_w * kr
    dr = kr - qr
    dc = kc - qc
    ok = (dr >= 0) & (dr <= 2 * RADIUS) & (dc >= 0) & (dc <= 2 * RADIUS)
    bias_ref[...] = jnp.where(ok, 0.0, -jnp.inf).astype(jnp.float32)

    nt = (((1,), (1,)), ((), ()))
    tn = (((0,), (0,)), ((), ()))

    def head(qh, gh, kp, vp):
        s = lax.dot_general(qh, kp, nt, preferred_element_type=jnp.float32) * scale + bias_ref[...]
        m = jnp.max(s, axis=1, keepdims=True)
        e = jnp.exp(s - m)
        total = jnp.sum(e, axis=1, keepdims=True)
        w = e * (1.0 / total)
        dw = lax.dot_general(gh, vp, nt, preferred_element_type=jnp.float32)
        corr = jnp.sum(w * dw, axis=1, keepdims=True)
        ds = (w * (dw - corr)).astype(jnp.bfloat16)
        return ds, w.astype(jnp.bfloat16)

    def body(p, carry):
        lanes = pl.ds(pl.multiple_of(p * LANES, LANES), LANES)
        for t in range(tiles):
            qp = q_ref[pl.ds(t * tq, tq), lanes]
            gp = g_ref[pl.ds(t * tq, tq), lanes]
            kp = k_ref[pl.ds(t * step_k, tk), lanes]
            vp = v_ref[pl.ds(t * step_k, tk), lanes]
            lo = lax.broadcasted_iota(jnp.int32, qp.shape, 1) < HEAD_DIM
            zero = jnp.zeros_like(qp)
            qa = jnp.where(lo, qp, zero)
            qb = jnp.where(lo, zero, qp)
            ga = jnp.where(lo, gp, zero)
            gb = jnp.where(lo, zero, gp)
            dsa, wa = head(qa, ga, kp, vp)
            dsb, wb = head(qb, gb, kp, vp)
            dqa = jnp.dot(dsa, kp, preferred_element_type=jnp.float32)
            dqb = jnp.dot(dsb, kp, preferred_element_type=jnp.float32)
            dq = jnp.where(lo, dqa, dqb) * scale
            dq_ref[pl.ds(t * tq, tq), lanes] = dq.astype(dq_ref.dtype)
            dk = (
                lax.dot_general(dsa, qa, tn, preferred_element_type=jnp.float32)
                + lax.dot_general(dsb, qb, tn, preferred_element_type=jnp.float32)
            ) * scale
            dv = lax.dot_general(wa, ga, tn, preferred_element_type=jnp.float32) + lax.dot_general(
                wb, gb, tn, preferred_element_type=jnp.float32
            )
            if t == 0:
                dk_ref[pl.ds(0, tk), lanes] = dk
                dv_ref[pl.ds(0, tk), lanes] = dv
            else:
                shared = tk - step_k
                base = t * step_k
                dk_ref[pl.ds(base, shared), lanes] += dk[:shared]
                dv_ref[pl.ds(base, shared), lanes] += dv[:shared]
                dk_ref[pl.ds(base + shared, step_k), lanes] = dk[shared:]
                dv_ref[pl.ds(base + shared, step_k), lanes] = dv[shared:]
        return carry

    lax.fori_loop(0, pairs, body, 0)


def attention_core(q2, g2, k2, v2, width):
    cells, features = q2.shape
    ext_cells = k2.shape[0]
    ext_w = width + 2 * RADIUS
    tq = TILE_ROWS * width
    tk = (TILE_ROWS + 2 * RADIUS) * ext_w
    tiles = cells // tq
    flops = 10 * 2 * tq * tk * LANES * (features // LANES) * tiles
    vmem = pl.BlockSpec(memory_space=pltpu.VMEM)
    return pl.pallas_call(
        lambda *refs: attention_kernel(width, *refs),
        out_shape=(
            jax.ShapeDtypeStruct((cells, features), jnp.bfloat16),
            jax.ShapeDtypeStruct((ext_cells, features), jnp.float32),
            jax.ShapeDtypeStruct((ext_cells, features), jnp.float32),
        ),
        in_specs=[vmem] * 4,
        out_specs=(vmem, vmem, vmem),
        scratch_shapes=[pltpu.VMEM((tq, tk), jnp.float32)],
        cost_estimate=pl.CostEstimate(
            flops=flops,
            transcendentals=2 * tq * tk * HEADS * tiles,
            bytes_accessed=2 * (2 * cells * features) + 2 * (2 * ext_cells * features)
            + 2 * cells * features + 2 * 4 * ext_cells * features,
        ),
        name="neighbourhood_attention_bwd",
    )(q2, g2, k2, v2)


def on_device(queries, keys, values, grad_out, fold_cols):
    height, width, features = queries.shape
    n_lat = lax.axis_size("lat")
    n_lon = lax.axis_size("lon")
    half = n_lon // 2
    i = lax.axis_index("lat")
    j = lax.axis_index("lon")
    at_north = i == 0
    at_south = i == n_lat - 1
    partner_j = (j + half) % n_lon
    r = RADIUS

    def flat(a, b):
        return a * n_lon + b

    down_pairs = [(flat(a, b), flat(a + 1, b)) for a in range(n_lat - 1) for b in range(n_lon)]
    up_pairs = [(flat(a + 1, b), flat(a, b)) for a in range(n_lat - 1) for b in range(n_lon)]
    pole_pairs = [(flat(a, b), flat(a, (b + half) % n_lon)) for a in (0, n_lat - 1) for b in range(n_lon)]
    right_pairs = [(b, (b + 1) % n_lon) for b in range(n_lon)]
    left_pairs = [(b, (b - 1) % n_lon) for b in range(n_lon)]
    both = ("lat", "lon")

    own_cols = j * width + jnp.arange(width)
    fold_row = jnp.where(at_north, fold_cols[0], fold_cols[1])
    fold_idx = jnp.take(fold_row, own_cols) - partner_j * width
    partner_cols = partner_j * width + jnp.arange(width)
    unfold_idx = (
        jnp.zeros((width,), jnp.int32)
        .at[jnp.take(fold_row, partner_cols) - j * width]
        .set(jnp.arange(width, dtype=jnp.int32))
    )

    kv = jnp.stack([keys, values])
    top_send = kv[:, :r]
    bottom_send = kv[:, height - r :]
    from_above = lax.ppermute(bottom_send, both, down_pairs)
    from_below = lax.ppermute(top_send, both, up_pairs)
    pole_send = jnp.where(at_north, top_send, bottom_send)
    pole_recv = lax.ppermute(pole_send, both, pole_pairs)
    pole_rows = jnp.take(pole_recv, fold_idx, axis=2)[:, ::-1]
    top = jnp.where(at_north, pole_rows, from_above)
    bottom = jnp.where(at_south, pole_rows, from_below)
    colfield = jnp.concatenate([top, kv, bottom], axis=1)
    from_left = lax.ppermute(colfield[:, :, width - r :], "lon", right_pairs)
    from_right = lax.ppermute(colfield[:, :, :r], "lon", left_pairs)
    ext = jnp.concatenate([from_left, colfield, from_right], axis=2)
    ext_rows = height + 2 * r
    ext_w = width + 2 * r
    ext = ext.reshape(2, ext_rows * ext_w, features)

    dq, dk, dv = attention_core(
        queries.reshape(height * width, features),
        grad_out.reshape(height * width, features),
        ext[0],
        ext[1],
        width,
    )

    dkv = jnp.stack([dk, dv]).reshape(2, ext_rows, ext_w, features)
    back_right = lax.ppermute(dkv[:, :, :r].astype(jnp.bfloat16), "lon", left_pairs)
    back_left = lax.ppermute(dkv[:, :, ext_w - r :].astype(jnp.bfloat16), "lon", right_pairs)
    col = jnp.concatenate(
        [
            dkv[:, :, r : 2 * r] + back_left.astype(jnp.float32),
            dkv[:, :, 2 * r : width],
            dkv[:, :, width : width + r] + back_right.astype(jnp.float32),
        ],
        axis=2,
    )
    top_g = col[:, :r].astype(jnp.bfloat16)
    bottom_g = col[:, ext_rows - r :].astype(jnp.bfloat16)
    up_recv = lax.ppermute(top_g, both, up_pairs)
    down_recv = lax.ppermute(bottom_g, both, down_pairs)
    pole_g = lax.ppermute(jnp.where(at_north, top_g, bottom_g), both, pole_pairs)
    unfolded = jnp.take(pole_g[:, ::-1], unfold_idx, axis=2)
    add_top = jnp.where(at_north, unfolded, down_recv).astype(jnp.float32)
    add_bottom = jnp.where(at_south, unfolded, up_recv).astype(jnp.float32)
    grads = jnp.concatenate(
        [
            col[:, r : 2 * r] + add_top,
            col[:, 2 * r : height],
            col[:, height : height + r] + add_bottom,
        ],
        axis=1,
    ).astype(jnp.bfloat16)
    return (dq.reshape(height, width, features), grads[0], grads[1])


def solution(mesh):
    placed = (
        P("lat", "lon", None),
        P("lat", "lon", None),
        P("lat", "lon", None),
        P("lat", "lon", None),
        P(),
    )
    return jax.shard_map(
        on_device,
        mesh=mesh,
        in_specs=placed,
        out_specs=(P("lat", "lon", None), P("lat", "lon", None), P("lat", "lon", None)),
        check_vma=False,
    )
```

```python
import jax
import jax.numpy as jnp
from jax import lax
from jax.experimental import pallas as pl
from jax.experimental.pallas import tpu as pltpu
from jax.sharding import PartitionSpec as P

HEADS = 16
HEAD_DIM = 64
RADIUS = 4

SPAN = 2 * RADIUS + 1
TILE_ROWS = 8
LANES = 128


def attention_kernel(width, q_ref, g_ref, k_ref, v_ref, dq_ref, dk_ref, dv_ref, bias_ref):
    scale = HEAD_DIM ** (-0.5)
    ext_w = width + 2 * RADIUS
    tq = TILE_ROWS * width
    tk = (TILE_ROWS + 2 * RADIUS) * ext_w
    step_k = TILE_ROWS * ext_w
    tiles = q_ref.shape[0] // tq
    pairs = q_ref.shape[1] // LANES

    qi = lax.broadcasted_iota(jnp.int32, (tq, tk), 0).astype(jnp.float32)
    ki = lax.broadcasted_iota(jnp.int32, (tq, tk), 1).astype(jnp.float32)
    qr = jnp.floor((qi + 0.5) * (1.0 / width))
    qc = qi - width * qr
    kr = jnp.floor((ki + 0.5) * (1.0 / ext_w))
    kc = ki - ext_w * kr
    dr = kr - qr
    dc = kc - qc
    ok = (dr >= 0) & (dr <= 2 * RADIUS) & (dc >= 0) & (dc <= 2 * RADIUS)
    bias_ref[...] = jnp.where(ok, 0.0, -jnp.inf).astype(jnp.float32)

    nt = (((1,), (1,)), ((), ()))
    tn = (((0,), (0,)), ((), ()))

    def head(qh, gh, kp, vp):
        s = lax.dot_general(qh, kp, nt, preferred_element_type=jnp.float32) * scale + bias_ref[...]
        m = jnp.max(s, axis=1, keepdims=True)
        e = jnp.exp(s - m)
        total = jnp.sum(e, axis=1, keepdims=True)
        w = e * (1.0 / total)
        dw = lax.dot_general(gh, vp, nt, preferred_element_type=jnp.float32)
        corr = jnp.sum(w * dw, axis=1, keepdims=True)
        ds = (w * (dw - corr)).astype(jnp.bfloat16)
        return ds, w.astype(jnp.bfloat16)

    def body(p, carry):
        lanes = pl.ds(pl.multiple_of(p * LANES, LANES), LANES)
        for t in range(tiles):
            qp = q_ref[pl.ds(t * tq, tq), lanes]
            gp = g_ref[pl.ds(t * tq, tq), lanes]
            kp = k_ref[pl.ds(t * step_k, tk), lanes]
            vp = v_ref[pl.ds(t * step_k, tk), lanes]
            lo = lax.broadcasted_iota(jnp.int32, qp.shape, 1) < HEAD_DIM
            zero = jnp.zeros_like(qp)
            qa = jnp.where(lo, qp, zero)
            qb = jnp.where(lo, zero, qp)
            ga = jnp.where(lo, gp, zero)
            gb = jnp.where(lo, zero, gp)
            dsa, wa = head(qa, ga, kp, vp)
            dsb, wb = head(qb, gb, kp, vp)
            dqa = jnp.dot(dsa, kp, preferred_element_type=jnp.float32)
            dqb = jnp.dot(dsb, kp, preferred_element_type=jnp.float32)
            dq = jnp.where(lo, dqa, dqb) * scale
            dq_ref[pl.ds(t * tq, tq), lanes] = dq.astype(dq_ref.dtype)
            dk = (
                lax.dot_general(dsa, qa, tn, preferred_element_type=jnp.float32)
                + lax.dot_general(dsb, qb, tn, preferred_element_type=jnp.float32)
            ) * scale
            dv = lax.dot_general(wa, ga, tn, preferred_element_type=jnp.float32) + lax.dot_general(
                wb, gb, tn, preferred_element_type=jnp.float32
            )
            if t == 0:
                dk_ref[pl.ds(0, tk), lanes] = dk
                dv_ref[pl.ds(0, tk), lanes] = dv
            else:
                shared = tk - step_k
                base = t * step_k
                dk_ref[pl.ds(base, shared), lanes] += dk[:shared]
                dv_ref[pl.ds(base, shared), lanes] += dv[:shared]
                dk_ref[pl.ds(base + shared, step_k), lanes] = dk[shared:]
                dv_ref[pl.ds(base + shared, step_k), lanes] = dv[shared:]
        return carry

    lax.fori_loop(0, pairs, body, 0)


def attention_core(q2, g2, k2, v2, width):
    cells, features = q2.shape
    ext_cells = k2.shape[0]
    ext_w = width + 2 * RADIUS
    tq = TILE_ROWS * width
    tk = (TILE_ROWS + 2 * RADIUS) * ext_w
    tiles = cells // tq
    flops = 10 * 2 * tq * tk * LANES * (features // LANES) * tiles
    vmem = pl.BlockSpec(memory_space=pltpu.VMEM)
    return pl.pallas_call(
        lambda *refs: attention_kernel(width, *refs),
        out_shape=(
            jax.ShapeDtypeStruct((cells, features), jnp.bfloat16),
            jax.ShapeDtypeStruct((ext_cells, features), jnp.float32),
            jax.ShapeDtypeStruct((ext_cells, features), jnp.float32),
        ),
        in_specs=[vmem] * 4,
        out_specs=(vmem, vmem, vmem),
        scratch_shapes=[pltpu.VMEM((tq, tk), jnp.float32)],
        cost_estimate=pl.CostEstimate(
            flops=flops,
            transcendentals=2 * tq * tk * HEADS * tiles,
            bytes_accessed=2 * (2 * cells * features) + 2 * (2 * ext_cells * features)
            + 2 * cells * features + 2 * 4 * ext_cells * features,
        ),
        name="neighbourhood_attention_bwd",
    )(q2, g2, k2, v2)


def on_device(queries, keys, values, grad_out, fold_cols):
    height, width, features = queries.shape
    n_lat = lax.axis_size("lat")
    n_lon = lax.axis_size("lon")
    half = n_lon // 2
    i = lax.axis_index("lat")
    j = lax.axis_index("lon")
    at_north = i == 0
    at_south = i == n_lat - 1
    partner_j = (j + half) % n_lon
    r = RADIUS

    def flat(a, b):
        return a * n_lon + b

    down_pairs = [(flat(a, b), flat(a + 1, b)) for a in range(n_lat - 1) for b in range(n_lon)]
    up_pairs = [(flat(a + 1, b), flat(a, b)) for a in range(n_lat - 1) for b in range(n_lon)]
    pole_pairs = [(flat(a, b), flat(a, (b + half) % n_lon)) for a in (0, n_lat - 1) for b in range(n_lon)]
    right_pairs = [(b, (b + 1) % n_lon) for b in range(n_lon)]
    left_pairs = [(b, (b - 1) % n_lon) for b in range(n_lon)]
    both = ("lat", "lon")

    ext_rows = height + 2 * r
    ext_w = width + 2 * r
    my_ext_cols = (j * width - r + jnp.arange(ext_w)) % (n_lon * width)
    partner_ext_cols = (partner_j * width - r + jnp.arange(ext_w)) % (n_lon * width)
    fold_row = jnp.where(at_north, fold_cols[0], fold_cols[1])
    fold_idx = (jnp.take(fold_row, my_ext_cols) - (partner_j * width - r)) % (n_lon * width)
    landing = (jnp.take(fold_row, partner_ext_cols) - (j * width - r)) % (n_lon * width)
    unfold_idx = jnp.zeros((ext_w,), jnp.int32).at[landing].set(jnp.arange(ext_w, dtype=jnp.int32))

    kv = jnp.stack([keys, values])
    from_left = lax.ppermute(kv[:, :, width - r :], "lon", right_pairs)
    from_right = lax.ppermute(kv[:, :, :r], "lon", left_pairs)
    rowfield = jnp.concatenate([from_left, kv, from_right], axis=2)
    top_send = rowfield[:, :r]
    bottom_send = rowfield[:, height - r :]
    from_above = lax.ppermute(bottom_send, both, down_pairs)
    from_below = lax.ppermute(top_send, both, up_pairs)
    pole_recv = lax.ppermute(jnp.where(at_north, top_send, bottom_send), both, pole_pairs)
    pole_rows = jnp.take(pole_recv, fold_idx, axis=2)[:, ::-1]
    top = jnp.where(at_north, pole_rows, from_above)
    bottom = jnp.where(at_south, pole_rows, from_below)
    ext = jnp.concatenate([top, rowfield, bottom], axis=1)
    ext = ext.reshape(2, ext_rows * ext_w, features)

    dq, dk, dv = attention_core(
        queries.reshape(height * width, features),
        grad_out.reshape(height * width, features),
        ext[0],
        ext[1],
        width,
    )

    dkv = jnp.stack([dk, dv]).reshape(2, ext_rows, ext_w, features)
    top_g = dkv[:, :r].astype(jnp.bfloat16)
    bottom_g = dkv[:, ext_rows - r :].astype(jnp.bfloat16)
    up_recv = lax.ppermute(top_g, both, up_pairs)
    down_recv = lax.ppermute(bottom_g, both, down_pairs)
    pole_g = lax.ppermute(jnp.where(at_north, top_g, bottom_g), both, pole_pairs)
    unfolded = jnp.take(pole_g[:, ::-1], unfold_idx, axis=2)
    add_top = jnp.where(at_north, unfolded, down_recv).astype(jnp.float32)
    add_bottom = jnp.where(at_south, unfolded, up_recv).astype(jnp.float32)
    rowgrad = jnp.concatenate(
        [
            dkv[:, r : 2 * r] + add_top,
            dkv[:, 2 * r : height],
            dkv[:, height : height + r] + add_bottom,
        ],
        axis=1,
    )
    back_right = lax.ppermute(rowgrad[:, :, :r].astype(jnp.bfloat16), "lon", left_pairs)
    back_left = lax.ppermute(rowgrad[:, :, ext_w - r :].astype(jnp.bfloat16), "lon", right_pairs)
    grads = jnp.concatenate(
        [
            rowgrad[:, :, r : 2 * r] + back_left.astype(jnp.float32),
            rowgrad[:, :, 2 * r : width],
            rowgrad[:, :, width : width + r] + back_right.astype(jnp.float32),
        ],
        axis=2,
    ).astype(jnp.bfloat16)
    return (dq.reshape(height, width, features), grads[0], grads[1])


def solution(mesh):
    placed = (
        P("lat", "lon", None),
        P("lat", "lon", None),
        P("lat", "lon", None),
        P("lat", "lon", None),
        P(),
    )
    return jax.shard_map(
        on_device,
        mesh=mesh,
        in_specs=placed,
        out_specs=(P("lat", "lon", None), P("lat", "lon", None), P("lat", "lon", None)),
        check_vma=False,
    )
```

```python
import jax
import jax.numpy as jnp
from jax import lax
from jax.experimental import pallas as pl
from jax.experimental.pallas import tpu as pltpu
from jax.sharding import PartitionSpec as P

HEADS = 16
HEAD_DIM = 64
RADIUS = 4

SPAN = 2 * RADIUS + 1
TILE_ROWS = 8
LANES = 128


def attention_kernel(width, q_ref, g_ref, k_ref, v_ref, dq_ref, dk_ref, dv_ref, bias_ref):
    scale = HEAD_DIM ** (-0.5)
    ext_w = width + 2 * RADIUS
    tq = TILE_ROWS * width
    tk = (TILE_ROWS + 2 * RADIUS) * ext_w
    step_k = TILE_ROWS * ext_w
    tiles = q_ref.shape[0] // tq
    pairs = q_ref.shape[1] // LANES

    qi = lax.broadcasted_iota(jnp.int32, (tq, tk), 0).astype(jnp.float32)
    ki = lax.broadcasted_iota(jnp.int32, (tq, tk), 1).astype(jnp.float32)
    qr = jnp.floor((qi + 0.5) * (1.0 / width))
    qc = qi - width * qr
    kr = jnp.floor((ki + 0.5) * (1.0 / ext_w))
    kc = ki - ext_w * kr
    dr = kr - qr
    dc = kc - qc
    ok = (dr >= 0) & (dr <= 2 * RADIUS) & (dc >= 0) & (dc <= 2 * RADIUS)
    bias_ref[...] = jnp.where(ok, 0.0, -jnp.inf).astype(jnp.float32)

    nt = (((1,), (1,)), ((), ()))
    tn = (((0,), (0,)), ((), ()))

    def head(qh, gh, kp, vp):
        s = lax.dot_general(qh, kp, nt, preferred_element_type=jnp.float32) * scale + bias_ref[...]
        m = jnp.max(s, axis=1, keepdims=True)
        e = jnp.exp(s - m)
        total = jnp.sum(e, axis=1, keepdims=True)
        w = e * (1.0 / total)
        dw = lax.dot_general(gh, vp, nt, preferred_element_type=jnp.float32)
        corr = jnp.sum(w * dw, axis=1, keepdims=True)
        ds = (w * (dw - corr)).astype(jnp.bfloat16)
        return ds, w.astype(jnp.bfloat16)

    def body(p, carry):
        lanes = pl.ds(pl.multiple_of(p * LANES, LANES), LANES)
        for t in range(tiles):
            qp = q_ref[pl.ds(t * tq, tq), lanes]
            gp = g_ref[pl.ds(t * tq, tq), lanes]
            kp = k_ref[pl.ds(t * step_k, tk), lanes].astype(jnp.bfloat16)
            vp = v_ref[pl.ds(t * step_k, tk), lanes].astype(jnp.bfloat16)
            lo = lax.broadcasted_iota(jnp.int32, qp.shape, 1) < HEAD_DIM
            zero = jnp.zeros_like(qp)
            qa = jnp.where(lo, qp, zero)
            qb = jnp.where(lo, zero, qp)
            ga = jnp.where(lo, gp, zero)
            gb = jnp.where(lo, zero, gp)
            dsa, wa = head(qa, ga, kp, vp)
            dsb, wb = head(qb, gb, kp, vp)
            dqa = jnp.dot(dsa, kp, preferred_element_type=jnp.float32)
            dqb = jnp.dot(dsb, kp, preferred_element_type=jnp.float32)
            dq = jnp.where(lo, dqa, dqb) * scale
            dq_ref[pl.ds(t * tq, tq), lanes] = dq.astype(dq_ref.dtype)
            dk = (
                lax.dot_general(dsa, qa, tn, preferred_element_type=jnp.float32)
                + lax.dot_general(dsb, qb, tn, preferred_element_type=jnp.float32)
            ) * scale
            dv = lax.dot_general(wa, ga, tn, preferred_element_type=jnp.float32) + lax.dot_general(
                wb, gb, tn, preferred_element_type=jnp.float32
            )
            if t == 0:
                dk_ref[pl.ds(0, tk), lanes] = dk
                dv_ref[pl.ds(0, tk), lanes] = dv
            else:
                shared = tk - step_k
                base = t * step_k
                dk_ref[pl.ds(base, shared), lanes] += dk[:shared]
                dv_ref[pl.ds(base, shared), lanes] += dv[:shared]
                dk_ref[pl.ds(base + shared, step_k), lanes] = dk[shared:]
                dv_ref[pl.ds(base + shared, step_k), lanes] = dv[shared:]
        return carry

    lax.fori_loop(0, pairs, body, 0)


def attention_core(q2, g2, k2, v2, width):
    cells, features = q2.shape
    ext_cells = k2.shape[0]
    ext_w = width + 2 * RADIUS
    tq = TILE_ROWS * width
    tk = (TILE_ROWS + 2 * RADIUS) * ext_w
    tiles = cells // tq
    flops = 10 * 2 * tq * tk * LANES * (features // LANES) * tiles
    vmem = pl.BlockSpec(memory_space=pltpu.VMEM)
    return pl.pallas_call(
        lambda *refs: attention_kernel(width, *refs),
        out_shape=(
            jax.ShapeDtypeStruct((cells, features), jnp.bfloat16),
            jax.ShapeDtypeStruct((ext_cells, features), jnp.float32),
            jax.ShapeDtypeStruct((ext_cells, features), jnp.float32),
        ),
        in_specs=[vmem] * 4,
        out_specs=(vmem, vmem, vmem),
        scratch_shapes=[pltpu.VMEM((tq, tk), jnp.float32)],
        cost_estimate=pl.CostEstimate(
            flops=flops,
            transcendentals=2 * tq * tk * HEADS * tiles,
            bytes_accessed=2 * (2 * cells * features) + 2 * (4 * ext_cells * features)
            + 2 * cells * features + 2 * 4 * ext_cells * features,
        ),
        name="neighbourhood_attention_bwd",
    )(q2, g2, k2, v2)


def on_device(queries, keys, values, grad_out, fold_cols):
    height, width, features = queries.shape
    n_lat = lax.axis_size("lat")
    n_lon = lax.axis_size("lon")
    half = n_lon // 2
    i = lax.axis_index("lat")
    j = lax.axis_index("lon")
    at_north = i == 0
    at_south = i == n_lat - 1
    partner_j = (j + half) % n_lon
    r = RADIUS
    f32 = jnp.float32
    bf16 = jnp.bfloat16

    def flat(a, b):
        return a * n_lon + b

    poles = (0, n_lat - 1)
    down_pairs = [(flat(a, b), flat(a + 1, b)) for a in range(n_lat - 1) for b in range(n_lon)]
    up_pairs = [(flat(a + 1, b), flat(a, b)) for a in range(n_lat - 1) for b in range(n_lon)]
    pole_pairs = [(flat(a, b), flat(a, (b + half) % n_lon)) for a in poles for b in range(n_lon)]
    pole_right = [(flat(a, b), flat(a, (b + 1) % n_lon)) for a in poles for b in range(n_lon)]
    pole_left = [(flat(a, b), flat(a, (b - 1) % n_lon)) for a in poles for b in range(n_lon)]
    right_pairs = [(b, (b + 1) % n_lon) for b in range(n_lon)]
    left_pairs = [(b, (b - 1) % n_lon) for b in range(n_lon)]
    both = ("lat", "lon")

    ext_rows = height + 2 * r
    ext_w = width + 2 * r
    own_cols = j * width + jnp.arange(width)
    partner_cols = partner_j * width + jnp.arange(width)
    fold_row = jnp.where(at_north, fold_cols[0], fold_cols[1])
    fold_idx = jnp.take(fold_row, own_cols) - partner_j * width
    landing = jnp.take(fold_row, partner_cols) - j * width
    unfold_idx = jnp.zeros((width,), jnp.int32).at[landing].set(jnp.arange(width, dtype=jnp.int32))

    def pair(a, b):
        return jnp.stack([a, b])

    from_left = lax.ppermute(pair(keys[:, width - r :], values[:, width - r :]), "lon", right_pairs)
    from_right = lax.ppermute(pair(keys[:, :r], values[:, :r]), "lon", left_pairs)
    top_own = pair(keys[:r], values[:r])
    bottom_own = pair(keys[height - r :], values[height - r :])
    pole_recv = lax.ppermute(jnp.where(at_north, top_own, bottom_own), both, pole_pairs)
    pole_rows = jnp.take(pole_recv, fold_idx, axis=2)[:, ::-1]

    top_send = jnp.concatenate([from_left[:, :r], top_own, from_right[:, :r]], axis=2)
    bottom_send = jnp.concatenate(
        [from_left[:, height - r :], bottom_own, from_right[:, height - r :]], axis=2
    )
    from_above = lax.ppermute(bottom_send, both, down_pairs)
    from_below = lax.ppermute(top_send, both, up_pairs)
    corner_left = lax.ppermute(pole_rows[:, :, width - r :], both, pole_right)
    corner_right = lax.ppermute(pole_rows[:, :, :r], both, pole_left)
    pole_full = jnp.concatenate([corner_left, pole_rows, corner_right], axis=2)
    top = jnp.where(at_north, pole_full, from_above)
    bottom = jnp.where(at_south, pole_full, from_below)

    def ext_of(c, own):
        middle = jnp.concatenate([from_left[c], own, from_right[c]], axis=1)
        whole = jnp.concatenate([top[c], middle, bottom[c]], axis=0).astype(f32)
        return whole.reshape(ext_rows * ext_w, features)

    dq, dk, dv = attention_core(
        queries.reshape(height * width, features),
        grad_out.reshape(height * width, features),
        ext_of(0, keys),
        ext_of(1, values),
        width,
    )
    dk = dk.reshape(ext_rows, ext_w, features)
    dv = dv.reshape(ext_rows, ext_w, features)

    top_g = pair(dk[:r], dv[:r]).astype(bf16)
    bottom_g = pair(dk[ext_rows - r :], dv[ext_rows - r :]).astype(bf16)
    up_recv = lax.ppermute(top_g, both, up_pairs)
    down_recv = lax.ppermute(bottom_g, both, down_pairs)
    pole_g = jnp.where(at_north, top_g, bottom_g)
    corner_back_right = lax.ppermute(pole_g[:, :, :r], both, pole_left)
    corner_back_left = lax.ppermute(pole_g[:, :, ext_w - r :], both, pole_right)
    pole_own = jnp.concatenate(
        [
            pole_g[:, :, r : 2 * r].astype(f32) + corner_back_left.astype(f32),
            pole_g[:, :, 2 * r : width].astype(f32),
            pole_g[:, :, width : width + r].astype(f32) + corner_back_right.astype(f32),
        ],
        axis=2,
    )

    def rows_of(c, d):
        return jnp.concatenate(
            [
                d[r : 2 * r] + down_recv[c].astype(f32),
                d[2 * r : height],
                d[height : height + r] + up_recv[c].astype(f32),
            ],
            axis=0,
        )

    rows_k = rows_of(0, dk)
    rows_v = rows_of(1, dv)

    back_right = lax.ppermute(
        pair(rows_k[:, :r], rows_v[:, :r]).astype(bf16), "lon", left_pairs
    )
    back_left = lax.ppermute(
        pair(rows_k[:, ext_w - r :], rows_v[:, ext_w - r :]).astype(bf16), "lon", right_pairs
    )
    pole_back = lax.ppermute(pole_own.astype(bf16), both, pole_pairs)
    unfolded = jnp.take(pole_back[:, ::-1], unfold_idx, axis=2).astype(f32)
    north_add = jnp.where(at_north, unfolded, 0.0)
    south_add = jnp.where(at_south, unfolded, 0.0)

    def final_of(c, rows):
        middle = jnp.concatenate(
            [
                rows[:, r : 2 * r] + back_left[c].astype(f32),
                rows[:, 2 * r : width],
                rows[:, width : width + r] + back_right[c].astype(f32),
            ],
            axis=1,
        )
        return jnp.concatenate(
            [middle[:r] + north_add[c], middle[r : height - r], middle[height - r :] + south_add[c]],
            axis=0,
        ).astype(bf16)

    return (dq.reshape(height, width, features), final_of(0, rows_k), final_of(1, rows_v))


def solution(mesh):
    placed = (
        P("lat", "lon", None),
        P("lat", "lon", None),
        P("lat", "lon", None),
        P("lat", "lon", None),
        P(),
    )
    return jax.shard_map(
        on_device,
        mesh=mesh,
        in_specs=placed,
        out_specs=(P("lat", "lon", None), P("lat", "lon", None), P("lat", "lon", None)),
        check_vma=False,
    )
```

```python
import jax
import jax.numpy as jnp
from jax import lax
from jax.experimental import pallas as pl
from jax.experimental.pallas import tpu as pltpu
from jax.sharding import PartitionSpec as P

HEADS = 16
HEAD_DIM = 64
RADIUS = 4

SPAN = 2 * RADIUS + 1
TILE_ROWS = 8
LANES = 128


def attention_kernel(width, *refs):
    (q_ref, g_ref, k_own, k_top, k_bot, k_left, k_right, v_own, v_top, v_bot, v_left, v_right) = refs[:12]
    (dq_ref, dk_own, dk_top, dk_bot, dk_left, dk_right, dv_own, dv_top, dv_bot, dv_left, dv_right) = refs[12:23]
    bias_ref = refs[23]
    scale = HEAD_DIM ** (-0.5)
    r = RADIUS
    tq = TILE_ROWS * width
    main = 2 * TILE_ROWS * width
    side = 2 * TILE_ROWS * r
    tk = main + 2 * side
    edge = r * width
    pairs = q_ref.shape[1] // LANES

    qi = lax.broadcasted_iota(jnp.int32, (tq, tk), 0).astype(jnp.float32)
    ki = lax.broadcasted_iota(jnp.int32, (tq, tk), 1).astype(jnp.float32)
    qr = jnp.floor((qi + 0.5) * (1.0 / width))
    qc = qi - width * qr
    in_main = ki < main
    in_left = (ki >= main) & (ki < main + side)
    kk = jnp.where(in_main, ki, jnp.where(in_left, ki - main, ki - main - side))
    per_row = jnp.where(in_main, float(width), float(r))
    kr = jnp.floor((kk + 0.5) / per_row)
    kc = kk - per_row * kr + jnp.where(in_main, float(r), jnp.where(in_left, 0.0, float(width + r)))
    dr = kr - qr
    dc = kc - qc
    ok = (dr >= 0) & (dr <= 2 * r) & (dc >= 0) & (dc <= 2 * r)
    bias_ref[...] = jnp.where(ok, 0.0, -jnp.inf).astype(jnp.float32)

    nt = (((1,), (1,)), ((), ()))
    tn = (((0,), (0,)), ((), ()))

    def head(qh, gh, kp, vp):
        s = lax.dot_general(qh, kp, nt, preferred_element_type=jnp.float32) * scale + bias_ref[...]
        m = jnp.max(s, axis=1, keepdims=True)
        e = jnp.exp(s - m)
        total = jnp.sum(e, axis=1, keepdims=True)
        w = e * (1.0 / total)
        dw = lax.dot_general(gh, vp, nt, preferred_element_type=jnp.float32)
        corr = jnp.sum(w * dw, axis=1, keepdims=True)
        ds = (w * (dw - corr)).astype(jnp.bfloat16)
        return ds, w.astype(jnp.bfloat16)

    def gather_keys(own, top, bot, left, right, t, lanes):
        if t == 0:
            middle = [top[pl.ds(0, edge), lanes], own[pl.ds(0, main - edge), lanes]]
        else:
            middle = [own[pl.ds(edge, main - edge), lanes], bot[pl.ds(0, edge), lanes]]
        sides = [left[pl.ds(t * side // 2, side), lanes], right[pl.ds(t * side // 2, side), lanes]]
        return jnp.concatenate(middle + sides, axis=0)

    def scatter_grads(d, own, top, bot, left, right, t, lanes):
        half = side // 2
        if t == 0:
            top[pl.ds(0, edge), lanes] = d[:edge]
            own[pl.ds(0, main - edge), lanes] = d[edge:main]
            left[pl.ds(0, side), lanes] = d[main : main + side]
            right[pl.ds(0, side), lanes] = d[main + side :]
        else:
            shared = main - 2 * edge
            own[pl.ds(edge, shared), lanes] += d[:shared]
            own[pl.ds(edge + shared, edge), lanes] = d[shared : main - edge]
            bot[pl.ds(0, edge), lanes] = d[main - edge : main]
            left[pl.ds(half, half), lanes] += d[main : main + half]
            left[pl.ds(side, half), lanes] = d[main + half : main + side]
            right[pl.ds(half, half), lanes] += d[main + side : main + side + half]
            right[pl.ds(side, half), lanes] = d[main + side + half :]

    def body(p, carry):
        lanes = pl.ds(pl.multiple_of(p * LANES, LANES), LANES)
        for t in range(2):
            qp = q_ref[pl.ds(t * tq, tq), lanes]
            gp = g_ref[pl.ds(t * tq, tq), lanes]
            kp = gather_keys(k_own, k_top, k_bot, k_left, k_right, t, lanes)
            vp = gather_keys(v_own, v_top, v_bot, v_left, v_right, t, lanes)
            lo = lax.broadcasted_iota(jnp.int32, qp.shape, 1) < HEAD_DIM
            zero = jnp.zeros_like(qp)
            qa = jnp.where(lo, qp, zero)
            qb = jnp.where(lo, zero, qp)
            ga = jnp.where(lo, gp, zero)
            gb = jnp.where(lo, zero, gp)
            dsa, wa = head(qa, ga, kp, vp)
            dsb, wb = head(qb, gb, kp, vp)
            dqa = jnp.dot(dsa, kp, preferred_element_type=jnp.float32)
            dqb = jnp.dot(dsb, kp, preferred_element_type=jnp.float32)
            dq = jnp.where(lo, dqa, dqb) * scale
            dq_ref[pl.ds(t * tq, tq), lanes] = dq.astype(dq_ref.dtype)
            dk = (
                lax.dot_general(dsa, qa, tn, preferred_element_type=jnp.float32)
                + lax.dot_general(dsb, qb, tn, preferred_element_type=jnp.float32)
            ) * scale
            dv = lax.dot_general(wa, ga, tn, preferred_element_type=jnp.float32) + lax.dot_general(
                wb, gb, tn, preferred_element_type=jnp.float32
            )
            scatter_grads(dk, dk_own, dk_top, dk_bot, dk_left, dk_right, t, lanes)
            scatter_grads(dv, dv_own, dv_top, dv_bot, dv_left, dv_right, t, lanes)
        return carry

    lax.fori_loop(0, pairs, body, 0)


def attention_core(q2, g2, k_parts, v_parts, width):
    cells, features = q2.shape
    r = RADIUS
    tq = TILE_ROWS * width
    tk = 2 * TILE_ROWS * (width + 2 * r)
    tiles = cells // tq
    assert tiles == 2
    part_shapes = [p.shape for p in k_parts]
    key_cells = sum(s[0] for s in part_shapes)
    flops = 10 * 2 * tq * tk * LANES * (features // LANES) * tiles
    vmem = pl.BlockSpec(memory_space=pltpu.VMEM)
    outs = [jax.ShapeDtypeStruct((cells, features), jnp.bfloat16)]
    outs += [jax.ShapeDtypeStruct(s, jnp.float32) for s in part_shapes] * 2
    results = pl.pallas_call(
        lambda *refs: attention_kernel(width, *refs),
        out_shape=tuple(outs),
        in_specs=[vmem] * 12,
        out_specs=tuple([vmem] * 11),
        scratch_shapes=[pltpu.VMEM((tq, tk), jnp.float32)],
        cost_estimate=pl.CostEstimate(
            flops=flops,
            transcendentals=2 * tq * tk * HEADS * tiles,
            bytes_accessed=2 * (3 * cells * features) + 2 * (2 * key_cells * features)
            + 4 * (2 * key_cells * features),
        ),
        name="neighbourhood_attention_bwd",
    )(q2, g2, *k_parts, *v_parts)
    return results[0], results[1:6], results[6:11]


def on_device(queries, keys, values, grad_out, fold_cols):
    height, width, features = queries.shape
    n_lat = lax.axis_size("lat")
    n_lon = lax.axis_size("lon")
    half = n_lon // 2
    i = lax.axis_index("lat")
    j = lax.axis_index("lon")
    at_north = i == 0
    at_south = i == n_lat - 1
    partner_j = (j + half) % n_lon
    r = RADIUS

    def flat(a, b):
        return a * n_lon + b

    down_pairs = [(flat(a, b), flat(a + 1, b)) for a in range(n_lat - 1) for b in range(n_lon)]
    up_pairs = [(flat(a + 1, b), flat(a, b)) for a in range(n_lat - 1) for b in range(n_lon)]
    pole_pairs = [(flat(a, b), flat(a, (b + half) % n_lon)) for a in (0, n_lat - 1) for b in range(n_lon)]
    right_pairs = [(b, (b + 1) % n_lon) for b in range(n_lon)]
    left_pairs = [(b, (b - 1) % n_lon) for b in range(n_lon)]
    both = ("lat", "lon")

    ext_rows = height + 2 * r
    ext_w = width + 2 * r
    my_ext_cols = (j * width - r + jnp.arange(ext_w)) % (n_lon * width)
    partner_ext_cols = (partner_j * width - r + jnp.arange(ext_w)) % (n_lon * width)
    fold_row = jnp.where(at_north, fold_cols[0], fold_cols[1])
    fold_idx = (jnp.take(fold_row, my_ext_cols) - (partner_j * width - r)) % (n_lon * width)
    landing = (jnp.take(fold_row, partner_ext_cols) - (j * width - r)) % (n_lon * width)
    unfold_idx = jnp.zeros((ext_w,), jnp.int32).at[landing].set(jnp.arange(ext_w, dtype=jnp.int32))

    f32 = jnp.float32
    bf16 = jnp.bfloat16

    def pair(a, b):
        return jnp.stack([a, b])

    from_left = lax.ppermute(pair(keys[:, width - r :], values[:, width - r :]), "lon", right_pairs)
    from_right = lax.ppermute(pair(keys[:, :r], values[:, :r]), "lon", left_pairs)
    top_send = jnp.concatenate([from_left[:, :r], pair(keys[:r], values[:r]), from_right[:, :r]], axis=2)
    bottom_send = jnp.concatenate(
        [from_left[:, height - r :], pair(keys[height - r :], values[height - r :]), from_right[:, height - r :]],
        axis=2,
    )
    from_above = lax.ppermute(bottom_send, both, down_pairs)
    from_below = lax.ppermute(top_send, both, up_pairs)
    pole_recv = lax.ppermute(jnp.where(at_north, top_send, bottom_send), both, pole_pairs)
    pole_rows = jnp.take(pole_recv, fold_idx, axis=2)[:, ::-1]
    top = jnp.where(at_north, pole_rows, from_above)
    bottom = jnp.where(at_south, pole_rows, from_below)

    def parts_of(c, own):
        side_l = jnp.concatenate([top[c, :, :r], from_left[c], bottom[c, :, :r]], axis=0)
        side_r = jnp.concatenate([top[c, :, ext_w - r :], from_right[c], bottom[c, :, ext_w - r :]], axis=0)
        return (
            own.reshape(height * width, features),
            top[c, :, r : ext_w - r].reshape(r * width, features),
            bottom[c, :, r : ext_w - r].reshape(r * width, features),
            side_l.reshape(ext_rows * r, features),
            side_r.reshape(ext_rows * r, features),
        )

    dq, dk, dv = attention_core(
        queries.reshape(height * width, features),
        grad_out.reshape(height * width, features),
        parts_of(0, keys),
        parts_of(1, values),
        width,
    )

    def strip(d, which):
        own, top_p, bot_p, left_p, right_p = d
        rows = slice(0, r) if which == 0 else slice(ext_rows - r, ext_rows)
        middle = top_p if which == 0 else bot_p
        return jnp.concatenate(
            [
                left_p.reshape(ext_rows, r, features)[rows],
                middle.reshape(r, width, features),
                right_p.reshape(ext_rows, r, features)[rows],
            ],
            axis=1,
        )

    top_g = pair(strip(dk, 0), strip(dv, 0)).astype(bf16)
    bottom_g = pair(strip(dk, 1), strip(dv, 1)).astype(bf16)
    up_recv = lax.ppermute(top_g, both, up_pairs)
    down_recv = lax.ppermute(bottom_g, both, down_pairs)
    pole_g = lax.ppermute(jnp.where(at_north, top_g, bottom_g), both, pole_pairs)
    unfolded = jnp.take(pole_g[:, ::-1], unfold_idx, axis=2)
    add_top = jnp.where(at_north, unfolded, down_recv).astype(f32)
    add_bottom = jnp.where(at_south, unfolded, up_recv).astype(f32)

    def rows_added(c, block, cols):
        return jnp.concatenate(
            [block[:r] + add_top[c, :, cols], block[r : height - r], block[height - r :] + add_bottom[c, :, cols]],
            axis=0,
        )

    def sides_of(c, d):
        left_p = d[3].reshape(ext_rows, r, features)[r : ext_rows - r]
        right_p = d[4].reshape(ext_rows, r, features)[r : ext_rows - r]
        return (
            rows_added(c, left_p, slice(0, r)),
            rows_added(c, right_p, slice(ext_w - r, ext_w)),
        )

    left_k, right_k = sides_of(0, dk)
    left_v, right_v = sides_of(1, dv)
    back_right = lax.ppermute(pair(left_k, left_v).astype(bf16), "lon", left_pairs)
    back_left = lax.ppermute(pair(right_k, right_v).astype(bf16), "lon", right_pairs)

    def final_of(c, d):
        own = rows_added(c, d[0].reshape(height, width, features), slice(r, ext_w - r))
        return jnp.concatenate(
            [
                own[:, :r] + back_left[c].astype(f32),
                own[:, r : width - r],
                own[:, width - r :] + back_right[c].astype(f32),
            ],
            axis=1,
        ).astype(bf16)

    return (dq.reshape(height, width, features), final_of(0, dk), final_of(1, dv))


def solution(mesh):
    placed = (
        P("lat", "lon", None),
        P("lat", "lon", None),
        P("lat", "lon", None),
        P("lat", "lon", None),
        P(),
    )
    return jax.shard_map(
        on_device,
        mesh=mesh,
        in_specs=placed,
        out_specs=(P("lat", "lon", None), P("lat", "lon", None), P("lat", "lon", None)),
        check_vma=False,
    )
```

```python
import jax
import jax.numpy as jnp
import numpy as np
from jax import lax
from jax.experimental import pallas as pl
from jax.experimental.pallas import tpu as pltpu
from jax.sharding import PartitionSpec as P

HEADS = 16
HEAD_DIM = 64
RADIUS = 4

SPAN = 2 * RADIUS + 1
TILE_ROWS = 8
LANES = 128


def attention_kernel(width, *refs):
    (q_ref, g_ref, k_own, v_own, top_in, bot_in, left_in, right_in) = refs[:8]
    (dq_ref, dk_own, dv_own, top_out, bot_out, left_out, right_out) = refs[8:15]
    bias_ref = refs[15]
    scale = HEAD_DIM ** (-0.5)
    r = RADIUS
    tq = TILE_ROWS * width
    main = 2 * TILE_ROWS * width
    side = 2 * TILE_ROWS * r
    tk = main + 2 * side
    edge = r * width
    corner = r * r
    pairs = q_ref.shape[1] // LANES

    qi = lax.broadcasted_iota(jnp.int32, (tq, tk), 0).astype(jnp.float32)
    ki = lax.broadcasted_iota(jnp.int32, (tq, tk), 1).astype(jnp.float32)
    qr = jnp.floor((qi + 0.5) * (1.0 / width))
    qc = qi - width * qr
    in_main = ki < main
    in_left = (ki >= main) & (ki < main + side)
    kk = jnp.where(in_main, ki, jnp.where(in_left, ki - main, ki - main - side))
    per_row = jnp.where(in_main, float(width), float(r))
    kr = jnp.floor((kk + 0.5) / per_row)
    kc = kk - per_row * kr + jnp.where(in_main, float(r), jnp.where(in_left, 0.0, float(width + r)))
    dr = kr - qr
    dc = kc - qc
    ok = (dr >= 0) & (dr <= 2 * r) & (dc >= 0) & (dc <= 2 * r)
    bias_ref[...] = jnp.where(ok, 0.0, -jnp.inf).astype(jnp.float32)

    nt = (((1,), (1,)), ((), ()))
    tn = (((0,), (0,)), ((), ()))

    def head(qh, gh, kp, vp):
        s = lax.dot_general(qh, kp, nt, preferred_element_type=jnp.float32) * scale + bias_ref[...]
        m = jnp.max(s, axis=1, keepdims=True)
        e = jnp.exp(s - m)
        total = jnp.sum(e, axis=1, keepdims=True)
        w = e * (1.0 / total)
        dw = lax.dot_general(gh, vp, nt, preferred_element_type=jnp.float32)
        corr = jnp.sum(w * dw, axis=1, keepdims=True)
        ds = (w * (dw - corr)).astype(jnp.bfloat16)
        return ds, w.astype(jnp.bfloat16)

    def gather_keys(own, c, t, lanes):
        rows = side - corner
        if t == 0:
            parts = [
                top_in[c, pl.ds(0, edge), lanes],
                own[pl.ds(0, main - edge), lanes],
                top_in[c, pl.ds(edge, corner), lanes],
                left_in[c, pl.ds(0, rows), lanes],
                top_in[c, pl.ds(edge + corner, corner), lanes],
                right_in[c, pl.ds(0, rows), lanes],
            ]
        else:
            start = left_in.shape[1] - rows
            parts = [
                own[pl.ds(edge, main - edge), lanes],
                bot_in[c, pl.ds(0, edge), lanes],
                left_in[c, pl.ds(start, rows), lanes],
                bot_in[c, pl.ds(edge, corner), lanes],
                right_in[c, pl.ds(start, rows), lanes],
                bot_in[c, pl.ds(edge + corner, corner), lanes],
            ]
        return jnp.concatenate(parts, axis=0)

    def scatter_grads(d, own, c, t, lanes):
        bf = jnp.bfloat16
        rows = side - corner
        n_side = left_out.shape[1]
        if t == 0:
            top_out[c, pl.ds(0, edge), lanes] = d[:edge].astype(bf)
            own[pl.ds(0, main - edge), lanes] = d[edge:main]
            top_out[c, pl.ds(edge, corner), lanes] = d[main : main + corner].astype(bf)
            left_out[c, pl.ds(0, rows), lanes] = d[main + corner : main + side]
            top_out[c, pl.ds(edge + corner, corner), lanes] = d[main + side : main + side + corner].astype(bf)
            right_out[c, pl.ds(0, rows), lanes] = d[main + side + corner :]
        else:
            shared = main - 2 * edge
            own[pl.ds(edge, shared), lanes] += d[:shared]
            own[pl.ds(edge + shared, edge), lanes] = d[shared : main - edge]
            bot_out[c, pl.ds(0, edge), lanes] = d[main - edge : main].astype(bf)
            start = n_side - rows
            overlap = rows - start
            left_out[c, pl.ds(start, overlap), lanes] += d[main : main + overlap]
            left_out[c, pl.ds(rows, n_side - rows), lanes] = d[main + overlap : main + rows]
            bot_out[c, pl.ds(edge, corner), lanes] = d[main + rows : main + side].astype(bf)
            right_out[c, pl.ds(start, overlap), lanes] += d[main + side : main + side + overlap]
            right_out[c, pl.ds(rows, n_side - rows), lanes] = d[main + side + overlap : main + side + rows]
            bot_out[c, pl.ds(edge + corner, corner), lanes] = d[main + side + rows :].astype(bf)

    def body(p, carry):
        lanes = pl.ds(pl.multiple_of(p * LANES, LANES), LANES)
        for t in range(2):
            qp = q_ref[pl.ds(t * tq, tq), lanes]
            gp = g_ref[pl.ds(t * tq, tq), lanes]
            kp = gather_keys(k_own, 0, t, lanes)
            vp = gather_keys(v_own, 1, t, lanes)
            lo = lax.broadcasted_iota(jnp.int32, qp.shape, 1) < HEAD_DIM
            zero = jnp.zeros_like(qp)
            qa = jnp.where(lo, qp, zero)
            qb = jnp.where(lo, zero, qp)
            ga = jnp.where(lo, gp, zero)
            gb = jnp.where(lo, zero, gp)
            dsa, wa = head(qa, ga, kp, vp)
            dsb, wb = head(qb, gb, kp, vp)
            dqa = jnp.dot(dsa, kp, preferred_element_type=jnp.float32)
            dqb = jnp.dot(dsb, kp, preferred_element_type=jnp.float32)
            dq = jnp.where(lo, dqa, dqb) * scale
            dq_ref[pl.ds(t * tq, tq), lanes] = dq.astype(dq_ref.dtype)
            dk = (
                lax.dot_general(dsa, qa, tn, preferred_element_type=jnp.float32)
                + lax.dot_general(dsb, qb, tn, preferred_element_type=jnp.float32)
            ) * scale
            dv = lax.dot_general(wa, ga, tn, preferred_element_type=jnp.float32) + lax.dot_general(
                wb, gb, tn, preferred_element_type=jnp.float32
            )
            scatter_grads(dk, dk_own, 0, t, lanes)
            scatter_grads(dv, dv_own, 1, t, lanes)
        return carry

    lax.fori_loop(0, pairs, body, 0)


def attention_core(q2, g2, k2, v2, top_in, bot_in, left_in, right_in, width):
    cells, features = q2.shape
    r = RADIUS
    tq = TILE_ROWS * width
    tk = 2 * TILE_ROWS * (width + 2 * r)
    tiles = cells // tq
    assert tiles == 2
    flops = 10 * 2 * tq * tk * LANES * (features // LANES) * tiles
    vmem = pl.BlockSpec(memory_space=pltpu.VMEM)
    f32 = jnp.float32
    outs = (
        jax.ShapeDtypeStruct((cells, features), jnp.bfloat16),
        jax.ShapeDtypeStruct((cells, features), f32),
        jax.ShapeDtypeStruct((cells, features), f32),
        jax.ShapeDtypeStruct(top_in.shape, jnp.bfloat16),
        jax.ShapeDtypeStruct(bot_in.shape, jnp.bfloat16),
        jax.ShapeDtypeStruct(left_in.shape, f32),
        jax.ShapeDtypeStruct(right_in.shape, f32),
    )
    in_bytes = 2 * (4 * cells * features + top_in.size + bot_in.size + left_in.size + right_in.size)
    out_bytes = 2 * cells * features + 8 * cells * features + 2 * (top_in.size + bot_in.size) + 4 * (
        left_in.size + right_in.size
    )
    return pl.pallas_call(
        lambda *refs: attention_kernel(width, *refs),
        out_shape=outs,
        in_specs=[vmem] * 8,
        out_specs=tuple([vmem] * 7),
        scratch_shapes=[pltpu.VMEM((tq, tk), jnp.float32)],
        cost_estimate=pl.CostEstimate(
            flops=flops,
            transcendentals=2 * tq * tk * HEADS * tiles,
            bytes_accessed=in_bytes + out_bytes,
        ),
        name="neighbourhood_attention_bwd",
    )(q2, g2, k2, v2, top_in, bot_in, left_in, right_in)


def on_device(queries, keys, values, grad_out, fold_cols):
    height, width, features = queries.shape
    n_lat = lax.axis_size("lat")
    n_lon = lax.axis_size("lon")
    half = n_lon // 2
    i = lax.axis_index("lat")
    j = lax.axis_index("lon")
    at_north = i == 0
    at_south = i == n_lat - 1
    partner_j = (j + half) % n_lon
    r = RADIUS
    f32 = jnp.float32
    bf16 = jnp.bfloat16
    cells = height * width
    edge = r * width
    corner = r * r

    def flat(a, b):
        return a * n_lon + b

    down_pairs = [(flat(a, b), flat(a + 1, b)) for a in range(n_lat - 1) for b in range(n_lon)]
    up_pairs = [(flat(a + 1, b), flat(a, b)) for a in range(n_lat - 1) for b in range(n_lon)]
    pole_pairs = [(flat(a, b), flat(a, (b + half) % n_lon)) for a in (0, n_lat - 1) for b in range(n_lon)]
    right_pairs = [(b, (b + 1) % n_lon) for b in range(n_lon)]
    left_pairs = [(b, (b - 1) % n_lon) for b in range(n_lon)]
    both = ("lat", "lon")

    ext_w = width + 2 * r
    n_cols = n_lon * width
    my_ext_cols = (j * width - r + jnp.arange(ext_w)) % n_cols
    partner_ext_cols = (partner_j * width - r + jnp.arange(ext_w)) % n_cols
    fold_row = jnp.where(at_north, fold_cols[0], fold_cols[1])
    fold_idx = (jnp.take(fold_row, my_ext_cols) - (partner_j * width - r)) % n_cols
    landing = (jnp.take(fold_row, partner_ext_cols) - (j * width - r)) % n_cols
    unfold_idx = jnp.zeros((ext_w,), jnp.int32).at[landing].set(jnp.arange(ext_w, dtype=jnp.int32))

    strip_row = np.concatenate([np.arange(edge) // width, np.arange(corner) // r, np.arange(corner) // r])
    strip_col = np.concatenate(
        [r + np.arange(edge) % width, np.arange(corner) % r, width + r + np.arange(corner) % r]
    )

    def strip_cell(row, col):
        return jnp.where(
            col < r,
            edge + row * r + col,
            jnp.where(col >= width + r, edge + corner + row * r + col - width - r, row * width + col - r),
        )

    pole_src = strip_cell(r - 1 - strip_row, jnp.take(fold_idx, strip_col))
    pole_dst = strip_cell(r - 1 - strip_row, jnp.take(unfold_idx, strip_col))

    def pair(a, b):
        return jnp.stack([a, b])

    kf = keys.reshape(cells, features)
    vf = values.reshape(cells, features)

    def cols(x, a, b):
        return x[:, a:b].reshape(height * (b - a), features)

    from_left = lax.ppermute(pair(cols(keys, width - r, width), cols(values, width - r, width)), "lon", right_pairs)
    from_right = lax.ppermute(pair(cols(keys, 0, r), cols(values, 0, r)), "lon", left_pairs)
    n_side = height * r
    top_send = jnp.concatenate(
        [pair(kf[:edge], vf[:edge]), from_left[:, :corner], from_right[:, :corner]], axis=1
    )
    bottom_send = jnp.concatenate(
        [pair(kf[cells - edge :], vf[cells - edge :]), from_left[:, n_side - corner :], from_right[:, n_side - corner :]],
        axis=1,
    )
    from_above = lax.ppermute(bottom_send, both, down_pairs)
    from_below = lax.ppermute(top_send, both, up_pairs)
    pole_recv = lax.ppermute(jnp.where(at_north, top_send, bottom_send), both, pole_pairs)
    pole_strip = jnp.take(pole_recv, pole_src, axis=1)
    top = jnp.where(at_north, pole_strip, from_above)
    bottom = jnp.where(at_south, pole_strip, from_below)

    dq, dk_own, dv_own, top_g, bottom_g, left_g, right_g = attention_core(
        queries.reshape(cells, features),
        grad_out.reshape(cells, features),
        kf,
        vf,
        top,
        bottom,
        from_left,
        from_right,
        width,
    )

    up_recv = lax.ppermute(top_g, both, up_pairs)
    down_recv = lax.ppermute(bottom_g, both, down_pairs)
    pole_g = lax.ppermute(jnp.where(at_north, top_g, bottom_g), both, pole_pairs)
    unfolded = jnp.take(pole_g, pole_dst, axis=1)
    add_top = jnp.where(at_north, unfolded, down_recv).astype(f32)
    add_bottom = jnp.where(at_south, unfolded, up_recv).astype(f32)

    def side_send(g, first):
        pads_top = [(0, 0), (0, n_side - corner), (0, 0)]
        pads_bottom = [(0, 0), (n_side - corner, 0), (0, 0)]
        return (
            g
            + jnp.pad(add_top[:, first : first + corner], pads_top)
            + jnp.pad(add_bottom[:, first : first + corner], pads_bottom)
        ).astype(bf16)

    back_right = lax.ppermute(side_send(left_g, edge), "lon", left_pairs)
    back_left = lax.ppermute(side_send(right_g, edge + corner), "lon", right_pairs)

    def final_of(c, own):
        block = own.reshape(height, width, features)
        row_pad = [(0, 0), (0, 0)]
        block = (
            block
            + jnp.pad(add_top[c, :edge].reshape(r, width, features), [(0, height - r)] + row_pad)
            + jnp.pad(add_bottom[c, :edge].reshape(r, width, features), [(height - r, 0)] + row_pad)
            + jnp.pad(
                back_left[c].reshape(height, r, features).astype(f32), [(0, 0), (0, width - r), (0, 0)]
            )
            + jnp.pad(
                back_right[c].reshape(height, r, features).astype(f32), [(0, 0), (width - r, 0), (0, 0)]
            )
        )
        return block.astype(bf16)

    return (dq.reshape(height, width, features), final_of(0, dk_own), final_of(1, dv_own))


def solution(mesh):
    placed = (
        P("lat", "lon", None),
        P("lat", "lon", None),
        P("lat", "lon", None),
        P("lat", "lon", None),
        P(),
    )
    return jax.shard_map(
        on_device,
        mesh=mesh,
        in_specs=placed,
        out_specs=(P("lat", "lon", None), P("lat", "lon", None), P("lat", "lon", None)),
        check_vma=False,
    )
```

```python
import jax
import jax.numpy as jnp
import numpy as np
from jax import lax
from jax.experimental import pallas as pl
from jax.experimental.pallas import tpu as pltpu
from jax.sharding import PartitionSpec as P

HEADS = 16
HEAD_DIM = 64
RADIUS = 4

SPAN = 2 * RADIUS + 1
TILE_ROWS = 8
LANES = 128


def attention_kernel(width, *refs):
    (q_ref, g_ref, k_own, v_own, top_in, bot_in, left_in, right_in) = refs[:8]
    (dq_ref, dk_own, dv_own, top_out, bot_out, left_out, right_out) = refs[8:15]
    bias_ref = refs[15]
    scale = HEAD_DIM ** (-0.5)
    r = RADIUS
    tq = TILE_ROWS * width
    main = 2 * TILE_ROWS * width
    side = 2 * TILE_ROWS * r
    tk = main + 2 * side
    edge = r * width
    corner = r * r
    pairs = q_ref.shape[1] // LANES

    qi = lax.broadcasted_iota(jnp.int32, (tq, tk), 0).astype(jnp.float32)
    ki = lax.broadcasted_iota(jnp.int32, (tq, tk), 1).astype(jnp.float32)
    qr = jnp.floor((qi + 0.5) * (1.0 / width))
    qc = qi - width * qr
    in_main = ki < main
    in_left = (ki >= main) & (ki < main + side)
    kk = jnp.where(in_main, ki, jnp.where(in_left, ki - main, ki - main - side))
    per_row = jnp.where(in_main, float(width), float(r))
    kr = jnp.floor((kk + 0.5) / per_row)
    kc = kk - per_row * kr + jnp.where(in_main, float(r), jnp.where(in_left, 0.0, float(width + r)))
    dr = kr - qr
    dc = kc - qc
    ok = (dr >= 0) & (dr <= 2 * r) & (dc >= 0) & (dc <= 2 * r)
    bias_ref[...] = jnp.where(ok, 0.0, -jnp.inf).astype(jnp.float32)

    nt = (((1,), (1,)), ((), ()))
    tn = (((0,), (0,)), ((), ()))

    def head(qh, gh, kp, vp):
        s = lax.dot_general(qh, kp, nt, preferred_element_type=jnp.float32) * scale + bias_ref[...]
        m = jnp.max(s, axis=1, keepdims=True)
        e = jnp.exp(s - m)
        total = jnp.sum(e, axis=1, keepdims=True)
        w = e * (1.0 / total)
        dw = lax.dot_general(gh, vp, nt, preferred_element_type=jnp.float32)
        corr = jnp.sum(w * dw, axis=1, keepdims=True)
        ds = (w * (dw - corr)).astype(jnp.bfloat16)
        return ds, w.astype(jnp.bfloat16)

    def gather_keys(own, c, t, lanes):
        rows = side - corner
        if t == 0:
            parts = [
                top_in[c, pl.ds(0, edge), lanes],
                own[pl.ds(0, main - edge), lanes],
                top_in[c, pl.ds(edge, corner), lanes],
                left_in[c, pl.ds(0, rows), lanes],
                top_in[c, pl.ds(edge + corner, corner), lanes],
                right_in[c, pl.ds(0, rows), lanes],
            ]
        else:
            start = left_in.shape[1] - rows
            parts = [
                own[pl.ds(edge, main - edge), lanes],
                bot_in[c, pl.ds(0, edge), lanes],
                left_in[c, pl.ds(start, rows), lanes],
                bot_in[c, pl.ds(edge, corner), lanes],
                right_in[c, pl.ds(start, rows), lanes],
                bot_in[c, pl.ds(edge + corner, corner), lanes],
            ]
        return jnp.concatenate(parts, axis=0)

    def scatter_grads(d, own, c, t, lanes):
        bf = jnp.bfloat16
        rows = side - corner
        n_side = left_out.shape[1]
        if t == 0:
            top_out[c, pl.ds(0, edge), lanes] = d[:edge].astype(bf)
            own[pl.ds(0, main - edge), lanes] = d[edge:main]
            top_out[c, pl.ds(edge, corner), lanes] = d[main : main + corner].astype(bf)
            left_out[c, pl.ds(0, rows), lanes] = d[main + corner : main + side]
            top_out[c, pl.ds(edge + corner, corner), lanes] = d[main + side : main + side + corner].astype(bf)
            right_out[c, pl.ds(0, rows), lanes] = d[main + side + corner :]
        else:
            shared = main - 2 * edge
            own[pl.ds(edge, shared), lanes] += d[:shared]
            own[pl.ds(edge + shared, edge), lanes] = d[shared : main - edge]
            bot_out[c, pl.ds(0, edge), lanes] = d[main - edge : main].astype(bf)
            start = n_side - rows
            overlap = rows - start
            left_out[c, pl.ds(start, overlap), lanes] += d[main : main + overlap]
            left_out[c, pl.ds(rows, n_side - rows), lanes] = d[main + overlap : main + rows]
            bot_out[c, pl.ds(edge, corner), lanes] = d[main + rows : main + side].astype(bf)
            right_out[c, pl.ds(start, overlap), lanes] += d[main + side : main + side + overlap]
            right_out[c, pl.ds(rows, n_side - rows), lanes] = d[main + side + overlap : main + side + rows]
            bot_out[c, pl.ds(edge + corner, corner), lanes] = d[main + side + rows :].astype(bf)

    def body(p, carry):
        lanes = pl.ds(pl.multiple_of(p * LANES, LANES), LANES)
        for t in range(2):
            qp = q_ref[pl.ds(t * tq, tq), lanes]
            gp = g_ref[pl.ds(t * tq, tq), lanes]
            kp = gather_keys(k_own, 0, t, lanes)
            vp = gather_keys(v_own, 1, t, lanes)
            lo = lax.broadcasted_iota(jnp.int32, qp.shape, 1) < HEAD_DIM
            zero = jnp.zeros_like(qp)
            qa = jnp.where(lo, qp, zero)
            qb = jnp.where(lo, zero, qp)
            ga = jnp.where(lo, gp, zero)
            gb = jnp.where(lo, zero, gp)
            dsa, wa = head(qa, ga, kp, vp)
            dsb, wb = head(qb, gb, kp, vp)
            dqa = jnp.dot(dsa, kp, preferred_element_type=jnp.float32)
            dqb = jnp.dot(dsb, kp, preferred_element_type=jnp.float32)
            dq = jnp.where(lo, dqa, dqb) * scale
            dq_ref[pl.ds(t * tq, tq), lanes] = dq.astype(dq_ref.dtype)
            dk = (
                lax.dot_general(dsa, qa, tn, preferred_element_type=jnp.float32)
                + lax.dot_general(dsb, qb, tn, preferred_element_type=jnp.float32)
            ) * scale
            dv = lax.dot_general(wa, ga, tn, preferred_element_type=jnp.float32) + lax.dot_general(
                wb, gb, tn, preferred_element_type=jnp.float32
            )
            scatter_grads(dk, dk_own, 0, t, lanes)
            scatter_grads(dv, dv_own, 1, t, lanes)
        return carry

    lax.fori_loop(0, pairs, body, 0)


def attention_core(q2, g2, k2, v2, top_in, bot_in, left_in, right_in, width):
    cells, features = q2.shape
    r = RADIUS
    tq = TILE_ROWS * width
    tk = 2 * TILE_ROWS * (width + 2 * r)
    tiles = cells // tq
    assert tiles == 2
    flops = 10 * 2 * tq * tk * LANES * (features // LANES) * tiles
    vmem = pl.BlockSpec(memory_space=pltpu.VMEM)
    f32 = jnp.float32
    outs = (
        jax.ShapeDtypeStruct((cells, features), jnp.bfloat16),
        jax.ShapeDtypeStruct((cells, features), f32),
        jax.ShapeDtypeStruct((cells, features), f32),
        jax.ShapeDtypeStruct(top_in.shape, jnp.bfloat16),
        jax.ShapeDtypeStruct(bot_in.shape, jnp.bfloat16),
        jax.ShapeDtypeStruct(left_in.shape, f32),
        jax.ShapeDtypeStruct(right_in.shape, f32),
    )
    in_bytes = 2 * (4 * cells * features + top_in.size + bot_in.size + left_in.size + right_in.size)
    out_bytes = 2 * cells * features + 8 * cells * features + 2 * (top_in.size + bot_in.size) + 4 * (
        left_in.size + right_in.size
    )
    return pl.pallas_call(
        lambda *refs: attention_kernel(width, *refs),
        out_shape=outs,
        in_specs=[vmem] * 8,
        out_specs=tuple([vmem] * 7),
        scratch_shapes=[pltpu.VMEM((tq, tk), jnp.float32)],
        cost_estimate=pl.CostEstimate(
            flops=flops,
            transcendentals=2 * tq * tk * HEADS * tiles,
            bytes_accessed=in_bytes + out_bytes,
        ),
        name="neighbourhood_attention_bwd",
    )(q2, g2, k2, v2, top_in, bot_in, left_in, right_in)


def on_device(queries, keys, values, grad_out, fold_cols):
    height, width, features = queries.shape
    n_lat = lax.axis_size("lat")
    n_lon = lax.axis_size("lon")
    half = n_lon // 2
    i = lax.axis_index("lat")
    j = lax.axis_index("lon")
    at_north = i == 0
    at_south = i == n_lat - 1
    partner_j = (j + half) % n_lon
    r = RADIUS
    f32 = jnp.float32
    bf16 = jnp.bfloat16
    cells = height * width
    edge = r * width
    corner = r * r

    def flat(a, b):
        return a * n_lon + b

    down_pairs = [(flat(a, b), flat(a + 1, b)) for a in range(n_lat - 1) for b in range(n_lon)]
    up_pairs = [(flat(a + 1, b), flat(a, b)) for a in range(n_lat - 1) for b in range(n_lon)]
    pole_pairs = [(flat(a, b), flat(a, (b + half) % n_lon)) for a in (0, n_lat - 1) for b in range(n_lon)]
    right_pairs = [(b, (b + 1) % n_lon) for b in range(n_lon)]
    left_pairs = [(b, (b - 1) % n_lon) for b in range(n_lon)]
    both = ("lat", "lon")

    ext_w = width + 2 * r
    n_cols = n_lon * width
    my_ext_cols = (j * width - r + jnp.arange(ext_w)) % n_cols
    partner_ext_cols = (partner_j * width - r + jnp.arange(ext_w)) % n_cols
    fold_row = jnp.where(at_north, fold_cols[0], fold_cols[1])
    fold_idx = (jnp.take(fold_row, my_ext_cols) - (partner_j * width - r)) % n_cols
    landing = (jnp.take(fold_row, partner_ext_cols) - (j * width - r)) % n_cols
    unfold_idx = jnp.zeros((ext_w,), jnp.int32).at[landing].set(jnp.arange(ext_w, dtype=jnp.int32))

    strip_row = np.concatenate([np.arange(edge) // width, np.arange(corner) // r, np.arange(corner) // r])
    strip_col = np.concatenate(
        [r + np.arange(edge) % width, np.arange(corner) % r, width + r + np.arange(corner) % r]
    )

    def strip_cell(row, col):
        return jnp.where(
            col < r,
            edge + row * r + col,
            jnp.where(col >= width + r, edge + corner + row * r + col - width - r, row * width + col - r),
        )

    pole_src = strip_cell(r - 1 - strip_row, jnp.take(fold_idx, strip_col))
    pole_dst = strip_cell(r - 1 - strip_row, jnp.take(unfold_idx, strip_col))

    def pair(a, b):
        return jnp.stack([a, b])

    kf = keys.reshape(cells, features)
    vf = values.reshape(cells, features)

    def cols(x, a, b):
        return x[:, a:b].reshape(height * (b - a), features)

    from_left = lax.ppermute(pair(cols(keys, width - r, width), cols(values, width - r, width)), "lon", right_pairs)
    from_right = lax.ppermute(pair(cols(keys, 0, r), cols(values, 0, r)), "lon", left_pairs)
    top_mid = pair(kf[:edge], vf[:edge])
    bottom_mid = pair(kf[cells - edge :], vf[cells - edge :])
    pole_mid = lax.ppermute(jnp.where(at_north, top_mid, bottom_mid), both, pole_pairs)
    n_side = height * r
    top_send = jnp.concatenate([top_mid, from_left[:, :corner], from_right[:, :corner]], axis=1)
    bottom_send = jnp.concatenate(
        [bottom_mid, from_left[:, n_side - corner :], from_right[:, n_side - corner :]], axis=1
    )
    from_above = lax.ppermute(bottom_send, both, down_pairs)
    from_below = lax.ppermute(top_send, both, up_pairs)
    pole_corners = lax.ppermute(
        jnp.where(at_north, top_send[:, edge:], bottom_send[:, edge:]), both, pole_pairs
    )
    pole_strip = jnp.concatenate(
        [jnp.take(pole_mid, pole_src[:edge], axis=1), jnp.take(pole_corners, pole_src[edge:] - edge, axis=1)],
        axis=1,
    )
    top = jnp.where(at_north, pole_strip, from_above)
    bottom = jnp.where(at_south, pole_strip, from_below)

    dq, dk_own, dv_own, top_g, bottom_g, left_g, right_g = attention_core(
        queries.reshape(cells, features),
        grad_out.reshape(cells, features),
        kf,
        vf,
        top,
        bottom,
        from_left,
        from_right,
        width,
    )

    up_recv = lax.ppermute(top_g, both, up_pairs)
    down_recv = lax.ppermute(bottom_g, both, down_pairs)
    pole_g = jnp.where(at_north, top_g, bottom_g)
    pole_g_corners = lax.ppermute(pole_g[:, edge:], both, pole_pairs)
    unfolded_corners = jnp.take(pole_g_corners, pole_dst[edge:] - edge, axis=1)
    zero_mid = jnp.zeros_like(up_recv[:, :edge])
    add_top = jnp.where(
        at_north, jnp.concatenate([zero_mid, unfolded_corners], axis=1), down_recv
    ).astype(f32)
    add_bottom = jnp.where(
        at_south, jnp.concatenate([zero_mid, unfolded_corners], axis=1), up_recv
    ).astype(f32)

    def side_send(g, first):
        pads_top = [(0, 0), (0, n_side - corner), (0, 0)]
        pads_bottom = [(0, 0), (n_side - corner, 0), (0, 0)]
        return (
            g
            + jnp.pad(add_top[:, first : first + corner], pads_top)
            + jnp.pad(add_bottom[:, first : first + corner], pads_bottom)
        ).astype(bf16)

    back_right = lax.ppermute(side_send(left_g, edge), "lon", left_pairs)
    back_left = lax.ppermute(side_send(right_g, edge + corner), "lon", right_pairs)
    pole_g_mid = lax.ppermute(pole_g[:, :edge], both, pole_pairs)
    unfolded_mid = jnp.take(pole_g_mid, pole_dst[:edge], axis=1).astype(f32)
    north_mid = jnp.where(at_north, unfolded_mid, 0.0)
    south_mid = jnp.where(at_south, unfolded_mid, 0.0)

    def final_of(c, own):
        block = own.reshape(height, width, features)
        row_pad = [(0, 0), (0, 0)]
        block = (
            block
            + jnp.pad((add_top[c, :edge] + north_mid[c]).reshape(r, width, features), [(0, height - r)] + row_pad)
            + jnp.pad((add_bottom[c, :edge] + south_mid[c]).reshape(r, width, features), [(height - r, 0)] + row_pad)
            + jnp.pad(
                back_left[c].reshape(height, r, features).astype(f32), [(0, 0), (0, width - r), (0, 0)]
            )
            + jnp.pad(
                back_right[c].reshape(height, r, features).astype(f32), [(0, 0), (width - r, 0), (0, 0)]
            )
        )
        return block.astype(bf16)

    return (dq.reshape(height, width, features), final_of(0, dk_own), final_of(1, dv_own))


def solution(mesh):
    placed = (
        P("lat", "lon", None),
        P("lat", "lon", None),
        P("lat", "lon", None),
        P("lat", "lon", None),
        P(),
    )
    return jax.shard_map(
        on_device,
        mesh=mesh,
        in_specs=placed,
        out_specs=(P("lat", "lon", None), P("lat", "lon", None), P("lat", "lon", None)),
        check_vma=False,
    )
```

```python
import jax
import jax.numpy as jnp
import numpy as np
from jax import lax
from jax.experimental import pallas as pl
from jax.experimental.pallas import tpu as pltpu
from jax.sharding import PartitionSpec as P

HEADS = 16
HEAD_DIM = 64
RADIUS = 4

SPAN = 2 * RADIUS + 1
TILE_ROWS = 4
LANES = 128


def attention_kernel(width, *refs):
    (q_ref, g_ref, k_own, v_own, top_in, bot_in, left_in, right_in) = refs[:8]
    (dq_ref, dk_own, dv_own, top_out, bot_out, left_out, right_out) = refs[8:15]
    bias_ref = refs[15]
    scale = HEAD_DIM ** (-0.5)
    r = RADIUS
    tq = TILE_ROWS * width
    win = TILE_ROWS + 2 * r
    main = win * width
    side = win * r
    tk = main + 2 * side
    edge = r * width
    corner = r * r
    tiles = q_ref.shape[0] // tq
    groups_per_tile = win // r
    last_group = (tiles * TILE_ROWS + 2 * r) // r - 1
    pairs = q_ref.shape[1] // LANES

    qi = lax.broadcasted_iota(jnp.int32, (tq, tk), 0).astype(jnp.float32)
    ki = lax.broadcasted_iota(jnp.int32, (tq, tk), 1).astype(jnp.float32)
    qr = jnp.floor((qi + 0.5) * (1.0 / width))
    qc = qi - width * qr
    in_main = ki < main
    in_left = (ki >= main) & (ki < main + side)
    kk = jnp.where(in_main, ki, jnp.where(in_left, ki - main, ki - main - side))
    per_row = jnp.where(in_main, float(width), float(r))
    kr = jnp.floor((kk + 0.5) / per_row)
    kc = kk - per_row * kr + jnp.where(in_main, float(r), jnp.where(in_left, 0.0, float(width + r)))
    dr = kr - qr
    dc = kc - qc
    ok = (dr >= 0) & (dr <= 2 * r) & (dc >= 0) & (dc <= 2 * r)
    bias_ref[...] = jnp.where(ok, 0.0, -jnp.inf).astype(jnp.float32)

    nt = (((1,), (1,)), ((), ()))
    tn = (((0,), (0,)), ((), ()))

    def head(qh, gh, kp, vp):
        s = lax.dot_general(qh, kp, nt, preferred_element_type=jnp.float32) * scale + bias_ref[...]
        m = jnp.max(s, axis=1, keepdims=True)
        e = jnp.exp(s - m)
        total = jnp.sum(e, axis=1, keepdims=True)
        w = e * (1.0 / total)
        dw = lax.dot_general(gh, vp, nt, preferred_element_type=jnp.float32)
        corr = jnp.sum(w * dw, axis=1, keepdims=True)
        ds = (w * (dw - corr)).astype(jnp.bfloat16)
        return ds, w.astype(jnp.bfloat16)

    def places(g, own, top, bot, left, right, c):
        if g == 0:
            return [(top, (c,), 0, edge), (top, (c,), edge, corner), (top, (c,), edge + corner, corner)]
        if g == last_group:
            return [(bot, (c,), 0, edge), (bot, (c,), edge, corner), (bot, (c,), edge + corner, corner)]
        return [(own, (), (g - 1) * edge, edge), (left, (c,), (g - 1) * corner, corner),
                (right, (c,), (g - 1) * corner, corner)]

    def gather_keys(own, c, t, lanes):
        parts = [[], [], []]
        for g in range(t, t + groups_per_tile):
            for kind, (ref, pre, start, size) in enumerate(places(g, own, top_in, bot_in, left_in, right_in, c)):
                parts[kind].append(ref[pre + (pl.ds(start, size), lanes)])
        return jnp.concatenate(parts[0] + parts[1] + parts[2], axis=0)

    def scatter_grads(d, own, c, t, lanes):
        offsets = [0, main, main + side]
        for n, g in enumerate(range(t, t + groups_per_tile)):
            first = t == max(0, g - (groups_per_tile - 1))
            for kind, (ref, pre, start, size) in enumerate(places(g, own, top_out, bot_out, left_out, right_out, c)):
                piece = d[offsets[kind] + n * size : offsets[kind] + (n + 1) * size]
                index = pre + (pl.ds(start, size), lanes)
                if first:
                    ref[index] = piece.astype(ref.dtype)
                else:
                    ref[index] += piece

    def body(p, carry):
        lanes = pl.ds(pl.multiple_of(p * LANES, LANES), LANES)
        for t in range(tiles):
            qp = q_ref[pl.ds(t * tq, tq), lanes]
            gp = g_ref[pl.ds(t * tq, tq), lanes]
            kp = gather_keys(k_own, 0, t, lanes)
            vp = gather_keys(v_own, 1, t, lanes)
            lo = lax.broadcasted_iota(jnp.int32, qp.shape, 1) < HEAD_DIM
            zero = jnp.zeros_like(qp)
            qa = jnp.where(lo, qp, zero)
            qb = jnp.where(lo, zero, qp)
            ga = jnp.where(lo, gp, zero)
            gb = jnp.where(lo, zero, gp)
            dsa, wa = head(qa, ga, kp, vp)
            dsb, wb = head(qb, gb, kp, vp)
            dqa = jnp.dot(dsa, kp, preferred_element_type=jnp.float32)
            dqb = jnp.dot(dsb, kp, preferred_element_type=jnp.float32)
            dq = jnp.where(lo, dqa, dqb) * scale
            dq_ref[pl.ds(t * tq, tq), lanes] = dq.astype(dq_ref.dtype)
            dk = (
                lax.dot_general(dsa, qa, tn, preferred_element_type=jnp.float32)
                + lax.dot_general(dsb, qb, tn, preferred_element_type=jnp.float32)
            ) * scale
            dv = lax.dot_general(wa, ga, tn, preferred_element_type=jnp.float32) + lax.dot_general(
                wb, gb, tn, preferred_element_type=jnp.float32
            )
            scatter_grads(dk, dk_own, 0, t, lanes)
            scatter_grads(dv, dv_own, 1, t, lanes)
        return carry

    lax.fori_loop(0, pairs, body, 0)


def attention_core(q2, g2, k2, v2, top_in, bot_in, left_in, right_in, width):
    cells, features = q2.shape
    r = RADIUS
    tq = TILE_ROWS * width
    tk = (TILE_ROWS + 2 * r) * (width + 2 * r)
    tiles = cells // tq
    assert TILE_ROWS % r == 0 and tiles * TILE_ROWS == cells // width
    flops = 10 * 2 * tq * tk * LANES * (features // LANES) * tiles
    vmem = pl.BlockSpec(memory_space=pltpu.VMEM)
    f32 = jnp.float32
    outs = (
        jax.ShapeDtypeStruct((cells, features), jnp.bfloat16),
        jax.ShapeDtypeStruct((cells, features), f32),
        jax.ShapeDtypeStruct((cells, features), f32),
        jax.ShapeDtypeStruct(top_in.shape, jnp.bfloat16),
        jax.ShapeDtypeStruct(bot_in.shape, jnp.bfloat16),
        jax.ShapeDtypeStruct(left_in.shape, f32),
        jax.ShapeDtypeStruct(right_in.shape, f32),
    )
    in_bytes = 2 * (4 * cells * features + top_in.size + bot_in.size + left_in.size + right_in.size)
    out_bytes = 2 * cells * features + 8 * cells * features + 2 * (top_in.size + bot_in.size) + 4 * (
        left_in.size + right_in.size
    )
    return pl.pallas_call(
        lambda *refs: attention_kernel(width, *refs),
        out_shape=outs,
        in_specs=[vmem] * 8,
        out_specs=tuple([vmem] * 7),
        scratch_shapes=[pltpu.VMEM((tq, tk), jnp.float32)],
        cost_estimate=pl.CostEstimate(
            flops=flops,
            transcendentals=2 * tq * tk * HEADS * tiles,
            bytes_accessed=in_bytes + out_bytes,
        ),
        name="neighbourhood_attention_bwd",
    )(q2, g2, k2, v2, top_in, bot_in, left_in, right_in)


def on_device(queries, keys, values, grad_out, fold_cols):
    height, width, features = queries.shape
    n_lat = lax.axis_size("lat")
    n_lon = lax.axis_size("lon")
    half = n_lon // 2
    i = lax.axis_index("lat")
    j = lax.axis_index("lon")
    at_north = i == 0
    at_south = i == n_lat - 1
    partner_j = (j + half) % n_lon
    r = RADIUS
    f32 = jnp.float32
    bf16 = jnp.bfloat16
    cells = height * width
    edge = r * width
    corner = r * r

    def flat(a, b):
        return a * n_lon + b

    down_pairs = [(flat(a, b), flat(a + 1, b)) for a in range(n_lat - 1) for b in range(n_lon)]
    up_pairs = [(flat(a + 1, b), flat(a, b)) for a in range(n_lat - 1) for b in range(n_lon)]
    pole_pairs = [(flat(a, b), flat(a, (b + half) % n_lon)) for a in (0, n_lat - 1) for b in range(n_lon)]
    right_pairs = [(b, (b + 1) % n_lon) for b in range(n_lon)]
    left_pairs = [(b, (b - 1) % n_lon) for b in range(n_lon)]
    both = ("lat", "lon")

    ext_w = width + 2 * r
    n_cols = n_lon * width
    my_ext_cols = (j * width - r + jnp.arange(ext_w)) % n_cols
    partner_ext_cols = (partner_j * width - r + jnp.arange(ext_w)) % n_cols
    fold_row = jnp.where(at_north, fold_cols[0], fold_cols[1])
    fold_idx = (jnp.take(fold_row, my_ext_cols) - (partner_j * width - r)) % n_cols
    landing = (jnp.take(fold_row, partner_ext_cols) - (j * width - r)) % n_cols
    unfold_idx = jnp.zeros((ext_w,), jnp.int32).at[landing].set(jnp.arange(ext_w, dtype=jnp.int32))

    strip_row = np.concatenate([np.arange(edge) // width, np.arange(corner) // r, np.arange(corner) // r])
    strip_col = np.concatenate(
        [r + np.arange(edge) % width, np.arange(corner) % r, width + r + np.arange(corner) % r]
    )

    def strip_cell(row, col):
        return jnp.where(
            col < r,
            edge + row * r + col,
            jnp.where(col >= width + r, edge + corner + row * r + col - width - r, row * width + col - r),
        )

    pole_src = strip_cell(r - 1 - strip_row, jnp.take(fold_idx, strip_col))
    pole_dst = strip_cell(r - 1 - strip_row, jnp.take(unfold_idx, strip_col))

    def pair(a, b):
        return jnp.stack([a, b])

    kf = keys.reshape(cells, features)
    vf = values.reshape(cells, features)

    def cols(x, a, b):
        return x[:, a:b].reshape(height * (b - a), features)

    from_left = lax.ppermute(pair(cols(keys, width - r, width), cols(values, width - r, width)), "lon", right_pairs)
    from_right = lax.ppermute(pair(cols(keys, 0, r), cols(values, 0, r)), "lon", left_pairs)
    top_mid = pair(kf[:edge], vf[:edge])
    bottom_mid = pair(kf[cells - edge :], vf[cells - edge :])
    pole_mid = lax.ppermute(jnp.where(at_north, top_mid, bottom_mid), both, pole_pairs)
    n_side = height * r
    top_send = jnp.concatenate([top_mid, from_left[:, :corner], from_right[:, :corner]], axis=1)
    bottom_send = jnp.concatenate(
        [bottom_mid, from_left[:, n_side - corner :], from_right[:, n_side - corner :]], axis=1
    )
    from_above = lax.ppermute(bottom_send, both, down_pairs)
    from_below = lax.ppermute(top_send, both, up_pairs)
    pole_corners = lax.ppermute(
        jnp.where(at_north, top_send[:, edge:], bottom_send[:, edge:]), both, pole_pairs
    )
    pole_strip = jnp.concatenate(
        [jnp.take(pole_mid, pole_src[:edge], axis=1), jnp.take(pole_corners, pole_src[edge:] - edge, axis=1)],
        axis=1,
    )
    top = jnp.where(at_north, pole_strip, from_above)
    bottom = jnp.where(at_south, pole_strip, from_below)

    dq, dk_own, dv_own, top_g, bottom_g, left_g, right_g = attention_core(
        queries.reshape(cells, features),
        grad_out.reshape(cells, features),
        kf,
        vf,
        top,
        bottom,
        from_left,
        from_right,
        width,
    )

    up_recv = lax.ppermute(top_g, both, up_pairs)
    down_recv = lax.ppermute(bottom_g, both, down_pairs)
    pole_g = jnp.where(at_north, top_g, bottom_g)
    pole_g_corners = lax.ppermute(pole_g[:, edge:], both, pole_pairs)
    unfolded_corners = jnp.take(pole_g_corners, pole_dst[edge:] - edge, axis=1)
    zero_mid = jnp.zeros_like(up_recv[:, :edge])
    add_top = jnp.where(
        at_north, jnp.concatenate([zero_mid, unfolded_corners], axis=1), down_recv
    ).astype(f32)
    add_bottom = jnp.where(
        at_south, jnp.concatenate([zero_mid, unfolded_corners], axis=1), up_recv
    ).astype(f32)

    def side_send(g, first):
        pads_top = [(0, 0), (0, n_side - corner), (0, 0)]
        pads_bottom = [(0, 0), (n_side - corner, 0), (0, 0)]
        return (
            g
            + jnp.pad(add_top[:, first : first + corner], pads_top)
            + jnp.pad(add_bottom[:, first : first + corner], pads_bottom)
        ).astype(bf16)

    back_right = lax.ppermute(side_send(left_g, edge), "lon", left_pairs)
    back_left = lax.ppermute(side_send(right_g, edge + corner), "lon", right_pairs)
    pole_g_mid = lax.ppermute(pole_g[:, :edge], both, pole_pairs)
    unfolded_mid = jnp.take(pole_g_mid, pole_dst[:edge], axis=1).astype(f32)
    north_mid = jnp.where(at_north, unfolded_mid, 0.0)
    south_mid = jnp.where(at_south, unfolded_mid, 0.0)

    def final_of(c, own):
        block = own.reshape(height, width, features)
        row_pad = [(0, 0), (0, 0)]
        block = (
            block
            + jnp.pad((add_top[c, :edge] + north_mid[c]).reshape(r, width, features), [(0, height - r)] + row_pad)
            + jnp.pad((add_bottom[c, :edge] + south_mid[c]).reshape(r, width, features), [(height - r, 0)] + row_pad)
            + jnp.pad(
                back_left[c].reshape(height, r, features).astype(f32), [(0, 0), (0, width - r), (0, 0)]
            )
            + jnp.pad(
                back_right[c].reshape(height, r, features).astype(f32), [(0, 0), (width - r, 0), (0, 0)]
            )
        )
        return block.astype(bf16)

    return (dq.reshape(height, width, features), final_of(0, dk_own), final_of(1, dv_own))


def solution(mesh):
    placed = (
        P("lat", "lon", None),
        P("lat", "lon", None),
        P("lat", "lon", None),
        P("lat", "lon", None),
        P(),
    )
    return jax.shard_map(
        on_device,
        mesh=mesh,
        in_specs=placed,
        out_specs=(P("lat", "lon", None), P("lat", "lon", None), P("lat", "lon", None)),
        check_vma=False,
    )
```

```python
import jax
import jax.numpy as jnp
import numpy as np
from jax import lax
from jax.experimental import pallas as pl
from jax.experimental.pallas import tpu as pltpu
from jax.sharding import PartitionSpec as P

HEADS = 16
HEAD_DIM = 64
RADIUS = 4

SPAN = 2 * RADIUS + 1
TILE_ROWS = 8
LANES = 128


def attention_kernel(width, *refs):
    (q_ref, g_ref, k_own, v_own, top_in, bot_in, left_in, right_in) = refs[:8]
    (dq_ref, dk_own, dv_own, top_out, bot_out, left_out, right_out) = refs[8:15]
    bias_ref = refs[15]
    scale = HEAD_DIM ** (-0.5)
    r = RADIUS
    tq = TILE_ROWS * width
    main = 2 * TILE_ROWS * width
    side = 2 * TILE_ROWS * r
    tk = main + 2 * side
    edge = r * width
    corner = r * r
    pairs = q_ref.shape[1] // LANES

    qi = lax.broadcasted_iota(jnp.int32, (2 * tq, tk), 0).astype(jnp.float32)
    ki = lax.broadcasted_iota(jnp.int32, (2 * tq, tk), 1).astype(jnp.float32)
    qi = jnp.where(qi >= tq, qi - tq, qi)
    qr = jnp.floor((qi + 0.5) * (1.0 / width))
    qc = qi - width * qr
    in_main = ki < main
    in_left = (ki >= main) & (ki < main + side)
    kk = jnp.where(in_main, ki, jnp.where(in_left, ki - main, ki - main - side))
    per_row = jnp.where(in_main, float(width), float(r))
    kr = jnp.floor((kk + 0.5) / per_row)
    kc = kk - per_row * kr + jnp.where(in_main, float(r), jnp.where(in_left, 0.0, float(width + r)))
    dr = kr - qr
    dc = kc - qc
    ok = (dr >= 0) & (dr <= 2 * r) & (dc >= 0) & (dc <= 2 * r)
    bias_ref[...] = jnp.where(ok, 0.0, -jnp.inf).astype(jnp.float32)

    nt = (((1,), (1,)), ((), ()))
    tn = (((0,), (0,)), ((), ()))

    def both_heads(qab, gab, kp, vp):
        s = lax.dot_general(qab, kp, nt, preferred_element_type=jnp.float32) * scale + bias_ref[...]
        m = jnp.max(s, axis=1, keepdims=True)
        e = jnp.exp(s - m)
        total = jnp.sum(e, axis=1, keepdims=True)
        w = e * (1.0 / total)
        dw = lax.dot_general(gab, vp, nt, preferred_element_type=jnp.float32)
        corr = jnp.sum(w * dw, axis=1, keepdims=True)
        ds = (w * (dw - corr)).astype(jnp.bfloat16)
        return ds, w.astype(jnp.bfloat16)

    def gather_keys(own, c, t, lanes):
        rows = side - corner
        if t == 0:
            parts = [
                top_in[c, pl.ds(0, edge), lanes],
                own[pl.ds(0, main - edge), lanes],
                top_in[c, pl.ds(edge, corner), lanes],
                left_in[c, pl.ds(0, rows), lanes],
                top_in[c, pl.ds(edge + corner, corner), lanes],
                right_in[c, pl.ds(0, rows), lanes],
            ]
        else:
            start = left_in.shape[1] - rows
            parts = [
                own[pl.ds(edge, main - edge), lanes],
                bot_in[c, pl.ds(0, edge), lanes],
                left_in[c, pl.ds(start, rows), lanes],
                bot_in[c, pl.ds(edge, corner), lanes],
                right_in[c, pl.ds(start, rows), lanes],
                bot_in[c, pl.ds(edge + corner, corner), lanes],
            ]
        return jnp.concatenate(parts, axis=0)

    def scatter_grads(d, own, c, t, lanes):
        bf = jnp.bfloat16
        rows = side - corner
        n_side = left_out.shape[1]
        if t == 0:
            top_out[c, pl.ds(0, edge), lanes] = d[:edge].astype(bf)
            own[pl.ds(0, main - edge), lanes] = d[edge:main]
            top_out[c, pl.ds(edge, corner), lanes] = d[main : main + corner].astype(bf)
            left_out[c, pl.ds(0, rows), lanes] = d[main + corner : main + side]
            top_out[c, pl.ds(edge + corner, corner), lanes] = d[main + side : main + side + corner].astype(bf)
            right_out[c, pl.ds(0, rows), lanes] = d[main + side + corner :]
        else:
            shared = main - 2 * edge
            own[pl.ds(edge, shared), lanes] += d[:shared]
            own[pl.ds(edge + shared, edge), lanes] = d[shared : main - edge]
            bot_out[c, pl.ds(0, edge), lanes] = d[main - edge : main].astype(bf)
            start = n_side - rows
            overlap = rows - start
            left_out[c, pl.ds(start, overlap), lanes] += d[main : main + overlap]
            left_out[c, pl.ds(rows, n_side - rows), lanes] = d[main + overlap : main + rows]
            bot_out[c, pl.ds(edge, corner), lanes] = d[main + rows : main + side].astype(bf)
            right_out[c, pl.ds(start, overlap), lanes] += d[main + side : main + side + overlap]
            right_out[c, pl.ds(rows, n_side - rows), lanes] = d[main + side + overlap : main + side + rows]
            bot_out[c, pl.ds(edge + corner, corner), lanes] = d[main + side + rows :].astype(bf)

    def body(p, carry):
        lanes = pl.ds(pl.multiple_of(p * LANES, LANES), LANES)
        for t in range(2):
            qp = q_ref[pl.ds(t * tq, tq), lanes]
            gp = g_ref[pl.ds(t * tq, tq), lanes]
            kp = gather_keys(k_own, 0, t, lanes)
            vp = gather_keys(v_own, 1, t, lanes)
            lo = lax.broadcasted_iota(jnp.int32, qp.shape, 1) < HEAD_DIM
            zero = jnp.zeros_like(qp)
            qab = jnp.concatenate([jnp.where(lo, qp, zero), jnp.where(lo, zero, qp)], axis=0)
            gab = jnp.concatenate([jnp.where(lo, gp, zero), jnp.where(lo, zero, gp)], axis=0)
            ds, w = both_heads(qab, gab, kp, vp)
            dq_ab = jnp.dot(ds, kp, preferred_element_type=jnp.float32)
            dq = jnp.where(lo, dq_ab[:tq], dq_ab[tq:]) * scale
            dq_ref[pl.ds(t * tq, tq), lanes] = dq.astype(dq_ref.dtype)
            dk = lax.dot_general(ds, qab, tn, preferred_element_type=jnp.float32) * scale
            dv = lax.dot_general(w, gab, tn, preferred_element_type=jnp.float32)
            scatter_grads(dk, dk_own, 0, t, lanes)
            scatter_grads(dv, dv_own, 1, t, lanes)
        return carry

    lax.fori_loop(0, pairs, body, 0)


def attention_core(q2, g2, k2, v2, top_in, bot_in, left_in, right_in, width):
    cells, features = q2.shape
    r = RADIUS
    tq = TILE_ROWS * width
    tk = 2 * TILE_ROWS * (width + 2 * r)
    tiles = cells // tq
    assert tiles == 2
    flops = 10 * 2 * tq * tk * LANES * (features // LANES) * tiles
    vmem = pl.BlockSpec(memory_space=pltpu.VMEM)
    f32 = jnp.float32
    outs = (
        jax.ShapeDtypeStruct((cells, features), jnp.bfloat16),
        jax.ShapeDtypeStruct((cells, features), f32),
        jax.ShapeDtypeStruct((cells, features), f32),
        jax.ShapeDtypeStruct(top_in.shape, jnp.bfloat16),
        jax.ShapeDtypeStruct(bot_in.shape, jnp.bfloat16),
        jax.ShapeDtypeStruct(left_in.shape, f32),
        jax.ShapeDtypeStruct(right_in.shape, f32),
    )
    in_bytes = 2 * (4 * cells * features + top_in.size + bot_in.size + left_in.size + right_in.size)
    out_bytes = 2 * cells * features + 8 * cells * features + 2 * (top_in.size + bot_in.size) + 4 * (
        left_in.size + right_in.size
    )
    return pl.pallas_call(
        lambda *refs: attention_kernel(width, *refs),
        out_shape=outs,
        in_specs=[vmem] * 8,
        out_specs=tuple([vmem] * 7),
        scratch_shapes=[pltpu.VMEM((2 * tq, tk), jnp.float32)],
        cost_estimate=pl.CostEstimate(
            flops=flops,
            transcendentals=2 * tq * tk * HEADS * tiles,
            bytes_accessed=in_bytes + out_bytes,
        ),
        name="neighbourhood_attention_bwd",
    )(q2, g2, k2, v2, top_in, bot_in, left_in, right_in)


def on_device(queries, keys, values, grad_out, fold_cols):
    height, width, features = queries.shape
    n_lat = lax.axis_size("lat")
    n_lon = lax.axis_size("lon")
    half = n_lon // 2
    i = lax.axis_index("lat")
    j = lax.axis_index("lon")
    at_north = i == 0
    at_south = i == n_lat - 1
    partner_j = (j + half) % n_lon
    r = RADIUS
    f32 = jnp.float32
    bf16 = jnp.bfloat16
    cells = height * width
    edge = r * width
    corner = r * r

    def flat(a, b):
        return a * n_lon + b

    down_pairs = [(flat(a, b), flat(a + 1, b)) for a in range(n_lat - 1) for b in range(n_lon)]
    up_pairs = [(flat(a + 1, b), flat(a, b)) for a in range(n_lat - 1) for b in range(n_lon)]
    pole_pairs = [(flat(a, b), flat(a, (b + half) % n_lon)) for a in (0, n_lat - 1) for b in range(n_lon)]
    right_pairs = [(b, (b + 1) % n_lon) for b in range(n_lon)]
    left_pairs = [(b, (b - 1) % n_lon) for b in range(n_lon)]
    both = ("lat", "lon")

    ext_w = width + 2 * r
    n_cols = n_lon * width
    my_ext_cols = (j * width - r + jnp.arange(ext_w)) % n_cols
    partner_ext_cols = (partner_j * width - r + jnp.arange(ext_w)) % n_cols
    fold_row = jnp.where(at_north, fold_cols[0], fold_cols[1])
    fold_idx = (jnp.take(fold_row, my_ext_cols) - (partner_j * width - r)) % n_cols
    landing = (jnp.take(fold_row, partner_ext_cols) - (j * width - r)) % n_cols
    unfold_idx = jnp.zeros((ext_w,), jnp.int32).at[landing].set(jnp.arange(ext_w, dtype=jnp.int32))

    strip_row = np.concatenate([np.arange(edge) // width, np.arange(corner) // r, np.arange(corner) // r])
    strip_col = np.concatenate(
        [r + np.arange(edge) % width, np.arange(corner) % r, width + r + np.arange(corner) % r]
    )

    def strip_cell(row, col):
        return jnp.where(
            col < r,
            edge + row * r + col,
            jnp.where(col >= width + r, edge + corner + row * r + col - width - r, row * width + col - r),
        )

    pole_src = strip_cell(r - 1 - strip_row, jnp.take(fold_idx, strip_col))
    pole_dst = strip_cell(r - 1 - strip_row, jnp.take(unfold_idx, strip_col))

    def pair(a, b):
        return jnp.stack([a, b])

    kf = keys.reshape(cells, features)
    vf = values.reshape(cells, features)

    def cols(x, a, b):
        return x[:, a:b].reshape(height * (b - a), features)

    from_left = lax.ppermute(pair(cols(keys, width - r, width), cols(values, width - r, width)), "lon", right_pairs)
    from_right = lax.ppermute(pair(cols(keys, 0, r), cols(values, 0, r)), "lon", left_pairs)
    top_mid = pair(kf[:edge], vf[:edge])
    bottom_mid = pair(kf[cells - edge :], vf[cells - edge :])
    pole_mid = lax.ppermute(jnp.where(at_north, top_mid, bottom_mid), both, pole_pairs)
    n_side = height * r
    top_send = jnp.concatenate([top_mid, from_left[:, :corner], from_right[:, :corner]], axis=1)
    bottom_send = jnp.concatenate(
        [bottom_mid, from_left[:, n_side - corner :], from_right[:, n_side - corner :]], axis=1
    )
    from_above = lax.ppermute(bottom_send, both, down_pairs)
    from_below = lax.ppermute(top_send, both, up_pairs)
    pole_corners = lax.ppermute(
        jnp.where(at_north, top_send[:, edge:], bottom_send[:, edge:]), both, pole_pairs
    )
    pole_strip = jnp.concatenate(
        [jnp.take(pole_mid, pole_src[:edge], axis=1), jnp.take(pole_corners, pole_src[edge:] - edge, axis=1)],
        axis=1,
    )
    top = jnp.where(at_north, pole_strip, from_above)
    bottom = jnp.where(at_south, pole_strip, from_below)

    dq, dk_own, dv_own, top_g, bottom_g, left_g, right_g = attention_core(
        queries.reshape(cells, features),
        grad_out.reshape(cells, features),
        kf,
        vf,
        top,
        bottom,
        from_left,
        from_right,
        width,
    )

    up_recv = lax.ppermute(top_g, both, up_pairs)
    down_recv = lax.ppermute(bottom_g, both, down_pairs)
    pole_g = jnp.where(at_north, top_g, bottom_g)
    pole_g_corners = lax.ppermute(pole_g[:, edge:], both, pole_pairs)
    unfolded_corners = jnp.take(pole_g_corners, pole_dst[edge:] - edge, axis=1)
    zero_mid = jnp.zeros_like(up_recv[:, :edge])
    add_top = jnp.where(
        at_north, jnp.concatenate([zero_mid, unfolded_corners], axis=1), down_recv
    ).astype(f32)
    add_bottom = jnp.where(
        at_south, jnp.concatenate([zero_mid, unfolded_corners], axis=1), up_recv
    ).astype(f32)

    def side_send(g, first):
        pads_top = [(0, 0), (0, n_side - corner), (0, 0)]
        pads_bottom = [(0, 0), (n_side - corner, 0), (0, 0)]
        return (
            g
            + jnp.pad(add_top[:, first : first + corner], pads_top)
            + jnp.pad(add_bottom[:, first : first + corner], pads_bottom)
        ).astype(bf16)

    back_right = lax.ppermute(side_send(left_g, edge), "lon", left_pairs)
    back_left = lax.ppermute(side_send(right_g, edge + corner), "lon", right_pairs)
    pole_g_mid = lax.ppermute(pole_g[:, :edge], both, pole_pairs)
    unfolded_mid = jnp.take(pole_g_mid, pole_dst[:edge], axis=1).astype(f32)
    north_mid = jnp.where(at_north, unfolded_mid, 0.0)
    south_mid = jnp.where(at_south, unfolded_mid, 0.0)

    def final_of(c, own):
        block = own.reshape(height, width, features)
        row_pad = [(0, 0), (0, 0)]
        block = (
            block
            + jnp.pad((add_top[c, :edge] + north_mid[c]).reshape(r, width, features), [(0, height - r)] + row_pad)
            + jnp.pad((add_bottom[c, :edge] + south_mid[c]).reshape(r, width, features), [(height - r, 0)] + row_pad)
            + jnp.pad(
                back_left[c].reshape(height, r, features).astype(f32), [(0, 0), (0, width - r), (0, 0)]
            )
            + jnp.pad(
                back_right[c].reshape(height, r, features).astype(f32), [(0, 0), (width - r, 0), (0, 0)]
            )
        )
        return block.astype(bf16)

    return (dq.reshape(height, width, features), final_of(0, dk_own), final_of(1, dv_own))


def solution(mesh):
    placed = (
        P("lat", "lon", None),
        P("lat", "lon", None),
        P("lat", "lon", None),
        P("lat", "lon", None),
        P(),
    )
    return jax.shard_map(
        on_device,
        mesh=mesh,
        in_specs=placed,
        out_specs=(P("lat", "lon", None), P("lat", "lon", None), P("lat", "lon", None)),
        check_vma=False,
    )
```

```python
import jax
import jax.numpy as jnp
import numpy as np
from jax import lax
from jax.experimental import pallas as pl
from jax.experimental.pallas import tpu as pltpu
from jax.sharding import PartitionSpec as P

HEADS = 16
HEAD_DIM = 64
RADIUS = 4

SPAN = 2 * RADIUS + 1
TILE_ROWS = 8
LANES = 128


def attention_kernel(width, *refs):
    (q_ref, g_ref, k_own, v_own, above_in, below_in, pole_mid_in, pole_corner_in, left_in, right_in, flag_ref) = refs[:11]
    (dq_ref, dk_own, dv_own, top_out, bot_out, left_out, right_out, pole_mid_out, pole_corner_out) = refs[11:20]
    bias_ref = refs[20]
    north = flag_ref[0:1, :] > 0.5
    south = flag_ref[1:2, :] > 0.5

    class Strip:
        def __init__(self, neighbour, pole):
            self.neighbour, self.pole = neighbour, pole

        def __getitem__(self, index):
            c, cells, lanes = index
            if cells.start >= edge:
                pole = self.pole_corner_ref[c, pl.ds(cells.start - edge, cells.size), lanes]
            else:
                pole = pole_mid_in[c, cells, lanes]
            return jnp.where(self.pole, pole, self.neighbour[c, cells, lanes])

    top_in = Strip(above_in, north)
    bot_in = Strip(below_in, south)
    top_in.pole_corner_ref = pole_corner_in
    bot_in.pole_corner_ref = pole_corner_in
    scale = HEAD_DIM ** (-0.5)
    r = RADIUS
    tq = TILE_ROWS * width
    main = 2 * TILE_ROWS * width
    side = 2 * TILE_ROWS * r
    tk = main + 2 * side
    edge = r * width
    corner = r * r
    pairs = q_ref.shape[1] // LANES

    qi = lax.broadcasted_iota(jnp.int32, (2 * tq, tk), 0).astype(jnp.float32)
    ki = lax.broadcasted_iota(jnp.int32, (2 * tq, tk), 1).astype(jnp.float32)
    qi = jnp.where(qi >= tq, qi - tq, qi)
    qr = jnp.floor((qi + 0.5) * (1.0 / width))
    qc = qi - width * qr
    in_main = ki < main
    in_left = (ki >= main) & (ki < main + side)
    kk = jnp.where(in_main, ki, jnp.where(in_left, ki - main, ki - main - side))
    per_row = jnp.where(in_main, float(width), float(r))
    kr = jnp.floor((kk + 0.5) / per_row)
    kc = kk - per_row * kr + jnp.where(in_main, float(r), jnp.where(in_left, 0.0, float(width + r)))
    dr = kr - qr
    dc = kc - qc
    ok = (dr >= 0) & (dr <= 2 * r) & (dc >= 0) & (dc <= 2 * r)
    bias_ref[...] = jnp.where(ok, 0.0, -jnp.inf).astype(jnp.float32)

    nt = (((1,), (1,)), ((), ()))
    tn = (((0,), (0,)), ((), ()))

    def both_heads(qab, gab, kp, vp):
        s = lax.dot_general(qab, kp, nt, preferred_element_type=jnp.float32) * scale + bias_ref[...]
        m = jnp.max(s, axis=1, keepdims=True)
        e = jnp.exp(s - m)
        total = jnp.sum(e, axis=1, keepdims=True)
        w = e * (1.0 / total)
        dw = lax.dot_general(gab, vp, nt, preferred_element_type=jnp.float32)
        corr = jnp.sum(w * dw, axis=1, keepdims=True)
        ds = (w * (dw - corr)).astype(jnp.bfloat16)
        return ds, w.astype(jnp.bfloat16)

    def gather_keys(own, c, t, lanes):
        rows = side - corner
        if t == 0:
            parts = [
                top_in[c, pl.ds(0, edge), lanes],
                own[pl.ds(0, main - edge), lanes],
                top_in[c, pl.ds(edge, corner), lanes],
                left_in[c, pl.ds(0, rows), lanes],
                top_in[c, pl.ds(edge + corner, corner), lanes],
                right_in[c, pl.ds(0, rows), lanes],
            ]
        else:
            start = left_in.shape[1] - rows
            parts = [
                own[pl.ds(edge, main - edge), lanes],
                bot_in[c, pl.ds(0, edge), lanes],
                left_in[c, pl.ds(start, rows), lanes],
                bot_in[c, pl.ds(edge, corner), lanes],
                right_in[c, pl.ds(start, rows), lanes],
                bot_in[c, pl.ds(edge + corner, corner), lanes],
            ]
        return jnp.concatenate(parts, axis=0)

    def put_strip(out, c, start, piece, t):
        bf = jnp.bfloat16
        piece = piece.astype(bf)
        out[c, pl.ds(start, piece.shape[0]), lanes_now[0]] = piece
        if start < edge:
            pole_ref, pole_start = pole_mid_out, start
        else:
            pole_ref, pole_start = pole_corner_out, start - edge
        index = (c, pl.ds(pole_start, piece.shape[0]), lanes_now[0])
        if t == 0:
            pole_ref[index] = piece
        else:
            pole_ref[index] = jnp.where(south, piece, pole_ref[index])

    lanes_now = [None]

    def scatter_grads(d, own, c, t, lanes):
        rows = side - corner
        n_side = left_out.shape[1]
        lanes_now[0] = lanes
        if t == 0:
            put_strip(top_out, c, 0, d[:edge], t)
            own[pl.ds(0, main - edge), lanes] = d[edge:main]
            put_strip(top_out, c, edge, d[main : main + corner], t)
            left_out[c, pl.ds(0, rows), lanes] = d[main + corner : main + side]
            put_strip(top_out, c, edge + corner, d[main + side : main + side + corner], t)
            right_out[c, pl.ds(0, rows), lanes] = d[main + side + corner :]
        else:
            shared = main - 2 * edge
            own[pl.ds(edge, shared), lanes] += d[:shared]
            own[pl.ds(edge + shared, edge), lanes] = d[shared : main - edge]
            put_strip(bot_out, c, 0, d[main - edge : main], t)
            start = n_side - rows
            overlap = rows - start
            left_out[c, pl.ds(start, overlap), lanes] += d[main : main + overlap]
            left_out[c, pl.ds(rows, n_side - rows), lanes] = d[main + overlap : main + rows]
            put_strip(bot_out, c, edge, d[main + rows : main + side], t)
            right_out[c, pl.ds(start, overlap), lanes] += d[main + side : main + side + overlap]
            right_out[c, pl.ds(rows, n_side - rows), lanes] = d[main + side + overlap : main + side + rows]
            put_strip(bot_out, c, edge + corner, d[main + side + rows :], t)

    def body(p, carry):
        lanes = pl.ds(pl.multiple_of(p * LANES, LANES), LANES)
        for t in range(2):
            qp = q_ref[pl.ds(t * tq, tq), lanes]
            gp = g_ref[pl.ds(t * tq, tq), lanes]
            kp = gather_keys(k_own, 0, t, lanes)
            vp = gather_keys(v_own, 1, t, lanes)
            lo = lax.broadcasted_iota(jnp.int32, qp.shape, 1) < HEAD_DIM
            zero = jnp.zeros_like(qp)
            qab = jnp.concatenate([jnp.where(lo, qp, zero), jnp.where(lo, zero, qp)], axis=0)
            gab = jnp.concatenate([jnp.where(lo, gp, zero), jnp.where(lo, zero, gp)], axis=0)
            ds, w = both_heads(qab, gab, kp, vp)
            dq_ab = jnp.dot(ds, kp, preferred_element_type=jnp.float32)
            dq = jnp.where(lo, dq_ab[:tq], dq_ab[tq:]) * scale
            dq_ref[pl.ds(t * tq, tq), lanes] = dq.astype(dq_ref.dtype)
            dk = lax.dot_general(ds, qab, tn, preferred_element_type=jnp.float32) * scale
            dv = lax.dot_general(w, gab, tn, preferred_element_type=jnp.float32)
            scatter_grads(dk, dk_own, 0, t, lanes)
            scatter_grads(dv, dv_own, 1, t, lanes)
        return carry

    lax.fori_loop(0, pairs, body, 0)


def attention_core(q2, g2, k2, v2, above, below, pole_mid, pole_corner, left_in, right_in, flags, width):
    cells, features = q2.shape
    r = RADIUS
    tq = TILE_ROWS * width
    tk = 2 * TILE_ROWS * (width + 2 * r)
    tiles = cells // tq
    assert tiles == 2
    flops = 10 * 2 * tq * tk * LANES * (features // LANES) * tiles
    vmem = pl.BlockSpec(memory_space=pltpu.VMEM)
    f32 = jnp.float32
    outs = (
        jax.ShapeDtypeStruct((cells, features), jnp.bfloat16),
        jax.ShapeDtypeStruct((cells, features), f32),
        jax.ShapeDtypeStruct((cells, features), f32),
        jax.ShapeDtypeStruct(above.shape, jnp.bfloat16),
        jax.ShapeDtypeStruct(below.shape, jnp.bfloat16),
        jax.ShapeDtypeStruct(left_in.shape, f32),
        jax.ShapeDtypeStruct(right_in.shape, f32),
        jax.ShapeDtypeStruct(pole_mid.shape, jnp.bfloat16),
        jax.ShapeDtypeStruct(pole_corner.shape, jnp.bfloat16),
    )
    strips = above.size + below.size + pole_mid.size + pole_corner.size
    in_bytes = 2 * (4 * cells * features + strips + left_in.size + right_in.size)
    out_bytes = 10 * cells * features + 2 * strips + 4 * (left_in.size + right_in.size)
    return pl.pallas_call(
        lambda *refs: attention_kernel(width, *refs),
        out_shape=outs,
        in_specs=[vmem] * 11,
        out_specs=tuple([vmem] * 9),
        scratch_shapes=[pltpu.VMEM((2 * tq, tk), jnp.float32)],
        cost_estimate=pl.CostEstimate(
            flops=flops,
            transcendentals=2 * tq * tk * HEADS * tiles,
            bytes_accessed=in_bytes + out_bytes,
        ),
        name="neighbourhood_attention_bwd",
    )(q2, g2, k2, v2, above, below, pole_mid, pole_corner, left_in, right_in, flags)


def on_device(queries, keys, values, grad_out, fold_cols):
    height, width, features = queries.shape
    n_lat = lax.axis_size("lat")
    n_lon = lax.axis_size("lon")
    half = n_lon // 2
    i = lax.axis_index("lat")
    j = lax.axis_index("lon")
    at_north = i == 0
    at_south = i == n_lat - 1
    partner_j = (j + half) % n_lon
    r = RADIUS
    f32 = jnp.float32
    bf16 = jnp.bfloat16
    cells = height * width
    edge = r * width
    corner = r * r

    def flat(a, b):
        return a * n_lon + b

    down_pairs = [(flat(a, b), flat(a + 1, b)) for a in range(n_lat - 1) for b in range(n_lon)]
    up_pairs = [(flat(a + 1, b), flat(a, b)) for a in range(n_lat - 1) for b in range(n_lon)]
    pole_pairs = [(flat(a, b), flat(a, (b + half) % n_lon)) for a in (0, n_lat - 1) for b in range(n_lon)]
    right_pairs = [(b, (b + 1) % n_lon) for b in range(n_lon)]
    left_pairs = [(b, (b - 1) % n_lon) for b in range(n_lon)]
    both = ("lat", "lon")

    ext_w = width + 2 * r
    n_cols = n_lon * width
    my_ext_cols = (j * width - r + jnp.arange(ext_w)) % n_cols
    partner_ext_cols = (partner_j * width - r + jnp.arange(ext_w)) % n_cols
    fold_row = jnp.where(at_north, fold_cols[0], fold_cols[1])
    fold_idx = (jnp.take(fold_row, my_ext_cols) - (partner_j * width - r)) % n_cols
    landing = (jnp.take(fold_row, partner_ext_cols) - (j * width - r)) % n_cols
    unfold_idx = jnp.zeros((ext_w,), jnp.int32).at[landing].set(jnp.arange(ext_w, dtype=jnp.int32))

    strip_row = np.concatenate([np.arange(edge) // width, np.arange(corner) // r, np.arange(corner) // r])
    strip_col = np.concatenate(
        [r + np.arange(edge) % width, np.arange(corner) % r, width + r + np.arange(corner) % r]
    )

    def strip_cell(row, col):
        return jnp.where(
            col < r,
            edge + row * r + col,
            jnp.where(col >= width + r, edge + corner + row * r + col - width - r, row * width + col - r),
        )

    pole_src = strip_cell(r - 1 - strip_row, jnp.take(fold_idx, strip_col))
    pole_dst = strip_cell(r - 1 - strip_row, jnp.take(unfold_idx, strip_col))

    def pair(a, b):
        return jnp.stack([a, b])

    kf = keys.reshape(cells, features)
    vf = values.reshape(cells, features)

    def cols(x, a, b):
        return x[:, a:b].reshape(height * (b - a), features)

    from_left = lax.ppermute(pair(cols(keys, width - r, width), cols(values, width - r, width)), "lon", right_pairs)
    from_right = lax.ppermute(pair(cols(keys, 0, r), cols(values, 0, r)), "lon", left_pairs)
    top_mid = pair(kf[:edge], vf[:edge])
    bottom_mid = pair(kf[cells - edge :], vf[cells - edge :])
    pole_mid = lax.ppermute(jnp.where(at_north, top_mid, bottom_mid), both, pole_pairs)
    n_side = height * r
    top_send = jnp.concatenate([top_mid, from_left[:, :corner], from_right[:, :corner]], axis=1)
    bottom_send = jnp.concatenate(
        [bottom_mid, from_left[:, n_side - corner :], from_right[:, n_side - corner :]], axis=1
    )
    from_above = lax.ppermute(bottom_send, both, down_pairs)
    from_below = lax.ppermute(top_send, both, up_pairs)
    pole_corners = lax.ppermute(
        jnp.where(at_north, top_send[:, edge:], bottom_send[:, edge:]), both, pole_pairs
    )
    pole_mid_rows = jnp.take(pole_mid, pole_src[:edge], axis=1)
    pole_corner_rows = jnp.take(pole_corners, pole_src[edge:] - edge, axis=1)
    flags = jnp.stack(
        [jnp.full((LANES,), at_north, f32), jnp.full((LANES,), at_south, f32)]
        + [jnp.zeros((LANES,), f32)] * 6
    )

    q2 = queries.reshape(cells, features)
    g2 = grad_out.reshape(cells, features)
    dq, dk_own, dv_own, top_g, bottom_g, left_g, right_g, pole_g_mid_send, pole_g_corner_send = attention_core(
        q2, g2, kf, vf, from_above, from_below, pole_mid_rows, pole_corner_rows, from_left, from_right, flags, width
    )

    up_recv = lax.ppermute(top_g, both, up_pairs)
    down_recv = lax.ppermute(bottom_g, both, down_pairs)
    pole_g_corners = lax.ppermute(pole_g_corner_send, both, pole_pairs)
    unfolded_corners = jnp.take(pole_g_corners, pole_dst[edge:] - edge, axis=1)
    zero_mid = jnp.zeros_like(up_recv[:, :edge])
    add_top = jnp.where(
        at_north, jnp.concatenate([zero_mid, unfolded_corners], axis=1), down_recv
    ).astype(f32)
    add_bottom = jnp.where(
        at_south, jnp.concatenate([zero_mid, unfolded_corners], axis=1), up_recv
    ).astype(f32)

    def side_send(g, first):
        pads_top = [(0, 0), (0, n_side - corner), (0, 0)]
        pads_bottom = [(0, 0), (n_side - corner, 0), (0, 0)]
        return (
            g
            + jnp.pad(add_top[:, first : first + corner], pads_top)
            + jnp.pad(add_bottom[:, first : first + corner], pads_bottom)
        ).astype(bf16)

    back_right = lax.ppermute(side_send(left_g, edge), "lon", left_pairs)
    back_left = lax.ppermute(side_send(right_g, edge + corner), "lon", right_pairs)
    pole_g_mid = lax.ppermute(pole_g_mid_send, both, pole_pairs)
    unfolded_mid = jnp.take(pole_g_mid, pole_dst[:edge], axis=1).astype(f32)
    north_mid = jnp.where(at_north, unfolded_mid, 0.0)
    south_mid = jnp.where(at_south, unfolded_mid, 0.0)

    def final_of(c, own):
        block = own.reshape(height, width, features)
        row_pad = [(0, 0), (0, 0)]
        block = (
            block
            + jnp.pad((add_top[c, :edge] + north_mid[c]).reshape(r, width, features), [(0, height - r)] + row_pad)
            + jnp.pad((add_bottom[c, :edge] + south_mid[c]).reshape(r, width, features), [(height - r, 0)] + row_pad)
            + jnp.pad(
                back_left[c].reshape(height, r, features).astype(f32), [(0, 0), (0, width - r), (0, 0)]
            )
            + jnp.pad(
                back_right[c].reshape(height, r, features).astype(f32), [(0, 0), (width - r, 0), (0, 0)]
            )
        )
        return block.astype(bf16)

    return (dq.reshape(height, width, features), final_of(0, dk_own), final_of(1, dv_own))


def solution(mesh):
    placed = (
        P("lat", "lon", None),
        P("lat", "lon", None),
        P("lat", "lon", None),
        P("lat", "lon", None),
        P(),
    )
    return jax.shard_map(
        on_device,
        mesh=mesh,
        in_specs=placed,
        out_specs=(P("lat", "lon", None), P("lat", "lon", None), P("lat", "lon", None)),
        check_vma=False,
    )
```

```python
import jax
import jax.numpy as jnp
import numpy as np
from jax import lax
from jax.experimental import pallas as pl
from jax.experimental.pallas import tpu as pltpu
from jax.sharding import PartitionSpec as P

HEADS = 16
HEAD_DIM = 64
RADIUS = 4

SPAN = 2 * RADIUS + 1
TILE_ROWS = 8
LANES = 128


def attention_kernel(width, n_lat, *refs):
    (q_ref, g_ref, k_own, v_own, above_in, below_in, pole_mid_in, pole_corner_in, left_in, right_in) = refs[:10]
    (dq_ref, dk_own, dv_own, top_out, bot_out, left_out, right_out, pole_mid_out, pole_corner_out) = refs[10:19]
    bias_ref = refs[19]
    lat = lax.axis_index("lat")
    north = lat == 0
    south = lat == n_lat - 1

    class Strip:
        def __init__(self, neighbour, pole):
            self.neighbour, self.pole = neighbour, pole

        def __getitem__(self, index):
            c, cells, lanes = index
            if cells.start >= edge:
                pole = self.pole_corner_ref[c, pl.ds(cells.start - edge, cells.size), lanes]
            else:
                pole = pole_mid_in[c, cells, lanes]
            return jnp.where(self.pole, pole, self.neighbour[c, cells, lanes])

    top_in = Strip(above_in, north)
    bot_in = Strip(below_in, south)
    top_in.pole_corner_ref = pole_corner_in
    bot_in.pole_corner_ref = pole_corner_in
    scale = HEAD_DIM ** (-0.5)
    r = RADIUS
    tq = TILE_ROWS * width
    main = 2 * TILE_ROWS * width
    side = 2 * TILE_ROWS * r
    tk = main + 2 * side
    edge = r * width
    corner = r * r
    pairs = q_ref.shape[1] // LANES

    qi = lax.broadcasted_iota(jnp.int32, (2 * tq, tk), 0).astype(jnp.float32)
    ki = lax.broadcasted_iota(jnp.int32, (2 * tq, tk), 1).astype(jnp.float32)
    qi = jnp.where(qi >= tq, qi - tq, qi)
    qr = jnp.floor((qi + 0.5) * (1.0 / width))
    qc = qi - width * qr
    in_main = ki < main
    in_left = (ki >= main) & (ki < main + side)
    kk = jnp.where(in_main, ki, jnp.where(in_left, ki - main, ki - main - side))
    per_row = jnp.where(in_main, float(width), float(r))
    kr = jnp.floor((kk + 0.5) / per_row)
    kc = kk - per_row * kr + jnp.where(in_main, float(r), jnp.where(in_left, 0.0, float(width + r)))
    dr = kr - qr
    dc = kc - qc
    ok = (dr >= 0) & (dr <= 2 * r) & (dc >= 0) & (dc <= 2 * r)
    bias_ref[...] = jnp.where(ok, 0.0, -jnp.inf).astype(jnp.float32)

    nt = (((1,), (1,)), ((), ()))
    tn = (((0,), (0,)), ((), ()))

    def both_heads(qab, gab, kp, vp):
        s = lax.dot_general(qab, kp, nt, preferred_element_type=jnp.float32) * scale + bias_ref[...]
        m = jnp.max(s, axis=1, keepdims=True)
        e = jnp.exp(s - m)
        total = jnp.sum(e, axis=1, keepdims=True)
        w = e * (1.0 / total)
        dw = lax.dot_general(gab, vp, nt, preferred_element_type=jnp.float32)
        corr = jnp.sum(w * dw, axis=1, keepdims=True)
        ds = (w * (dw - corr)).astype(jnp.bfloat16)
        return ds, w.astype(jnp.bfloat16)

    def gather_keys(own, c, t, lanes):
        rows = side - corner
        if t == 0:
            parts = [
                top_in[c, pl.ds(0, edge), lanes],
                own[pl.ds(0, main - edge), lanes],
                top_in[c, pl.ds(edge, corner), lanes],
                left_in[c, pl.ds(0, rows), lanes],
                top_in[c, pl.ds(edge + corner, corner), lanes],
                right_in[c, pl.ds(0, rows), lanes],
            ]
        else:
            start = left_in.shape[1] - rows
            parts = [
                own[pl.ds(edge, main - edge), lanes],
                bot_in[c, pl.ds(0, edge), lanes],
                left_in[c, pl.ds(start, rows), lanes],
                bot_in[c, pl.ds(edge, corner), lanes],
                right_in[c, pl.ds(start, rows), lanes],
                bot_in[c, pl.ds(edge + corner, corner), lanes],
            ]
        return jnp.concatenate(parts, axis=0)

    def put_strip(out, c, start, piece, t):
        bf = jnp.bfloat16
        piece = piece.astype(bf)
        out[c, pl.ds(start, piece.shape[0]), lanes_now[0]] = piece
        if start < edge:
            pole_ref, pole_start = pole_mid_out, start
        else:
            pole_ref, pole_start = pole_corner_out, start - edge
        index = (c, pl.ds(pole_start, piece.shape[0]), lanes_now[0])
        if t == 0:
            pole_ref[index] = piece
        else:
            pole_ref[index] = jnp.where(south, piece, pole_ref[index])

    lanes_now = [None]

    def scatter_grads(d, own, c, t, lanes):
        rows = side - corner
        n_side = left_out.shape[1]
        lanes_now[0] = lanes
        if t == 0:
            put_strip(top_out, c, 0, d[:edge], t)
            own[pl.ds(0, main - edge), lanes] = d[edge:main]
            put_strip(top_out, c, edge, d[main : main + corner], t)
            left_out[c, pl.ds(0, rows), lanes] = d[main + corner : main + side]
            put_strip(top_out, c, edge + corner, d[main + side : main + side + corner], t)
            right_out[c, pl.ds(0, rows), lanes] = d[main + side + corner :]
        else:
            shared = main - 2 * edge
            own[pl.ds(edge, shared), lanes] += d[:shared]
            own[pl.ds(edge + shared, edge), lanes] = d[shared : main - edge]
            put_strip(bot_out, c, 0, d[main - edge : main], t)
            start = n_side - rows
            overlap = rows - start
            left_out[c, pl.ds(start, overlap), lanes] += d[main : main + overlap]
            left_out[c, pl.ds(rows, n_side - rows), lanes] = d[main + overlap : main + rows]
            put_strip(bot_out, c, edge, d[main + rows : main + side], t)
            right_out[c, pl.ds(start, overlap), lanes] += d[main + side : main + side + overlap]
            right_out[c, pl.ds(rows, n_side - rows), lanes] = d[main + side + overlap : main + side + rows]
            put_strip(bot_out, c, edge + corner, d[main + side + rows :], t)

    def body(p, carry):
        lanes = pl.ds(pl.multiple_of(p * LANES, LANES), LANES)
        for t in range(2):
            qp = q_ref[pl.ds(t * tq, tq), lanes]
            gp = g_ref[pl.ds(t * tq, tq), lanes]
            kp = gather_keys(k_own, 0, t, lanes)
            vp = gather_keys(v_own, 1, t, lanes)
            lo = lax.broadcasted_iota(jnp.int32, qp.shape, 1) < HEAD_DIM
            zero = jnp.zeros_like(qp)
            qab = jnp.concatenate([jnp.where(lo, qp, zero), jnp.where(lo, zero, qp)], axis=0)
            gab = jnp.concatenate([jnp.where(lo, gp, zero), jnp.where(lo, zero, gp)], axis=0)
            ds, w = both_heads(qab, gab, kp, vp)
            dq_ab = jnp.dot(ds, kp, preferred_element_type=jnp.float32)
            dq = jnp.where(lo, dq_ab[:tq], dq_ab[tq:]) * scale
            dq_ref[pl.ds(t * tq, tq), lanes] = dq.astype(dq_ref.dtype)
            dk = lax.dot_general(ds, qab, tn, preferred_element_type=jnp.float32) * scale
            dv = lax.dot_general(w, gab, tn, preferred_element_type=jnp.float32)
            scatter_grads(dk, dk_own, 0, t, lanes)
            scatter_grads(dv, dv_own, 1, t, lanes)
        return carry

    lax.fori_loop(0, pairs, body, 0)


def attention_core(q2, g2, k2, v2, above, below, pole_mid, pole_corner, left_in, right_in, width, n_lat):
    cells, features = q2.shape
    r = RADIUS
    tq = TILE_ROWS * width
    tk = 2 * TILE_ROWS * (width + 2 * r)
    tiles = cells // tq
    assert tiles == 2
    flops = 10 * 2 * tq * tk * LANES * (features // LANES) * tiles
    vmem = pl.BlockSpec(memory_space=pltpu.VMEM)
    f32 = jnp.float32
    outs = (
        jax.ShapeDtypeStruct((cells, features), jnp.bfloat16),
        jax.ShapeDtypeStruct((cells, features), f32),
        jax.ShapeDtypeStruct((cells, features), f32),
        jax.ShapeDtypeStruct(above.shape, jnp.bfloat16),
        jax.ShapeDtypeStruct(below.shape, jnp.bfloat16),
        jax.ShapeDtypeStruct(left_in.shape, f32),
        jax.ShapeDtypeStruct(right_in.shape, f32),
        jax.ShapeDtypeStruct(pole_mid.shape, jnp.bfloat16),
        jax.ShapeDtypeStruct(pole_corner.shape, jnp.bfloat16),
    )
    strips = above.size + below.size + pole_mid.size + pole_corner.size
    in_bytes = 2 * (4 * cells * features + strips + left_in.size + right_in.size)
    out_bytes = 10 * cells * features + 2 * strips + 4 * (left_in.size + right_in.size)
    return pl.pallas_call(
        lambda *refs: attention_kernel(width, n_lat, *refs),
        out_shape=outs,
        in_specs=[vmem] * 10,
        out_specs=tuple([vmem] * 9),
        scratch_shapes=[pltpu.VMEM((2 * tq, tk), jnp.float32)],
        cost_estimate=pl.CostEstimate(
            flops=flops,
            transcendentals=2 * tq * tk * HEADS * tiles,
            bytes_accessed=in_bytes + out_bytes,
        ),
        name="neighbourhood_attention_bwd",
    )(q2, g2, k2, v2, above, below, pole_mid, pole_corner, left_in, right_in)


def on_device(queries, keys, values, grad_out, fold_cols):
    height, width, features = queries.shape
    n_lat = lax.axis_size("lat")
    n_lon = lax.axis_size("lon")
    half = n_lon // 2
    i = lax.axis_index("lat")
    j = lax.axis_index("lon")
    at_north = i == 0
    at_south = i == n_lat - 1
    partner_j = (j + half) % n_lon
    r = RADIUS
    f32 = jnp.float32
    bf16 = jnp.bfloat16
    cells = height * width
    edge = r * width
    corner = r * r

    def flat(a, b):
        return a * n_lon + b

    down_pairs = [(flat(a, b), flat(a + 1, b)) for a in range(n_lat - 1) for b in range(n_lon)]
    up_pairs = [(flat(a + 1, b), flat(a, b)) for a in range(n_lat - 1) for b in range(n_lon)]
    pole_pairs = [(flat(a, b), flat(a, (b + half) % n_lon)) for a in (0, n_lat - 1) for b in range(n_lon)]
    right_pairs = [(b, (b + 1) % n_lon) for b in range(n_lon)]
    left_pairs = [(b, (b - 1) % n_lon) for b in range(n_lon)]
    both = ("lat", "lon")

    ext_w = width + 2 * r
    n_cols = n_lon * width
    my_ext_cols = (j * width - r + jnp.arange(ext_w)) % n_cols
    partner_ext_cols = (partner_j * width - r + jnp.arange(ext_w)) % n_cols
    fold_row = jnp.where(at_north, fold_cols[0], fold_cols[1])
    fold_idx = (jnp.take(fold_row, my_ext_cols) - (partner_j * width - r)) % n_cols
    landing = (jnp.take(fold_row, partner_ext_cols) - (j * width - r)) % n_cols
    unfold_idx = jnp.zeros((ext_w,), jnp.int32).at[landing].set(jnp.arange(ext_w, dtype=jnp.int32))

    strip_row = np.concatenate([np.arange(edge) // width, np.arange(corner) // r, np.arange(corner) // r])
    strip_col = np.concatenate(
        [r + np.arange(edge) % width, np.arange(corner) % r, width + r + np.arange(corner) % r]
    )

    def strip_cell(row, col):
        return jnp.where(
            col < r,
            edge + row * r + col,
            jnp.where(col >= width + r, edge + corner + row * r + col - width - r, row * width + col - r),
        )

    pole_src = strip_cell(r - 1 - strip_row, jnp.take(fold_idx, strip_col))
    pole_dst = strip_cell(r - 1 - strip_row, jnp.take(unfold_idx, strip_col))

    def pair(a, b):
        return jnp.stack([a, b])

    kf = keys.reshape(cells, features)
    vf = values.reshape(cells, features)

    def cols(x, a, b):
        return x[:, a:b].reshape(height * (b - a), features)

    from_left = lax.ppermute(pair(cols(keys, width - r, width), cols(values, width - r, width)), "lon", right_pairs)
    from_right = lax.ppermute(pair(cols(keys, 0, r), cols(values, 0, r)), "lon", left_pairs)
    top_mid = pair(kf[:edge], vf[:edge])
    bottom_mid = pair(kf[cells - edge :], vf[cells - edge :])
    pole_mid = lax.ppermute(jnp.where(at_north, top_mid, bottom_mid), both, pole_pairs)
    n_side = height * r
    top_send = jnp.concatenate([top_mid, from_left[:, :corner], from_right[:, :corner]], axis=1)
    bottom_send = jnp.concatenate(
        [bottom_mid, from_left[:, n_side - corner :], from_right[:, n_side - corner :]], axis=1
    )
    from_above = lax.ppermute(bottom_send, both, down_pairs)
    from_below = lax.ppermute(top_send, both, up_pairs)
    pole_corners = lax.ppermute(
        jnp.where(at_north, top_send[:, edge:], bottom_send[:, edge:]), both, pole_pairs
    )
    pole_mid_rows = jnp.take(pole_mid, pole_src[:edge], axis=1)
    pole_corner_rows = jnp.take(pole_corners, pole_src[edge:] - edge, axis=1)

    q2 = queries.reshape(cells, features)
    g2 = grad_out.reshape(cells, features)
    dq, dk_own, dv_own, top_g, bottom_g, left_g, right_g, pole_g_mid_send, pole_g_corner_send = attention_core(
        q2, g2, kf, vf, from_above, from_below, pole_mid_rows, pole_corner_rows, from_left, from_right, width, n_lat
    )

    up_recv = lax.ppermute(top_g, both, up_pairs)
    down_recv = lax.ppermute(bottom_g, both, down_pairs)
    pole_g_corners = lax.ppermute(pole_g_corner_send, both, pole_pairs)
    unfolded_corners = jnp.take(pole_g_corners, pole_dst[edge:] - edge, axis=1)
    zero_mid = jnp.zeros_like(up_recv[:, :edge])
    add_top = jnp.where(
        at_north, jnp.concatenate([zero_mid, unfolded_corners], axis=1), down_recv
    ).astype(f32)
    add_bottom = jnp.where(
        at_south, jnp.concatenate([zero_mid, unfolded_corners], axis=1), up_recv
    ).astype(f32)

    def side_send(g, first):
        pads_top = [(0, 0), (0, n_side - corner), (0, 0)]
        pads_bottom = [(0, 0), (n_side - corner, 0), (0, 0)]
        return (
            g
            + jnp.pad(add_top[:, first : first + corner], pads_top)
            + jnp.pad(add_bottom[:, first : first + corner], pads_bottom)
        ).astype(bf16)

    back_right = lax.ppermute(side_send(left_g, edge), "lon", left_pairs)
    back_left = lax.ppermute(side_send(right_g, edge + corner), "lon", right_pairs)
    pole_g_mid = lax.ppermute(pole_g_mid_send, both, pole_pairs)
    unfolded_mid = jnp.take(pole_g_mid, pole_dst[:edge], axis=1).astype(f32)
    north_mid = jnp.where(at_north, unfolded_mid, 0.0)
    south_mid = jnp.where(at_south, unfolded_mid, 0.0)

    def final_of(c, own):
        block = own.reshape(height, width, features)
        row_pad = [(0, 0), (0, 0)]
        block = (
            block
            + jnp.pad((add_top[c, :edge] + north_mid[c]).reshape(r, width, features), [(0, height - r)] + row_pad)
            + jnp.pad((add_bottom[c, :edge] + south_mid[c]).reshape(r, width, features), [(height - r, 0)] + row_pad)
            + jnp.pad(
                back_left[c].reshape(height, r, features).astype(f32), [(0, 0), (0, width - r), (0, 0)]
            )
            + jnp.pad(
                back_right[c].reshape(height, r, features).astype(f32), [(0, 0), (width - r, 0), (0, 0)]
            )
        )
        return block.astype(bf16)

    return (dq.reshape(height, width, features), final_of(0, dk_own), final_of(1, dv_own))


def solution(mesh):
    placed = (
        P("lat", "lon", None),
        P("lat", "lon", None),
        P("lat", "lon", None),
        P("lat", "lon", None),
        P(),
    )
    return jax.shard_map(
        on_device,
        mesh=mesh,
        in_specs=placed,
        out_specs=(P("lat", "lon", None), P("lat", "lon", None), P("lat", "lon", None)),
        check_vma=False,
    )
```

```python
import jax
import jax.numpy as jnp
import numpy as np
from jax import lax
from jax.experimental import pallas as pl
from jax.experimental.pallas import tpu as pltpu
from jax.sharding import PartitionSpec as P

HEADS = 16
HEAD_DIM = 64
RADIUS = 4

SPAN = 2 * RADIUS + 1
TILE_ROWS = 8
LANES = 128


def attention_kernel(width, n_lat, *refs):
    (q_ref, g_ref, k_own, v_own, above_in, below_in, pole_mid_in, pole_corner_in, left_in, right_in) = refs[:10]
    (dq_ref, dk_own, dv_own, top_out, bot_out, left_out, right_out, pole_mid_out, pole_corner_out) = refs[10:19]
    bias_ref = refs[19]
    lat = lax.axis_index("lat")
    north = lat == 0
    south = lat == n_lat - 1

    class Strip:
        def __init__(self, neighbour, pole):
            self.neighbour, self.pole = neighbour, pole

        def __getitem__(self, index):
            c, cells, lanes = index
            if cells.start >= edge:
                pole = self.pole_corner_ref[c, pl.ds(cells.start - edge, cells.size), lanes]
            else:
                pole = pole_mid_in[c, cells, lanes]
            return jnp.where(self.pole, pole, self.neighbour[c, cells, lanes])

    top_in = Strip(above_in, north)
    bot_in = Strip(below_in, south)
    top_in.pole_corner_ref = pole_corner_in
    bot_in.pole_corner_ref = pole_corner_in
    scale = HEAD_DIM ** (-0.5)
    r = RADIUS
    tq = TILE_ROWS * width
    main = 2 * TILE_ROWS * width
    side = 2 * TILE_ROWS * r
    tk = main + 2 * side
    edge = r * width
    corner = r * r
    pairs = q_ref.shape[1] // LANES

    qi = lax.broadcasted_iota(jnp.int32, (2 * tq, tk), 0).astype(jnp.float32)
    ki = lax.broadcasted_iota(jnp.int32, (2 * tq, tk), 1).astype(jnp.float32)
    qi = jnp.where(qi >= tq, qi - tq, qi)
    qr = jnp.floor((qi + 0.5) * (1.0 / width))
    qc = qi - width * qr
    in_main = ki < main
    in_left = (ki >= main) & (ki < main + side)
    kk = jnp.where(in_main, ki, jnp.where(in_left, ki - main, ki - main - side))
    per_row = jnp.where(in_main, float(width), float(r))
    kr = jnp.floor((kk + 0.5) / per_row)
    kc = kk - per_row * kr + jnp.where(in_main, float(r), jnp.where(in_left, 0.0, float(width + r)))
    dr = kr - qr
    dc = kc - qc
    ok = (dr >= 0) & (dr <= 2 * r) & (dc >= 0) & (dc <= 2 * r)
    bias_ref[...] = jnp.where(ok, 0.0, -jnp.inf).astype(jnp.float32)

    nt = (((1,), (1,)), ((), ()))
    tn = (((0,), (0,)), ((), ()))

    def both_heads(qab, gab, kp, vp):
        s = lax.dot_general(qab, kp, nt, preferred_element_type=jnp.float32) * scale + bias_ref[...]
        m = jnp.max(s, axis=1, keepdims=True)
        e = jnp.exp(s - m)
        total = jnp.sum(e, axis=1, keepdims=True)
        w = e * (1.0 / total)
        dw = lax.dot_general(gab, vp, nt, preferred_element_type=jnp.float32)
        corr = jnp.sum(w * dw, axis=1, keepdims=True)
        ds = (w * (dw - corr)).astype(jnp.bfloat16)
        return ds, w.astype(jnp.bfloat16)

    def gather_keys(own, c, t, lanes):
        rows = side - corner
        if t == 0:
            parts = [
                top_in[c, pl.ds(0, edge), lanes],
                own[pl.ds(0, main - edge), lanes],
                top_in[c, pl.ds(edge, corner), lanes],
                left_in[c, pl.ds(0, rows), lanes],
                top_in[c, pl.ds(edge + corner, corner), lanes],
                right_in[c, pl.ds(0, rows), lanes],
            ]
        else:
            start = left_in.shape[1] - rows
            parts = [
                own[pl.ds(edge, main - edge), lanes],
                bot_in[c, pl.ds(0, edge), lanes],
                left_in[c, pl.ds(start, rows), lanes],
                bot_in[c, pl.ds(edge, corner), lanes],
                right_in[c, pl.ds(start, rows), lanes],
                bot_in[c, pl.ds(edge + corner, corner), lanes],
            ]
        return jnp.concatenate(parts, axis=0)

    def put_strip(out, c, start, piece, t):
        bf = jnp.bfloat16
        piece = piece.astype(bf)
        out[c, pl.ds(start, piece.shape[0]), lanes_now[0]] = piece
        if start < edge:
            pole_ref, pole_start = pole_mid_out, start
        else:
            pole_ref, pole_start = pole_corner_out, start - edge
        index = (c, pl.ds(pole_start, piece.shape[0]), lanes_now[0])
        if t == 0:
            pole_ref[index] = piece
        else:
            pole_ref[index] = jnp.where(south, piece, pole_ref[index])

    lanes_now = [None]

    def scatter_grads(d, own, c, t, lanes):
        rows = side - corner
        n_side = left_out.shape[1]
        lanes_now[0] = lanes
        if t == 0:
            put_strip(top_out, c, 0, d[:edge], t)
            own[pl.ds(0, main - edge), lanes] = d[edge:main]
            put_strip(top_out, c, edge, d[main : main + corner], t)
            left_out[c, pl.ds(0, rows), lanes] = d[main + corner : main + side]
            put_strip(top_out, c, edge + corner, d[main + side : main + side + corner], t)
            right_out[c, pl.ds(0, rows), lanes] = d[main + side + corner :]
        else:
            shared = main - 2 * edge
            own[pl.ds(edge, shared), lanes] += d[:shared]
            own[pl.ds(edge + shared, edge), lanes] = d[shared : main - edge]
            put_strip(bot_out, c, 0, d[main - edge : main], t)
            start = n_side - rows
            overlap = rows - start
            left_out[c, pl.ds(start, overlap), lanes] += d[main : main + overlap]
            left_out[c, pl.ds(rows, n_side - rows), lanes] = d[main + overlap : main + rows]
            put_strip(bot_out, c, edge, d[main + rows : main + side], t)
            right_out[c, pl.ds(start, overlap), lanes] += d[main + side : main + side + overlap]
            right_out[c, pl.ds(rows, n_side - rows), lanes] = d[main + side + overlap : main + side + rows]
            put_strip(bot_out, c, edge + corner, d[main + side + rows :], t)

    def body(p, carry):
        lanes = pl.ds(pl.multiple_of(p * LANES, LANES), LANES)
        for t in range(2):
            qp = q_ref[pl.ds(t * tq, tq), lanes]
            gp = g_ref[pl.ds(t * tq, tq), lanes]
            kp = gather_keys(k_own, 0, t, lanes)
            vp = gather_keys(v_own, 1, t, lanes)
            lo = lax.broadcasted_iota(jnp.int32, qp.shape, 1) < HEAD_DIM
            zero = jnp.zeros_like(qp)
            qab = jnp.concatenate([jnp.where(lo, qp, zero), jnp.where(lo, zero, qp)], axis=0)
            gab = jnp.concatenate([jnp.where(lo, gp, zero), jnp.where(lo, zero, gp)], axis=0)
            ds, w = both_heads(qab, gab, kp, vp)
            dq_ab = jnp.dot(ds, kp, preferred_element_type=jnp.float32)
            dq = jnp.where(lo, dq_ab[:tq], dq_ab[tq:]) * scale
            dq_ref[pl.ds(t * tq, tq), lanes] = dq.astype(dq_ref.dtype)
            dk = lax.dot_general(ds, qab, tn, preferred_element_type=jnp.float32) * scale
            dv = lax.dot_general(w, gab, tn, preferred_element_type=jnp.float32)
            scatter_grads(dk, dk_own, 0, t, lanes)
            scatter_grads(dv, dv_own, 1, t, lanes)
        return carry

    lax.fori_loop(0, pairs, body, 0)


def attention_core(q2, g2, k2, v2, above, below, pole_mid, pole_corner, left_in, right_in, width, n_lat):
    cells, features = q2.shape
    r = RADIUS
    tq = TILE_ROWS * width
    tk = 2 * TILE_ROWS * (width + 2 * r)
    tiles = cells // tq
    assert tiles == 2
    flops = 10 * 2 * tq * tk * LANES * (features // LANES) * tiles
    vmem = pl.BlockSpec(memory_space=pltpu.VMEM)
    f32 = jnp.float32
    outs = (
        jax.ShapeDtypeStruct((cells, features), jnp.bfloat16),
        jax.ShapeDtypeStruct((cells, features), f32),
        jax.ShapeDtypeStruct((cells, features), f32),
        jax.ShapeDtypeStruct(above.shape, jnp.bfloat16),
        jax.ShapeDtypeStruct(below.shape, jnp.bfloat16),
        jax.ShapeDtypeStruct(left_in.shape, f32),
        jax.ShapeDtypeStruct(right_in.shape, f32),
        jax.ShapeDtypeStruct(pole_mid.shape, jnp.bfloat16),
        jax.ShapeDtypeStruct(pole_corner.shape, jnp.bfloat16),
    )
    strips = above.size + below.size + pole_mid.size + pole_corner.size
    in_bytes = 2 * (4 * cells * features + strips + left_in.size + right_in.size)
    out_bytes = 10 * cells * features + 2 * strips + 4 * (left_in.size + right_in.size)
    return pl.pallas_call(
        lambda *refs: attention_kernel(width, n_lat, *refs),
        out_shape=outs,
        in_specs=[vmem] * 10,
        out_specs=tuple([vmem] * 9),
        scratch_shapes=[pltpu.VMEM((2 * tq, tk), jnp.float32)],
        cost_estimate=pl.CostEstimate(
            flops=flops,
            transcendentals=2 * tq * tk * HEADS * tiles,
            bytes_accessed=in_bytes + out_bytes,
        ),
        name="neighbourhood_attention_bwd",
    )(q2, g2, k2, v2, above, below, pole_mid, pole_corner, left_in, right_in)


def on_device(queries, keys, values, grad_out, fold_cols):
    height, width, features = queries.shape
    n_lat = lax.axis_size("lat")
    n_lon = lax.axis_size("lon")
    half = n_lon // 2
    i = lax.axis_index("lat")
    j = lax.axis_index("lon")
    at_north = i == 0
    at_south = i == n_lat - 1
    partner_j = (j + half) % n_lon
    r = RADIUS
    f32 = jnp.float32
    bf16 = jnp.bfloat16
    cells = height * width
    edge = r * width
    corner = r * r

    def flat(a, b):
        return a * n_lon + b

    down_pairs = [(flat(a, b), flat(a + 1, b)) for a in range(n_lat - 1) for b in range(n_lon)]
    up_pairs = [(flat(a + 1, b), flat(a, b)) for a in range(n_lat - 1) for b in range(n_lon)]
    pole_pairs = [(flat(a, b), flat(a, (b + half) % n_lon)) for a in (0, n_lat - 1) for b in range(n_lon)]
    right_pairs = [(b, (b + 1) % n_lon) for b in range(n_lon)]
    left_pairs = [(b, (b - 1) % n_lon) for b in range(n_lon)]
    both = ("lat", "lon")

    ext_w = width + 2 * r
    n_cols = n_lon * width
    my_ext_cols = (j * width - r + jnp.arange(ext_w)) % n_cols
    partner_ext_cols = (partner_j * width - r + jnp.arange(ext_w)) % n_cols
    fold_row = jnp.where(at_north, fold_cols[0], fold_cols[1])
    fold_idx = (jnp.take(fold_row, my_ext_cols) - (partner_j * width - r)) % n_cols
    landing = (jnp.take(fold_row, partner_ext_cols) - (j * width - r)) % n_cols
    unfold_idx = jnp.zeros((ext_w,), jnp.int32).at[landing].set(jnp.arange(ext_w, dtype=jnp.int32))

    strip_row = np.concatenate([np.arange(edge) // width, np.arange(corner) // r, np.arange(corner) // r])
    strip_col = np.concatenate(
        [r + np.arange(edge) % width, np.arange(corner) % r, width + r + np.arange(corner) % r]
    )

    def strip_cell(row, col):
        return jnp.where(
            col < r,
            edge + row * r + col,
            jnp.where(col >= width + r, edge + corner + row * r + col - width - r, row * width + col - r),
        )

    pole_src = strip_cell(r - 1 - strip_row, jnp.take(fold_idx, strip_col))
    pole_dst = strip_cell(r - 1 - strip_row, jnp.take(unfold_idx, strip_col))

    def pair(a, b):
        return jnp.stack([a, b])

    kf = keys.reshape(cells, features)
    vf = values.reshape(cells, features)

    def cols(x, a, b):
        return x[:, a:b].reshape(height * (b - a), features)

    from_left = lax.ppermute(pair(cols(keys, width - r, width), cols(values, width - r, width)), "lon", right_pairs)
    from_right = lax.ppermute(pair(cols(keys, 0, r), cols(values, 0, r)), "lon", left_pairs)
    top_mid = pair(kf[:edge], vf[:edge])
    bottom_mid = pair(kf[cells - edge :], vf[cells - edge :])
    partner_src = strip_cell(r - 1 - strip_row, jnp.take(landing, strip_col))
    pole_mid_rows = lax.ppermute(
        jnp.take(jnp.where(at_north, top_mid, bottom_mid), partner_src[:edge], axis=1), both, pole_pairs
    )
    n_side = height * r
    top_send = jnp.concatenate([top_mid, from_left[:, :corner], from_right[:, :corner]], axis=1)
    bottom_send = jnp.concatenate(
        [bottom_mid, from_left[:, n_side - corner :], from_right[:, n_side - corner :]], axis=1
    )
    from_above = lax.ppermute(bottom_send, both, down_pairs)
    from_below = lax.ppermute(top_send, both, up_pairs)
    pole_corner_rows = lax.ppermute(
        jnp.take(jnp.where(at_north, top_send[:, edge:], bottom_send[:, edge:]), partner_src[edge:] - edge, axis=1),
        both,
        pole_pairs,
    )

    q2 = queries.reshape(cells, features)
    g2 = grad_out.reshape(cells, features)
    dq, dk_own, dv_own, top_g, bottom_g, left_g, right_g, pole_g_mid_send, pole_g_corner_send = attention_core(
        q2, g2, kf, vf, from_above, from_below, pole_mid_rows, pole_corner_rows, from_left, from_right, width, n_lat
    )

    up_recv = lax.ppermute(top_g, both, up_pairs)
    down_recv = lax.ppermute(bottom_g, both, down_pairs)
    pole_g_corners = lax.ppermute(pole_g_corner_send, both, pole_pairs)
    unfolded_corners = jnp.take(pole_g_corners, pole_dst[edge:] - edge, axis=1)
    zero_mid = jnp.zeros_like(up_recv[:, :edge])
    add_top = jnp.where(
        at_north, jnp.concatenate([zero_mid, unfolded_corners], axis=1), down_recv
    ).astype(f32)
    add_bottom = jnp.where(
        at_south, jnp.concatenate([zero_mid, unfolded_corners], axis=1), up_recv
    ).astype(f32)

    def side_send(g, first):
        pads_top = [(0, 0), (0, n_side - corner), (0, 0)]
        pads_bottom = [(0, 0), (n_side - corner, 0), (0, 0)]
        return (
            g
            + jnp.pad(add_top[:, first : first + corner], pads_top)
            + jnp.pad(add_bottom[:, first : first + corner], pads_bottom)
        ).astype(bf16)

    back_right = lax.ppermute(side_send(left_g, edge), "lon", left_pairs)
    back_left = lax.ppermute(side_send(right_g, edge + corner), "lon", right_pairs)
    pole_g_mid = lax.ppermute(pole_g_mid_send, both, pole_pairs)
    unfolded_mid = jnp.take(pole_g_mid, pole_dst[:edge], axis=1).astype(f32)
    north_mid = jnp.where(at_north, unfolded_mid, 0.0)
    south_mid = jnp.where(at_south, unfolded_mid, 0.0)

    def final_of(c, own):
        block = own.reshape(height, width, features)
        row_pad = [(0, 0), (0, 0)]
        block = (
            block
            + jnp.pad((add_top[c, :edge] + north_mid[c]).reshape(r, width, features), [(0, height - r)] + row_pad)
            + jnp.pad((add_bottom[c, :edge] + south_mid[c]).reshape(r, width, features), [(height - r, 0)] + row_pad)
            + jnp.pad(
                back_left[c].reshape(height, r, features).astype(f32), [(0, 0), (0, width - r), (0, 0)]
            )
            + jnp.pad(
                back_right[c].reshape(height, r, features).astype(f32), [(0, 0), (width - r, 0), (0, 0)]
            )
        )
        return block.astype(bf16)

    return (dq.reshape(height, width, features), final_of(0, dk_own), final_of(1, dv_own))


def solution(mesh):
    placed = (
        P("lat", "lon", None),
        P("lat", "lon", None),
        P("lat", "lon", None),
        P("lat", "lon", None),
        P(),
    )
    return jax.shard_map(
        on_device,
        mesh=mesh,
        in_specs=placed,
        out_specs=(P("lat", "lon", None), P("lat", "lon", None), P("lat", "lon", None)),
        check_vma=False,
    )
```

```python
import jax
import jax.numpy as jnp
import numpy as np
from jax import lax
from jax.experimental import pallas as pl
from jax.experimental.pallas import tpu as pltpu
from jax.sharding import PartitionSpec as P

HEADS = 16
HEAD_DIM = 64
RADIUS = 4

SPAN = 2 * RADIUS + 1
TILE_ROWS = 8
LANES = 128


def attention_kernel(width, n_lat, *refs):
    (q_ref, g_ref, k_own, v_own, above_in, below_in, pole_mid_in, pole_corner_in, left_in, right_in) = refs[:10]
    (dq_ref, dk_own, dv_own, top_out, bot_out, left_out, right_out, pole_mid_out, pole_corner_out) = refs[10:19]
    bias_ref = refs[19]
    lat = lax.axis_index("lat")
    north = lat == 0
    south = lat == n_lat - 1

    class Strip:
        def __init__(self, neighbour, pole):
            self.neighbour, self.pole = neighbour, pole

        def __getitem__(self, index):
            c, cells, lanes = index
            if cells.start >= edge:
                pole = self.pole_corner_ref[c, pl.ds(cells.start - edge, cells.size), lanes]
            else:
                pole = pole_mid_in[c, cells, lanes]
            return jnp.where(self.pole, pole, self.neighbour[c, cells, lanes])

    top_in = Strip(above_in, north)
    bot_in = Strip(below_in, south)
    top_in.pole_corner_ref = pole_corner_in
    bot_in.pole_corner_ref = pole_corner_in
    scale = HEAD_DIM ** (-0.5)
    r = RADIUS
    tq = TILE_ROWS * width
    main = 2 * TILE_ROWS * width
    side = 2 * TILE_ROWS * r
    tk = main + 2 * side
    edge = r * width
    corner = r * r
    pairs = q_ref.shape[1] // LANES

    qi = lax.broadcasted_iota(jnp.int32, (2 * tq, tk), 0).astype(jnp.float32)
    ki = lax.broadcasted_iota(jnp.int32, (2 * tq, tk), 1).astype(jnp.float32)
    qi = jnp.where(qi >= tq, qi - tq, qi)
    qr = jnp.floor((qi + 0.5) * (1.0 / width))
    qc = qi - width * qr
    in_main = ki < main
    in_left = (ki >= main) & (ki < main + side)
    kk = jnp.where(in_main, ki, jnp.where(in_left, ki - main, ki - main - side))
    per_row = jnp.where(in_main, float(width), float(r))
    kr = jnp.floor((kk + 0.5) / per_row)
    kc = kk - per_row * kr + jnp.where(in_main, float(r), jnp.where(in_left, 0.0, float(width + r)))
    dr = kr - qr
    dc = kc - qc
    ok = (dr >= 0) & (dr <= 2 * r) & (dc >= 0) & (dc <= 2 * r)
    bias_ref[...] = jnp.where(ok, 0.0, -jnp.inf).astype(jnp.float32)

    nt = (((1,), (1,)), ((), ()))
    tn = (((0,), (0,)), ((), ()))

    def both_heads(qab, gab, kp, vp):
        s = lax.dot_general(qab, kp, nt, preferred_element_type=jnp.float32) + bias_ref[...]
        m = jnp.max(s, axis=1, keepdims=True)
        e = jnp.exp(s - m)
        total = jnp.sum(e, axis=1, keepdims=True)
        w = e * (1.0 / total)
        dw = lax.dot_general(gab, vp, nt, preferred_element_type=jnp.float32)
        corr = jnp.sum(w * dw, axis=1, keepdims=True)
        ds = (w * (dw - corr)).astype(jnp.bfloat16)
        return ds, w.astype(jnp.bfloat16)

    def gather_keys(own, c, t, lanes):
        rows = side - corner
        if t == 0:
            parts = [
                top_in[c, pl.ds(0, edge), lanes],
                own[pl.ds(0, main - edge), lanes],
                top_in[c, pl.ds(edge, corner), lanes],
                left_in[c, pl.ds(0, rows), lanes],
                top_in[c, pl.ds(edge + corner, corner), lanes],
                right_in[c, pl.ds(0, rows), lanes],
            ]
        else:
            start = left_in.shape[1] - rows
            parts = [
                own[pl.ds(edge, main - edge), lanes],
                bot_in[c, pl.ds(0, edge), lanes],
                left_in[c, pl.ds(start, rows), lanes],
                bot_in[c, pl.ds(edge, corner), lanes],
                right_in[c, pl.ds(start, rows), lanes],
                bot_in[c, pl.ds(edge + corner, corner), lanes],
            ]
        return jnp.concatenate(parts, axis=0)

    def put_strip(out, c, start, piece, t):
        bf = jnp.bfloat16
        piece = piece.astype(bf)
        out[c, pl.ds(start, piece.shape[0]), lanes_now[0]] = piece
        if start < edge:
            pole_ref, pole_start = pole_mid_out, start
        else:
            pole_ref, pole_start = pole_corner_out, start - edge
        index = (c, pl.ds(pole_start, piece.shape[0]), lanes_now[0])
        if t == 0:
            pole_ref[index] = piece
        else:
            pole_ref[index] = jnp.where(south, piece, pole_ref[index])

    lanes_now = [None]

    def scatter_grads(d, own, c, t, lanes):
        rows = side - corner
        n_side = left_out.shape[1]
        lanes_now[0] = lanes
        if t == 0:
            put_strip(top_out, c, 0, d[:edge], t)
            own[pl.ds(0, main - edge), lanes] = d[edge:main]
            put_strip(top_out, c, edge, d[main : main + corner], t)
            left_out[c, pl.ds(0, rows), lanes] = d[main + corner : main + side]
            put_strip(top_out, c, edge + corner, d[main + side : main + side + corner], t)
            right_out[c, pl.ds(0, rows), lanes] = d[main + side + corner :]
        else:
            shared = main - 2 * edge
            own[pl.ds(edge, shared), lanes] += d[:shared]
            own[pl.ds(edge + shared, edge), lanes] = d[shared : main - edge]
            put_strip(bot_out, c, 0, d[main - edge : main], t)
            start = n_side - rows
            overlap = rows - start
            left_out[c, pl.ds(start, overlap), lanes] += d[main : main + overlap]
            left_out[c, pl.ds(rows, n_side - rows), lanes] = d[main + overlap : main + rows]
            put_strip(bot_out, c, edge, d[main + rows : main + side], t)
            right_out[c, pl.ds(start, overlap), lanes] += d[main + side : main + side + overlap]
            right_out[c, pl.ds(rows, n_side - rows), lanes] = d[main + side + overlap : main + side + rows]
            put_strip(bot_out, c, edge + corner, d[main + side + rows :], t)

    def body(p, carry):
        lanes = pl.ds(pl.multiple_of(p * LANES, LANES), LANES)
        for t in range(2):
            qp = q_ref[pl.ds(t * tq, tq), lanes]
            gp = g_ref[pl.ds(t * tq, tq), lanes]
            kp = gather_keys(k_own, 0, t, lanes)
            vp = gather_keys(v_own, 1, t, lanes)
            lo = lax.broadcasted_iota(jnp.int32, qp.shape, 1) < HEAD_DIM
            zero = jnp.zeros_like(qp)
            qs = qp * jnp.asarray(scale, qp.dtype)
            qab = jnp.concatenate([jnp.where(lo, qs, zero), jnp.where(lo, zero, qs)], axis=0)
            gab = jnp.concatenate([jnp.where(lo, gp, zero), jnp.where(lo, zero, gp)], axis=0)
            ds, w = both_heads(qab, gab, kp, vp)
            dq_ab = jnp.dot(ds, kp, preferred_element_type=jnp.float32)
            dq = jnp.where(lo, dq_ab[:tq], dq_ab[tq:]) * scale
            dq_ref[pl.ds(t * tq, tq), lanes] = dq.astype(dq_ref.dtype)
            dk = lax.dot_general(ds, qab, tn, preferred_element_type=jnp.float32)
            dv = lax.dot_general(w, gab, tn, preferred_element_type=jnp.float32)
            scatter_grads(dk, dk_own, 0, t, lanes)
            scatter_grads(dv, dv_own, 1, t, lanes)
        return carry

    lax.fori_loop(0, pairs, body, 0)


def attention_core(q2, g2, k2, v2, above, below, pole_mid, pole_corner, left_in, right_in, width, n_lat):
    cells, features = q2.shape
    r = RADIUS
    tq = TILE_ROWS * width
    tk = 2 * TILE_ROWS * (width + 2 * r)
    tiles = cells // tq
    assert tiles == 2
    flops = 10 * 2 * tq * tk * LANES * (features // LANES) * tiles
    vmem = pl.BlockSpec(memory_space=pltpu.VMEM)
    f32 = jnp.float32
    outs = (
        jax.ShapeDtypeStruct((cells, features), jnp.bfloat16),
        jax.ShapeDtypeStruct((cells, features), f32),
        jax.ShapeDtypeStruct((cells, features), f32),
        jax.ShapeDtypeStruct(above.shape, jnp.bfloat16),
        jax.ShapeDtypeStruct(below.shape, jnp.bfloat16),
        jax.ShapeDtypeStruct(left_in.shape, f32),
        jax.ShapeDtypeStruct(right_in.shape, f32),
        jax.ShapeDtypeStruct(pole_mid.shape, jnp.bfloat16),
        jax.ShapeDtypeStruct(pole_corner.shape, jnp.bfloat16),
    )
    strips = above.size + below.size + pole_mid.size + pole_corner.size
    in_bytes = 2 * (4 * cells * features + strips + left_in.size + right_in.size)
    out_bytes = 10 * cells * features + 2 * strips + 4 * (left_in.size + right_in.size)
    return pl.pallas_call(
        lambda *refs: attention_kernel(width, n_lat, *refs),
        out_shape=outs,
        in_specs=[vmem] * 10,
        out_specs=tuple([vmem] * 9),
        scratch_shapes=[pltpu.VMEM((2 * tq, tk), jnp.float32)],
        cost_estimate=pl.CostEstimate(
            flops=flops,
            transcendentals=2 * tq * tk * HEADS * tiles,
            bytes_accessed=in_bytes + out_bytes,
        ),
        name="neighbourhood_attention_bwd",
    )(q2, g2, k2, v2, above, below, pole_mid, pole_corner, left_in, right_in)


def on_device(queries, keys, values, grad_out, fold_cols):
    height, width, features = queries.shape
    n_lat = lax.axis_size("lat")
    n_lon = lax.axis_size("lon")
    half = n_lon // 2
    i = lax.axis_index("lat")
    j = lax.axis_index("lon")
    at_north = i == 0
    at_south = i == n_lat - 1
    partner_j = (j + half) % n_lon
    r = RADIUS
    f32 = jnp.float32
    bf16 = jnp.bfloat16
    cells = height * width
    edge = r * width
    corner = r * r

    def flat(a, b):
        return a * n_lon + b

    down_pairs = [(flat(a, b), flat(a + 1, b)) for a in range(n_lat - 1) for b in range(n_lon)]
    up_pairs = [(flat(a + 1, b), flat(a, b)) for a in range(n_lat - 1) for b in range(n_lon)]
    pole_pairs = [(flat(a, b), flat(a, (b + half) % n_lon)) for a in (0, n_lat - 1) for b in range(n_lon)]
    right_pairs = [(b, (b + 1) % n_lon) for b in range(n_lon)]
    left_pairs = [(b, (b - 1) % n_lon) for b in range(n_lon)]
    both = ("lat", "lon")

    ext_w = width + 2 * r
    n_cols = n_lon * width
    my_ext_cols = (j * width - r + jnp.arange(ext_w)) % n_cols
    partner_ext_cols = (partner_j * width - r + jnp.arange(ext_w)) % n_cols
    fold_row = jnp.where(at_north, fold_cols[0], fold_cols[1])
    fold_idx = (jnp.take(fold_row, my_ext_cols) - (partner_j * width - r)) % n_cols
    landing = (jnp.take(fold_row, partner_ext_cols) - (j * width - r)) % n_cols
    unfold_idx = jnp.zeros((ext_w,), jnp.int32).at[landing].set(jnp.arange(ext_w, dtype=jnp.int32))

    strip_row = np.concatenate([np.arange(edge) // width, np.arange(corner) // r, np.arange(corner) // r])
    strip_col = np.concatenate(
        [r + np.arange(edge) % width, np.arange(corner) % r, width + r + np.arange(corner) % r]
    )

    def strip_cell(row, col):
        return jnp.where(
            col < r,
            edge + row * r + col,
            jnp.where(col >= width + r, edge + corner + row * r + col - width - r, row * width + col - r),
        )

    pole_src = strip_cell(r - 1 - strip_row, jnp.take(fold_idx, strip_col))
    pole_dst = strip_cell(r - 1 - strip_row, jnp.take(unfold_idx, strip_col))

    def pair(a, b):
        return jnp.stack([a, b])

    kf = keys.reshape(cells, features)
    vf = values.reshape(cells, features)

    def cols(x, a, b):
        return x[:, a:b].reshape(height * (b - a), features)

    from_left = lax.ppermute(pair(cols(keys, width - r, width), cols(values, width - r, width)), "lon", right_pairs)
    from_right = lax.ppermute(pair(cols(keys, 0, r), cols(values, 0, r)), "lon", left_pairs)
    top_mid = pair(kf[:edge], vf[:edge])
    bottom_mid = pair(kf[cells - edge :], vf[cells - edge :])
    pole_mid = lax.ppermute(jnp.where(at_north, top_mid, bottom_mid), both, pole_pairs)
    n_side = height * r
    top_send = jnp.concatenate([top_mid, from_left[:, :corner], from_right[:, :corner]], axis=1)
    bottom_send = jnp.concatenate(
        [bottom_mid, from_left[:, n_side - corner :], from_right[:, n_side - corner :]], axis=1
    )
    from_above = lax.ppermute(bottom_send, both, down_pairs)
    from_below = lax.ppermute(top_send, both, up_pairs)
    pole_corners = lax.ppermute(
        jnp.where(at_north, top_send[:, edge:], bottom_send[:, edge:]), both, pole_pairs
    )
    pole_mid_rows = jnp.take(pole_mid, pole_src[:edge], axis=1)
    pole_corner_rows = jnp.take(pole_corners, pole_src[edge:] - edge, axis=1)

    q2 = queries.reshape(cells, features)
    g2 = grad_out.reshape(cells, features)
    dq, dk_own, dv_own, top_g, bottom_g, left_g, right_g, pole_g_mid_send, pole_g_corner_send = attention_core(
        q2, g2, kf, vf, from_above, from_below, pole_mid_rows, pole_corner_rows, from_left, from_right, width, n_lat
    )

    up_recv = lax.ppermute(top_g, both, up_pairs)
    down_recv = lax.ppermute(bottom_g, both, down_pairs)
    pole_g_corners = lax.ppermute(pole_g_corner_send, both, pole_pairs)
    unfolded_corners = jnp.take(pole_g_corners, pole_dst[edge:] - edge, axis=1)
    zero_mid = jnp.zeros_like(up_recv[:, :edge])
    add_top = jnp.where(
        at_north, jnp.concatenate([zero_mid, unfolded_corners], axis=1), down_recv
    ).astype(f32)
    add_bottom = jnp.where(
        at_south, jnp.concatenate([zero_mid, unfolded_corners], axis=1), up_recv
    ).astype(f32)

    def side_send(g, first):
        pads_top = [(0, 0), (0, n_side - corner), (0, 0)]
        pads_bottom = [(0, 0), (n_side - corner, 0), (0, 0)]
        return (
            g
            + jnp.pad(add_top[:, first : first + corner], pads_top)
            + jnp.pad(add_bottom[:, first : first + corner], pads_bottom)
        ).astype(bf16)

    back_right = lax.ppermute(side_send(left_g, edge), "lon", left_pairs)
    back_left = lax.ppermute(side_send(right_g, edge + corner), "lon", right_pairs)
    pole_g_mid = lax.ppermute(pole_g_mid_send, both, pole_pairs)
    unfolded_mid = jnp.take(pole_g_mid, pole_dst[:edge], axis=1).astype(f32)
    north_mid = jnp.where(at_north, unfolded_mid, 0.0)
    south_mid = jnp.where(at_south, unfolded_mid, 0.0)

    def final_of(c, own):
        block = own.reshape(height, width, features)
        row_pad = [(0, 0), (0, 0)]
        block = (
            block
            + jnp.pad((add_top[c, :edge] + north_mid[c]).reshape(r, width, features), [(0, height - r)] + row_pad)
            + jnp.pad((add_bottom[c, :edge] + south_mid[c]).reshape(r, width, features), [(height - r, 0)] + row_pad)
            + jnp.pad(
                back_left[c].reshape(height, r, features).astype(f32), [(0, 0), (0, width - r), (0, 0)]
            )
            + jnp.pad(
                back_right[c].reshape(height, r, features).astype(f32), [(0, 0), (width - r, 0), (0, 0)]
            )
        )
        return block.astype(bf16)

    return (dq.reshape(height, width, features), final_of(0, dk_own), final_of(1, dv_own))


def solution(mesh):
    placed = (
        P("lat", "lon", None),
        P("lat", "lon", None),
        P("lat", "lon", None),
        P("lat", "lon", None),
        P(),
    )
    return jax.shard_map(
        on_device,
        mesh=mesh,
        in_specs=placed,
        out_specs=(P("lat", "lon", None), P("lat", "lon", None), P("lat", "lon", None)),
        check_vma=False,
    )
```

```python
import jax
import jax.numpy as jnp
import numpy as np
from jax import lax
from jax.experimental import pallas as pl
from jax.experimental.pallas import tpu as pltpu
from jax.sharding import PartitionSpec as P

HEADS = 16
HEAD_DIM = 64
RADIUS = 4

SPAN = 2 * RADIUS + 1
TILE_ROWS = 8
LANES = 128


def attention_kernel(width, n_lat, *refs):
    (q_ref, g_ref, k_own, v_own, above_in, below_in, pole_mid_in, pole_corner_in, left_in, right_in) = refs[:10]
    (mid_pick, corner_pick) = refs[10:12]
    (dq_ref, dk_own, dv_own, top_out, bot_out, left_out, right_out, pole_mid_out, pole_corner_out) = refs[12:21]
    bias_ref = refs[21]
    lat = lax.axis_index("lat")
    north = lat == 0
    south = lat == n_lat - 1

    class Strip:
        def __init__(self, neighbour, pole):
            self.neighbour, self.pole = neighbour, pole

        def __getitem__(self, index):
            c, cells, lanes = index
            mid, corners = pole_now[0]
            if cells.start >= edge:
                pole = corners[c][cells.start - edge : cells.start - edge + cells.size]
            else:
                pole = mid[c][cells.start : cells.start + cells.size]
            return jnp.where(self.pole, pole, self.neighbour[c, cells, lanes])

    top_in = Strip(above_in, north)
    bot_in = Strip(below_in, south)
    top_in.pole_corner_ref = pole_corner_in
    bot_in.pole_corner_ref = pole_corner_in
    scale = HEAD_DIM ** (-0.5)
    r = RADIUS
    tq = TILE_ROWS * width
    main = 2 * TILE_ROWS * width
    side = 2 * TILE_ROWS * r
    tk = main + 2 * side
    edge = r * width
    corner = r * r
    pairs = q_ref.shape[1] // LANES

    qi = lax.broadcasted_iota(jnp.int32, (2 * tq, tk), 0).astype(jnp.float32)
    ki = lax.broadcasted_iota(jnp.int32, (2 * tq, tk), 1).astype(jnp.float32)
    qi = jnp.where(qi >= tq, qi - tq, qi)
    qr = jnp.floor((qi + 0.5) * (1.0 / width))
    qc = qi - width * qr
    in_main = ki < main
    in_left = (ki >= main) & (ki < main + side)
    kk = jnp.where(in_main, ki, jnp.where(in_left, ki - main, ki - main - side))
    per_row = jnp.where(in_main, float(width), float(r))
    kr = jnp.floor((kk + 0.5) / per_row)
    kc = kk - per_row * kr + jnp.where(in_main, float(r), jnp.where(in_left, 0.0, float(width + r)))
    dr = kr - qr
    dc = kc - qc
    ok = (dr >= 0) & (dr <= 2 * r) & (dc >= 0) & (dc <= 2 * r)
    bias_ref[...] = jnp.where(ok, 0.0, -jnp.inf).astype(jnp.float32)

    nt = (((1,), (1,)), ((), ()))
    tn = (((0,), (0,)), ((), ()))

    def both_heads(qab, gab, kp, vp):
        s = lax.dot_general(qab, kp, nt, preferred_element_type=jnp.float32) + bias_ref[...]
        m = jnp.max(s, axis=1, keepdims=True)
        e = jnp.exp(s - m)
        total = jnp.sum(e, axis=1, keepdims=True)
        w = e * (1.0 / total)
        dw = lax.dot_general(gab, vp, nt, preferred_element_type=jnp.float32)
        corr = jnp.sum(w * dw, axis=1, keepdims=True)
        ds = (w * (dw - corr)).astype(jnp.bfloat16)
        return ds, w.astype(jnp.bfloat16)

    def gather_keys(own, c, t, lanes):
        rows = side - corner
        if t == 0:
            parts = [
                top_in[c, pl.ds(0, edge), lanes],
                own[pl.ds(0, main - edge), lanes],
                top_in[c, pl.ds(edge, corner), lanes],
                left_in[c, pl.ds(0, rows), lanes],
                top_in[c, pl.ds(edge + corner, corner), lanes],
                right_in[c, pl.ds(0, rows), lanes],
            ]
        else:
            start = left_in.shape[1] - rows
            parts = [
                own[pl.ds(edge, main - edge), lanes],
                bot_in[c, pl.ds(0, edge), lanes],
                left_in[c, pl.ds(start, rows), lanes],
                bot_in[c, pl.ds(edge, corner), lanes],
                right_in[c, pl.ds(start, rows), lanes],
                bot_in[c, pl.ds(edge + corner, corner), lanes],
            ]
        return jnp.concatenate(parts, axis=0)

    def put_strip(out, c, start, piece, t):
        bf = jnp.bfloat16
        piece = piece.astype(bf)
        out[c, pl.ds(start, piece.shape[0]), lanes_now[0]] = piece
        if start < edge:
            pole_ref, pole_start = pole_mid_out, start
        else:
            pole_ref, pole_start = pole_corner_out, start - edge
        index = (c, pl.ds(pole_start, piece.shape[0]), lanes_now[0])
        if t == 0:
            pole_ref[index] = piece
        else:
            pole_ref[index] = jnp.where(south, piece, pole_ref[index])

    lanes_now = [None]
    pole_now = [None]

    def fold(pick, ref, c, lanes):
        return jnp.dot(pick[...], ref[c, :, lanes], preferred_element_type=jnp.float32).astype(jnp.bfloat16)

    def scatter_grads(d, own, c, t, lanes):
        rows = side - corner
        n_side = left_out.shape[1]
        lanes_now[0] = lanes
        if t == 0:
            put_strip(top_out, c, 0, d[:edge], t)
            own[pl.ds(0, main - edge), lanes] = d[edge:main]
            put_strip(top_out, c, edge, d[main : main + corner], t)
            left_out[c, pl.ds(0, rows), lanes] = d[main + corner : main + side]
            put_strip(top_out, c, edge + corner, d[main + side : main + side + corner], t)
            right_out[c, pl.ds(0, rows), lanes] = d[main + side + corner :]
        else:
            shared = main - 2 * edge
            own[pl.ds(edge, shared), lanes] += d[:shared]
            own[pl.ds(edge + shared, edge), lanes] = d[shared : main - edge]
            put_strip(bot_out, c, 0, d[main - edge : main], t)
            start = n_side - rows
            overlap = rows - start
            left_out[c, pl.ds(start, overlap), lanes] += d[main : main + overlap]
            left_out[c, pl.ds(rows, n_side - rows), lanes] = d[main + overlap : main + rows]
            put_strip(bot_out, c, edge, d[main + rows : main + side], t)
            right_out[c, pl.ds(start, overlap), lanes] += d[main + side : main + side + overlap]
            right_out[c, pl.ds(rows, n_side - rows), lanes] = d[main + side + overlap : main + side + rows]
            put_strip(bot_out, c, edge + corner, d[main + side + rows :], t)

    def body(p, carry):
        lanes = pl.ds(pl.multiple_of(p * LANES, LANES), LANES)
        pole_now[0] = (
            [fold(mid_pick, pole_mid_in, c, lanes) for c in range(2)],
            [fold(corner_pick, pole_corner_in, c, lanes) for c in range(2)],
        )
        for t in range(2):
            qp = q_ref[pl.ds(t * tq, tq), lanes]
            gp = g_ref[pl.ds(t * tq, tq), lanes]
            kp = gather_keys(k_own, 0, t, lanes)
            vp = gather_keys(v_own, 1, t, lanes)
            lo = lax.broadcasted_iota(jnp.int32, qp.shape, 1) < HEAD_DIM
            zero = jnp.zeros_like(qp)
            qs = qp * jnp.asarray(scale, qp.dtype)
            qab = jnp.concatenate([jnp.where(lo, qs, zero), jnp.where(lo, zero, qs)], axis=0)
            gab = jnp.concatenate([jnp.where(lo, gp, zero), jnp.where(lo, zero, gp)], axis=0)
            ds, w = both_heads(qab, gab, kp, vp)
            dq_ab = jnp.dot(ds, kp, preferred_element_type=jnp.float32)
            dq = jnp.where(lo, dq_ab[:tq], dq_ab[tq:]) * scale
            dq_ref[pl.ds(t * tq, tq), lanes] = dq.astype(dq_ref.dtype)
            dk = lax.dot_general(ds, qab, tn, preferred_element_type=jnp.float32)
            dv = lax.dot_general(w, gab, tn, preferred_element_type=jnp.float32)
            scatter_grads(dk, dk_own, 0, t, lanes)
            scatter_grads(dv, dv_own, 1, t, lanes)
        return carry

    lax.fori_loop(0, pairs, body, 0)


def attention_core(q2, g2, k2, v2, above, below, pole_mid, pole_corner, left_in, right_in, picks, width, n_lat):
    cells, features = q2.shape
    r = RADIUS
    tq = TILE_ROWS * width
    tk = 2 * TILE_ROWS * (width + 2 * r)
    tiles = cells // tq
    assert tiles == 2
    flops = 10 * 2 * tq * tk * LANES * (features // LANES) * tiles
    vmem = pl.BlockSpec(memory_space=pltpu.VMEM)
    f32 = jnp.float32
    outs = (
        jax.ShapeDtypeStruct((cells, features), jnp.bfloat16),
        jax.ShapeDtypeStruct((cells, features), f32),
        jax.ShapeDtypeStruct((cells, features), f32),
        jax.ShapeDtypeStruct(above.shape, jnp.bfloat16),
        jax.ShapeDtypeStruct(below.shape, jnp.bfloat16),
        jax.ShapeDtypeStruct(left_in.shape, f32),
        jax.ShapeDtypeStruct(right_in.shape, f32),
        jax.ShapeDtypeStruct(pole_mid.shape, jnp.bfloat16),
        jax.ShapeDtypeStruct(pole_corner.shape, jnp.bfloat16),
    )
    strips = above.size + below.size + pole_mid.size + pole_corner.size
    in_bytes = 2 * (4 * cells * features + strips + left_in.size + right_in.size)
    out_bytes = 10 * cells * features + 2 * strips + 4 * (left_in.size + right_in.size)
    return pl.pallas_call(
        lambda *refs: attention_kernel(width, n_lat, *refs),
        out_shape=outs,
        in_specs=[vmem] * 12,
        out_specs=tuple([vmem] * 9),
        scratch_shapes=[pltpu.VMEM((2 * tq, tk), jnp.float32)],
        cost_estimate=pl.CostEstimate(
            flops=flops,
            transcendentals=2 * tq * tk * HEADS * tiles,
            bytes_accessed=in_bytes + out_bytes,
        ),
        name="neighbourhood_attention_bwd",
    )(q2, g2, k2, v2, above, below, pole_mid, pole_corner, left_in, right_in, *picks)


def on_device(queries, keys, values, grad_out, fold_cols):
    height, width, features = queries.shape
    n_lat = lax.axis_size("lat")
    n_lon = lax.axis_size("lon")
    half = n_lon // 2
    i = lax.axis_index("lat")
    j = lax.axis_index("lon")
    at_north = i == 0
    at_south = i == n_lat - 1
    partner_j = (j + half) % n_lon
    r = RADIUS
    f32 = jnp.float32
    bf16 = jnp.bfloat16
    cells = height * width
    edge = r * width
    corner = r * r

    def flat(a, b):
        return a * n_lon + b

    down_pairs = [(flat(a, b), flat(a + 1, b)) for a in range(n_lat - 1) for b in range(n_lon)]
    up_pairs = [(flat(a + 1, b), flat(a, b)) for a in range(n_lat - 1) for b in range(n_lon)]
    pole_pairs = [(flat(a, b), flat(a, (b + half) % n_lon)) for a in (0, n_lat - 1) for b in range(n_lon)]
    right_pairs = [(b, (b + 1) % n_lon) for b in range(n_lon)]
    left_pairs = [(b, (b - 1) % n_lon) for b in range(n_lon)]
    both = ("lat", "lon")

    ext_w = width + 2 * r
    n_cols = n_lon * width
    my_ext_cols = (j * width - r + jnp.arange(ext_w)) % n_cols
    partner_ext_cols = (partner_j * width - r + jnp.arange(ext_w)) % n_cols
    fold_row = jnp.where(at_north, fold_cols[0], fold_cols[1])
    fold_idx = (jnp.take(fold_row, my_ext_cols) - (partner_j * width - r)) % n_cols
    landing = (jnp.take(fold_row, partner_ext_cols) - (j * width - r)) % n_cols
    unfold_idx = jnp.zeros((ext_w,), jnp.int32).at[landing].set(jnp.arange(ext_w, dtype=jnp.int32))

    strip_row = np.concatenate([np.arange(edge) // width, np.arange(corner) // r, np.arange(corner) // r])
    strip_col = np.concatenate(
        [r + np.arange(edge) % width, np.arange(corner) % r, width + r + np.arange(corner) % r]
    )

    def strip_cell(row, col):
        return jnp.where(
            col < r,
            edge + row * r + col,
            jnp.where(col >= width + r, edge + corner + row * r + col - width - r, row * width + col - r),
        )

    pole_src = strip_cell(r - 1 - strip_row, jnp.take(fold_idx, strip_col))
    pole_dst = strip_cell(r - 1 - strip_row, jnp.take(unfold_idx, strip_col))

    def pair(a, b):
        return jnp.stack([a, b])

    kf = keys.reshape(cells, features)
    vf = values.reshape(cells, features)

    def cols(x, a, b):
        return x[:, a:b].reshape(height * (b - a), features)

    from_left = lax.ppermute(pair(cols(keys, width - r, width), cols(values, width - r, width)), "lon", right_pairs)
    from_right = lax.ppermute(pair(cols(keys, 0, r), cols(values, 0, r)), "lon", left_pairs)
    top_mid = pair(kf[:edge], vf[:edge])
    bottom_mid = pair(kf[cells - edge :], vf[cells - edge :])
    pole_mid = lax.ppermute(jnp.where(at_north, top_mid, bottom_mid), both, pole_pairs)
    n_side = height * r
    top_send = jnp.concatenate([top_mid, from_left[:, :corner], from_right[:, :corner]], axis=1)
    bottom_send = jnp.concatenate(
        [bottom_mid, from_left[:, n_side - corner :], from_right[:, n_side - corner :]], axis=1
    )
    from_above = lax.ppermute(bottom_send, both, down_pairs)
    from_below = lax.ppermute(top_send, both, up_pairs)
    pole_corners = lax.ppermute(
        jnp.where(at_north, top_send[:, edge:], bottom_send[:, edge:]), both, pole_pairs
    )
    mid_pick = (pole_src[:edge, None] == jnp.arange(edge)[None, :]).astype(bf16)
    corner_pick = (pole_src[edge:, None] - edge == jnp.arange(2 * corner)[None, :]).astype(bf16)

    q2 = queries.reshape(cells, features)
    g2 = grad_out.reshape(cells, features)
    dq, dk_own, dv_own, top_g, bottom_g, left_g, right_g, pole_g_mid_send, pole_g_corner_send = attention_core(
        q2, g2, kf, vf, from_above, from_below, pole_mid, pole_corners, from_left, from_right, (mid_pick, corner_pick), width, n_lat
    )

    up_recv = lax.ppermute(top_g, both, up_pairs)
    down_recv = lax.ppermute(bottom_g, both, down_pairs)
    pole_g_corners = lax.ppermute(pole_g_corner_send, both, pole_pairs)
    unfolded_corners = jnp.take(pole_g_corners, pole_dst[edge:] - edge, axis=1)
    zero_mid = jnp.zeros_like(up_recv[:, :edge])
    add_top = jnp.where(
        at_north, jnp.concatenate([zero_mid, unfolded_corners], axis=1), down_recv
    ).astype(f32)
    add_bottom = jnp.where(
        at_south, jnp.concatenate([zero_mid, unfolded_corners], axis=1), up_recv
    ).astype(f32)

    def side_send(g, first):
        pads_top = [(0, 0), (0, n_side - corner), (0, 0)]
        pads_bottom = [(0, 0), (n_side - corner, 0), (0, 0)]
        return (
            g
            + jnp.pad(add_top[:, first : first + corner], pads_top)
            + jnp.pad(add_bottom[:, first : first + corner], pads_bottom)
        ).astype(bf16)

    back_right = lax.ppermute(side_send(left_g, edge), "lon", left_pairs)
    back_left = lax.ppermute(side_send(right_g, edge + corner), "lon", right_pairs)
    pole_g_mid = lax.ppermute(pole_g_mid_send, both, pole_pairs)
    unfolded_mid = jnp.take(pole_g_mid, pole_dst[:edge], axis=1).astype(f32)
    north_mid = jnp.where(at_north, unfolded_mid, 0.0)
    south_mid = jnp.where(at_south, unfolded_mid, 0.0)

    def final_of(c, own):
        block = own.reshape(height, width, features)
        row_pad = [(0, 0), (0, 0)]
        block = (
            block
            + jnp.pad((add_top[c, :edge] + north_mid[c]).reshape(r, width, features), [(0, height - r)] + row_pad)
            + jnp.pad((add_bottom[c, :edge] + south_mid[c]).reshape(r, width, features), [(height - r, 0)] + row_pad)
            + jnp.pad(
                back_left[c].reshape(height, r, features).astype(f32), [(0, 0), (0, width - r), (0, 0)]
            )
            + jnp.pad(
                back_right[c].reshape(height, r, features).astype(f32), [(0, 0), (width - r, 0), (0, 0)]
            )
        )
        return block.astype(bf16)

    return (dq.reshape(height, width, features), final_of(0, dk_own), final_of(1, dv_own))


def solution(mesh):
    placed = (
        P("lat", "lon", None),
        P("lat", "lon", None),
        P("lat", "lon", None),
        P("lat", "lon", None),
        P(),
    )
    return jax.shard_map(
        on_device,
        mesh=mesh,
        in_specs=placed,
        out_specs=(P("lat", "lon", None), P("lat", "lon", None), P("lat", "lon", None)),
        check_vma=False,
    )
```

```python
import jax
import jax.numpy as jnp
import numpy as np
from jax import lax
from jax.experimental import pallas as pl
from jax.experimental.pallas import tpu as pltpu
from jax.sharding import PartitionSpec as P

HEADS = 16
HEAD_DIM = 64
RADIUS = 4

SPAN = 2 * RADIUS + 1
TILE_ROWS = 8
LANES = 128


def attention_kernel(width, n_lat, *refs):
    (q_ref, g_ref, k_own, v_own, above_in, below_in, pole_mid_in, pole_corner_in, left_in, right_in) = refs[:10]
    (dq_ref, dk_own, dv_own, top_out, bot_out, left_out, right_out, pole_mid_out, pole_corner_out) = refs[10:19]
    bias_ref = refs[19]
    lat = lax.axis_index("lat")
    north = lat == 0
    south = lat == n_lat - 1

    class Strip:
        def __init__(self, neighbour, pole):
            self.neighbour, self.pole = neighbour, pole

        def __getitem__(self, index):
            c, cells, lanes = index
            if cells.start >= edge:
                pole = self.pole_corner_ref[c, pl.ds(cells.start - edge, cells.size), lanes]
            else:
                pole = pole_mid_in[c, cells, lanes]
            return jnp.where(self.pole, pole, self.neighbour[c, cells, lanes])

    top_in = Strip(above_in, north)
    bot_in = Strip(below_in, south)
    top_in.pole_corner_ref = pole_corner_in
    bot_in.pole_corner_ref = pole_corner_in
    scale = HEAD_DIM ** (-0.5)
    r = RADIUS
    tq = TILE_ROWS * width
    main = 2 * TILE_ROWS * width
    side = 2 * TILE_ROWS * r
    tk = main + 2 * side
    edge = r * width
    corner = r * r
    pairs = q_ref.shape[1] // LANES

    qi = lax.broadcasted_iota(jnp.int32, (2 * tq, tk), 0).astype(jnp.float32)
    ki = lax.broadcasted_iota(jnp.int32, (2 * tq, tk), 1).astype(jnp.float32)
    qi = jnp.where(qi >= tq, qi - tq, qi)
    qr = jnp.floor((qi + 0.5) * (1.0 / width))
    qc = qi - width * qr
    in_main = ki < main
    in_left = (ki >= main) & (ki < main + side)
    kk = jnp.where(in_main, ki, jnp.where(in_left, ki - main, ki - main - side))
    per_row = jnp.where(in_main, float(width), float(r))
    kr = jnp.floor((kk + 0.5) / per_row)
    kc = kk - per_row * kr + jnp.where(in_main, float(r), jnp.where(in_left, 0.0, float(width + r)))
    dr = kr - qr
    dc = kc - qc
    ok = (dr >= 0) & (dr <= 2 * r) & (dc >= 0) & (dc <= 2 * r)
    bias_ref[...] = jnp.where(ok, 0.0, -jnp.inf).astype(jnp.float32)

    nt = (((1,), (1,)), ((), ()))
    tn = (((0,), (0,)), ((), ()))

    def both_heads(qab, gab, kp, vp):
        s = lax.dot_general(qab, kp, nt, preferred_element_type=jnp.float32) + bias_ref[...]
        m = jnp.max(s, axis=1, keepdims=True)
        e = jnp.exp(s - m)
        total = jnp.sum(e, axis=1, keepdims=True)
        w = e * (1.0 / total)
        dw = lax.dot_general(gab, vp, nt, preferred_element_type=jnp.float32)
        corr = jnp.sum(w * dw, axis=1, keepdims=True)
        ds = (w * (dw - corr)).astype(jnp.bfloat16)
        return ds, w.astype(jnp.bfloat16)

    def gather_keys(own, c, t, lanes):
        rows = side - corner
        if t == 0:
            parts = [
                top_in[c, pl.ds(0, edge), lanes],
                own[pl.ds(0, main - edge), lanes],
                top_in[c, pl.ds(edge, corner), lanes],
                left_in[c, pl.ds(0, rows), lanes],
                top_in[c, pl.ds(edge + corner, corner), lanes],
                right_in[c, pl.ds(0, rows), lanes],
            ]
        else:
            start = left_in.shape[1] - rows
            parts = [
                own[pl.ds(edge, main - edge), lanes],
                bot_in[c, pl.ds(0, edge), lanes],
                left_in[c, pl.ds(start, rows), lanes],
                bot_in[c, pl.ds(edge, corner), lanes],
                right_in[c, pl.ds(start, rows), lanes],
                bot_in[c, pl.ds(edge + corner, corner), lanes],
            ]
        return jnp.concatenate(parts, axis=0)

    def put_strip(out, c, start, piece, t):
        bf = jnp.bfloat16
        piece = piece.astype(bf)
        out[c, pl.ds(start, piece.shape[0]), lanes_now[0]] = piece
        if start < edge:
            pole_ref, pole_start = pole_mid_out, start
        else:
            pole_ref, pole_start = pole_corner_out, start - edge
        index = (c, pl.ds(pole_start, piece.shape[0]), lanes_now[0])
        if t == 0:
            pole_ref[index] = piece
        else:
            pole_ref[index] = jnp.where(south, piece, pole_ref[index])

    lanes_now = [None]

    def scatter_grads(d, own, c, t, lanes):
        rows = side - corner
        n_side = left_out.shape[1]
        lanes_now[0] = lanes
        if t == 0:
            put_strip(top_out, c, 0, d[:edge], t)
            own[pl.ds(0, main - edge), lanes] = d[edge:main]
            put_strip(top_out, c, edge, d[main : main + corner], t)
            left_out[c, pl.ds(0, rows), lanes] = d[main + corner : main + side]
            put_strip(top_out, c, edge + corner, d[main + side : main + side + corner], t)
            right_out[c, pl.ds(0, rows), lanes] = d[main + side + corner :]
        else:
            shared = main - 2 * edge
            own[pl.ds(edge, shared), lanes] += d[:shared]
            own[pl.ds(edge + shared, edge), lanes] = d[shared : main - edge]
            put_strip(bot_out, c, 0, d[main - edge : main], t)
            start = n_side - rows
            overlap = rows - start
            left_out[c, pl.ds(start, overlap), lanes] += d[main : main + overlap]
            left_out[c, pl.ds(rows, n_side - rows), lanes] = d[main + overlap : main + rows]
            put_strip(bot_out, c, edge, d[main + rows : main + side], t)
            right_out[c, pl.ds(start, overlap), lanes] += d[main + side : main + side + overlap]
            right_out[c, pl.ds(rows, n_side - rows), lanes] = d[main + side + overlap : main + side + rows]
            put_strip(bot_out, c, edge + corner, d[main + side + rows :], t)

    def body(p, carry):
        lanes = pl.ds(pl.multiple_of(p * LANES, LANES), LANES)
        for t in range(2):
            qp = q_ref[pl.ds(t * tq, tq), lanes]
            gp = g_ref[pl.ds(t * tq, tq), lanes]
            kp = gather_keys(k_own, 0, t, lanes)
            vp = gather_keys(v_own, 1, t, lanes)
            lo = lax.broadcasted_iota(jnp.int32, qp.shape, 1) < HEAD_DIM
            zero = jnp.zeros_like(qp)
            qs = qp * jnp.asarray(scale, qp.dtype)
            qab = jnp.concatenate([jnp.where(lo, qs, zero), jnp.where(lo, zero, qs)], axis=0)
            gab = jnp.concatenate([jnp.where(lo, gp, zero), jnp.where(lo, zero, gp)], axis=0)
            ds, w = both_heads(qab, gab, kp, vp)
            dq_ab = jnp.dot(ds, kp, preferred_element_type=jnp.float32)
            dq = jnp.where(lo, dq_ab[:tq], dq_ab[tq:]) * scale
            dq_ref[pl.ds(t * tq, tq), lanes] = dq.astype(dq_ref.dtype)
            dk = lax.dot_general(ds, qab, tn, preferred_element_type=jnp.float32)
            dv = lax.dot_general(w, gab, tn, preferred_element_type=jnp.float32)
            scatter_grads(dk, dk_own, 0, t, lanes)
            scatter_grads(dv, dv_own, 1, t, lanes)
        return carry

    lax.fori_loop(0, pairs, body, 0, unroll=2)


def attention_core(q2, g2, k2, v2, above, below, pole_mid, pole_corner, left_in, right_in, width, n_lat):
    cells, features = q2.shape
    r = RADIUS
    tq = TILE_ROWS * width
    tk = 2 * TILE_ROWS * (width + 2 * r)
    tiles = cells // tq
    assert tiles == 2
    flops = 10 * 2 * tq * tk * LANES * (features // LANES) * tiles
    vmem = pl.BlockSpec(memory_space=pltpu.VMEM)
    f32 = jnp.float32
    outs = (
        jax.ShapeDtypeStruct((cells, features), jnp.bfloat16),
        jax.ShapeDtypeStruct((cells, features), f32),
        jax.ShapeDtypeStruct((cells, features), f32),
        jax.ShapeDtypeStruct(above.shape, jnp.bfloat16),
        jax.ShapeDtypeStruct(below.shape, jnp.bfloat16),
        jax.ShapeDtypeStruct(left_in.shape, f32),
        jax.ShapeDtypeStruct(right_in.shape, f32),
        jax.ShapeDtypeStruct(pole_mid.shape, jnp.bfloat16),
        jax.ShapeDtypeStruct(pole_corner.shape, jnp.bfloat16),
    )
    strips = above.size + below.size + pole_mid.size + pole_corner.size
    in_bytes = 2 * (4 * cells * features + strips + left_in.size + right_in.size)
    out_bytes = 10 * cells * features + 2 * strips + 4 * (left_in.size + right_in.size)
    return pl.pallas_call(
        lambda *refs: attention_kernel(width, n_lat, *refs),
        out_shape=outs,
        in_specs=[vmem] * 10,
        out_specs=tuple([vmem] * 9),
        scratch_shapes=[pltpu.VMEM((2 * tq, tk), jnp.float32)],
        cost_estimate=pl.CostEstimate(
            flops=flops,
            transcendentals=2 * tq * tk * HEADS * tiles,
            bytes_accessed=in_bytes + out_bytes,
        ),
        name="neighbourhood_attention_bwd",
    )(q2, g2, k2, v2, above, below, pole_mid, pole_corner, left_in, right_in)


def on_device(queries, keys, values, grad_out, fold_cols):
    height, width, features = queries.shape
    n_lat = lax.axis_size("lat")
    n_lon = lax.axis_size("lon")
    half = n_lon // 2
    i = lax.axis_index("lat")
    j = lax.axis_index("lon")
    at_north = i == 0
    at_south = i == n_lat - 1
    partner_j = (j + half) % n_lon
    r = RADIUS
    f32 = jnp.float32
    bf16 = jnp.bfloat16
    cells = height * width
    edge = r * width
    corner = r * r

    def flat(a, b):
        return a * n_lon + b

    down_pairs = [(flat(a, b), flat(a + 1, b)) for a in range(n_lat - 1) for b in range(n_lon)]
    up_pairs = [(flat(a + 1, b), flat(a, b)) for a in range(n_lat - 1) for b in range(n_lon)]
    pole_pairs = [(flat(a, b), flat(a, (b + half) % n_lon)) for a in (0, n_lat - 1) for b in range(n_lon)]
    right_pairs = [(b, (b + 1) % n_lon) for b in range(n_lon)]
    left_pairs = [(b, (b - 1) % n_lon) for b in range(n_lon)]
    both = ("lat", "lon")

    ext_w = width + 2 * r
    n_cols = n_lon * width
    my_ext_cols = (j * width - r + jnp.arange(ext_w)) % n_cols
    partner_ext_cols = (partner_j * width - r + jnp.arange(ext_w)) % n_cols
    fold_row = jnp.where(at_north, fold_cols[0], fold_cols[1])
    fold_idx = (jnp.take(fold_row, my_ext_cols) - (partner_j * width - r)) % n_cols
    landing = (jnp.take(fold_row, partner_ext_cols) - (j * width - r)) % n_cols
    unfold_idx = jnp.zeros((ext_w,), jnp.int32).at[landing].set(jnp.arange(ext_w, dtype=jnp.int32))

    strip_row = np.concatenate([np.arange(edge) // width, np.arange(corner) // r, np.arange(corner) // r])
    strip_col = np.concatenate(
        [r + np.arange(edge) % width, np.arange(corner) % r, width + r + np.arange(corner) % r]
    )

    def strip_cell(row, col):
        return jnp.where(
            col < r,
            edge + row * r + col,
            jnp.where(col >= width + r, edge + corner + row * r + col - width - r, row * width + col - r),
        )

    pole_src = strip_cell(r - 1 - strip_row, jnp.take(fold_idx, strip_col))
    pole_dst = strip_cell(r - 1 - strip_row, jnp.take(unfold_idx, strip_col))

    def pair(a, b):
        return jnp.stack([a, b])

    kf = keys.reshape(cells, features)
    vf = values.reshape(cells, features)

    def cols(x, a, b):
        return x[:, a:b].reshape(height * (b - a), features)

    from_left = lax.ppermute(pair(cols(keys, width - r, width), cols(values, width - r, width)), "lon", right_pairs)
    from_right = lax.ppermute(pair(cols(keys, 0, r), cols(values, 0, r)), "lon", left_pairs)
    top_mid = pair(kf[:edge], vf[:edge])
    bottom_mid = pair(kf[cells - edge :], vf[cells - edge :])
    pole_mid = lax.ppermute(jnp.where(at_north, top_mid, bottom_mid), both, pole_pairs)
    n_side = height * r
    top_send = jnp.concatenate([top_mid, from_left[:, :corner], from_right[:, :corner]], axis=1)
    bottom_send = jnp.concatenate(
        [bottom_mid, from_left[:, n_side - corner :], from_right[:, n_side - corner :]], axis=1
    )
    from_above = lax.ppermute(bottom_send, both, down_pairs)
    from_below = lax.ppermute(top_send, both, up_pairs)
    pole_corners = lax.ppermute(
        jnp.where(at_north, top_send[:, edge:], bottom_send[:, edge:]), both, pole_pairs
    )
    pole_mid_rows = jnp.take(pole_mid, pole_src[:edge], axis=1)
    pole_corner_rows = jnp.take(pole_corners, pole_src[edge:] - edge, axis=1)

    q2 = queries.reshape(cells, features)
    g2 = grad_out.reshape(cells, features)
    dq, dk_own, dv_own, top_g, bottom_g, left_g, right_g, pole_g_mid_send, pole_g_corner_send = attention_core(
        q2, g2, kf, vf, from_above, from_below, pole_mid_rows, pole_corner_rows, from_left, from_right, width, n_lat
    )

    up_recv = lax.ppermute(top_g, both, up_pairs)
    down_recv = lax.ppermute(bottom_g, both, down_pairs)
    pole_g_corners = lax.ppermute(pole_g_corner_send, both, pole_pairs)
    unfolded_corners = jnp.take(pole_g_corners, pole_dst[edge:] - edge, axis=1)
    zero_mid = jnp.zeros_like(up_recv[:, :edge])
    add_top = jnp.where(
        at_north, jnp.concatenate([zero_mid, unfolded_corners], axis=1), down_recv
    ).astype(f32)
    add_bottom = jnp.where(
        at_south, jnp.concatenate([zero_mid, unfolded_corners], axis=1), up_recv
    ).astype(f32)

    def side_send(g, first):
        pads_top = [(0, 0), (0, n_side - corner), (0, 0)]
        pads_bottom = [(0, 0), (n_side - corner, 0), (0, 0)]
        return (
            g
            + jnp.pad(add_top[:, first : first + corner], pads_top)
            + jnp.pad(add_bottom[:, first : first + corner], pads_bottom)
        ).astype(bf16)

    back_right = lax.ppermute(side_send(left_g, edge), "lon", left_pairs)
    back_left = lax.ppermute(side_send(right_g, edge + corner), "lon", right_pairs)
    pole_g_mid = lax.ppermute(pole_g_mid_send, both, pole_pairs)
    unfolded_mid = jnp.take(pole_g_mid, pole_dst[:edge], axis=1).astype(f32)
    north_mid = jnp.where(at_north, unfolded_mid, 0.0)
    south_mid = jnp.where(at_south, unfolded_mid, 0.0)

    def final_of(c, own):
        block = own.reshape(height, width, features)
        row_pad = [(0, 0), (0, 0)]
        block = (
            block
            + jnp.pad((add_top[c, :edge] + north_mid[c]).reshape(r, width, features), [(0, height - r)] + row_pad)
            + jnp.pad((add_bottom[c, :edge] + south_mid[c]).reshape(r, width, features), [(height - r, 0)] + row_pad)
            + jnp.pad(
                back_left[c].reshape(height, r, features).astype(f32), [(0, 0), (0, width - r), (0, 0)]
            )
            + jnp.pad(
                back_right[c].reshape(height, r, features).astype(f32), [(0, 0), (width - r, 0), (0, 0)]
            )
        )
        return block.astype(bf16)

    return (dq.reshape(height, width, features), final_of(0, dk_own), final_of(1, dv_own))


def solution(mesh):
    placed = (
        P("lat", "lon", None),
        P("lat", "lon", None),
        P("lat", "lon", None),
        P("lat", "lon", None),
        P(),
    )
    return jax.shard_map(
        on_device,
        mesh=mesh,
        in_specs=placed,
        out_specs=(P("lat", "lon", None), P("lat", "lon", None), P("lat", "lon", None)),
        check_vma=False,
    )
```

```python
import jax
import jax.numpy as jnp
import numpy as np
from jax import lax
from jax.experimental import pallas as pl
from jax.experimental.pallas import tpu as pltpu
from jax.sharding import PartitionSpec as P

HEADS = 16
HEAD_DIM = 64
RADIUS = 4

SPAN = 2 * RADIUS + 1
TILE_ROWS = 8
LANES = 128


def attention_kernel(width, n_lat, *refs):
    (q_ref, g_ref, k_own, v_own, above_in, below_in, pole_mid_in, pole_corner_in, left_in, right_in) = refs[:10]
    (dq_ref, dk_own, dv_own, top_out, bot_out, left_out, right_out, pole_mid_out, pole_corner_out) = refs[10:19]
    bias_ref = refs[19]
    lat = lax.axis_index("lat")
    north = lat == 0
    south = lat == n_lat - 1

    class Strip:
        def __init__(self, neighbour, pole):
            self.neighbour, self.pole = neighbour, pole

        def __getitem__(self, index):
            c, cells, lanes = index
            if cells.start >= edge:
                pole = self.pole_corner_ref[c, pl.ds(cells.start - edge, cells.size), lanes]
            else:
                pole = pole_mid_in[c, cells, lanes]
            return jnp.where(self.pole, pole, self.neighbour[c, cells, lanes])

    top_in = Strip(above_in, north)
    bot_in = Strip(below_in, south)
    top_in.pole_corner_ref = pole_corner_in
    bot_in.pole_corner_ref = pole_corner_in
    scale = HEAD_DIM ** (-0.5)
    r = RADIUS
    tq = TILE_ROWS * width
    main = 2 * TILE_ROWS * width
    side = 2 * TILE_ROWS * r
    tk = main + 2 * side
    edge = r * width
    corner = r * r
    pairs = q_ref.shape[1] // LANES

    qi = lax.broadcasted_iota(jnp.int32, (2 * tq, tk), 0).astype(jnp.float32)
    ki = lax.broadcasted_iota(jnp.int32, (2 * tq, tk), 1).astype(jnp.float32)
    qi = jnp.where(qi >= tq, qi - tq, qi)
    qr = jnp.floor((qi + 0.5) * (1.0 / width))
    qc = qi - width * qr
    in_main = ki < main
    in_left = (ki >= main) & (ki < main + side)
    kk = jnp.where(in_main, ki, jnp.where(in_left, ki - main, ki - main - side))
    per_row = jnp.where(in_main, float(width), float(r))
    kr = jnp.floor((kk + 0.5) / per_row)
    kc = kk - per_row * kr + jnp.where(in_main, float(r), jnp.where(in_left, 0.0, float(width + r)))
    dr = kr - qr
    dc = kc - qc
    ok = (dr >= 0) & (dr <= 2 * r) & (dc >= 0) & (dc <= 2 * r)
    bias_ref[...] = jnp.where(ok, 0.0, -jnp.inf).astype(jnp.float32)

    nt = (((1,), (1,)), ((), ()))
    tn = (((0,), (0,)), ((), ()))

    def both_heads(qab, gab, kp, vp):
        s = lax.dot_general(qab, kp, nt, preferred_element_type=jnp.float32) + bias_ref[...]
        m = jnp.max(s, axis=1, keepdims=True)
        e = jnp.exp(s - m)
        total = jnp.sum(e, axis=1, keepdims=True)
        w = e * (1.0 / total)
        dw = lax.dot_general(gab, vp, nt, preferred_element_type=jnp.float32)
        corr = jnp.sum(w * dw, axis=1, keepdims=True)
        ds = (w * (dw - corr)).astype(jnp.bfloat16)
        return ds, w.astype(jnp.bfloat16)

    def gather_keys(own, c, t, lanes):
        rows = side - corner
        if t == 0:
            parts = [
                top_in[c, pl.ds(0, edge), lanes],
                own[pl.ds(0, main - edge), lanes],
                top_in[c, pl.ds(edge, corner), lanes],
                left_in[c, pl.ds(0, rows), lanes],
                top_in[c, pl.ds(edge + corner, corner), lanes],
                right_in[c, pl.ds(0, rows), lanes],
            ]
        else:
            start = left_in.shape[1] - rows
            parts = [
                own[pl.ds(edge, main - edge), lanes],
                bot_in[c, pl.ds(0, edge), lanes],
                left_in[c, pl.ds(start, rows), lanes],
                bot_in[c, pl.ds(edge, corner), lanes],
                right_in[c, pl.ds(start, rows), lanes],
                bot_in[c, pl.ds(edge + corner, corner), lanes],
            ]
        return jnp.concatenate(parts, axis=0)

    def put_strip(out, c, start, piece, t):
        bf = jnp.bfloat16
        piece = piece.astype(bf)
        out[c, pl.ds(start, piece.shape[0]), lanes_now[0]] = piece
        if start < edge:
            pole_ref, pole_start = pole_mid_out, start
        else:
            pole_ref, pole_start = pole_corner_out, start - edge
        index = (c, pl.ds(pole_start, piece.shape[0]), lanes_now[0])
        if t == 0:
            pole_ref[index] = piece
        else:
            pole_ref[index] = jnp.where(south, piece, pole_ref[index])

    lanes_now = [None]

    def scatter_grads(d, own, c, t, lanes):
        rows = side - corner
        n_side = left_out.shape[1]
        lanes_now[0] = lanes
        if t == 0:
            put_strip(top_out, c, 0, d[:edge], t)
            own[pl.ds(0, main - edge), lanes] = d[edge:main]
            put_strip(top_out, c, edge, d[main : main + corner], t)
            left_out[c, pl.ds(0, rows), lanes] = d[main + corner : main + side]
            put_strip(top_out, c, edge + corner, d[main + side : main + side + corner], t)
            right_out[c, pl.ds(0, rows), lanes] = d[main + side + corner :]
        else:
            shared = main - 2 * edge
            own[pl.ds(edge, shared), lanes] += d[:shared]
            own[pl.ds(edge + shared, edge), lanes] = d[shared : main - edge]
            put_strip(bot_out, c, 0, d[main - edge : main], t)
            start = n_side - rows
            overlap = rows - start
            left_out[c, pl.ds(start, overlap), lanes] += d[main : main + overlap]
            left_out[c, pl.ds(rows, n_side - rows), lanes] = d[main + overlap : main + rows]
            put_strip(bot_out, c, edge, d[main + rows : main + side], t)
            right_out[c, pl.ds(start, overlap), lanes] += d[main + side : main + side + overlap]
            right_out[c, pl.ds(rows, n_side - rows), lanes] = d[main + side + overlap : main + side + rows]
            put_strip(bot_out, c, edge + corner, d[main + side + rows :], t)

    def body(p, carry):
        lanes = pl.ds(pl.multiple_of(p * LANES, LANES), LANES)
        for t in range(2):
            qp = q_ref[pl.ds(t * tq, tq), lanes]
            gp = g_ref[pl.ds(t * tq, tq), lanes]
            kp = gather_keys(k_own, 0, t, lanes)
            vp = gather_keys(v_own, 1, t, lanes)
            lo = lax.broadcasted_iota(jnp.int32, qp.shape, 1) < HEAD_DIM
            zero = jnp.zeros_like(qp)
            qs = qp * jnp.asarray(scale, qp.dtype)
            qab = jnp.concatenate([jnp.where(lo, qs, zero), jnp.where(lo, zero, qs)], axis=0)
            gab = jnp.concatenate([jnp.where(lo, gp, zero), jnp.where(lo, zero, gp)], axis=0)
            ds, w = both_heads(qab, gab, kp, vp)
            dq_ab = jnp.dot(ds, kp, preferred_element_type=jnp.float32)
            dq = jnp.where(lo, dq_ab[:tq], dq_ab[tq:]) * scale
            dq_ref[pl.ds(t * tq, tq), lanes] = dq.astype(dq_ref.dtype)
            dk = lax.dot_general(ds, qab, tn, preferred_element_type=jnp.float32)
            dv = lax.dot_general(w, gab, tn, preferred_element_type=jnp.float32)
            scatter_grads(dk, dk_own, 0, t, lanes)
            scatter_grads(dv, dv_own, 1, t, lanes)
        return carry

    lax.fori_loop(0, pairs, body, 0, unroll=4)


def attention_core(q2, g2, k2, v2, above, below, pole_mid, pole_corner, left_in, right_in, width, n_lat):
    cells, features = q2.shape
    r = RADIUS
    tq = TILE_ROWS * width
    tk = 2 * TILE_ROWS * (width + 2 * r)
    tiles = cells // tq
    assert tiles == 2
    flops = 10 * 2 * tq * tk * LANES * (features // LANES) * tiles
    vmem = pl.BlockSpec(memory_space=pltpu.VMEM)
    f32 = jnp.float32
    outs = (
        jax.ShapeDtypeStruct((cells, features), jnp.bfloat16),
        jax.ShapeDtypeStruct((cells, features), f32),
        jax.ShapeDtypeStruct((cells, features), f32),
        jax.ShapeDtypeStruct(above.shape, jnp.bfloat16),
        jax.ShapeDtypeStruct(below.shape, jnp.bfloat16),
        jax.ShapeDtypeStruct(left_in.shape, f32),
        jax.ShapeDtypeStruct(right_in.shape, f32),
        jax.ShapeDtypeStruct(pole_mid.shape, jnp.bfloat16),
        jax.ShapeDtypeStruct(pole_corner.shape, jnp.bfloat16),
    )
    strips = above.size + below.size + pole_mid.size + pole_corner.size
    in_bytes = 2 * (4 * cells * features + strips + left_in.size + right_in.size)
    out_bytes = 10 * cells * features + 2 * strips + 4 * (left_in.size + right_in.size)
    return pl.pallas_call(
        lambda *refs: attention_kernel(width, n_lat, *refs),
        out_shape=outs,
        in_specs=[vmem] * 10,
        out_specs=tuple([vmem] * 9),
        scratch_shapes=[pltpu.VMEM((2 * tq, tk), jnp.float32)],
        cost_estimate=pl.CostEstimate(
            flops=flops,
            transcendentals=2 * tq * tk * HEADS * tiles,
            bytes_accessed=in_bytes + out_bytes,
        ),
        name="neighbourhood_attention_bwd",
    )(q2, g2, k2, v2, above, below, pole_mid, pole_corner, left_in, right_in)


def on_device(queries, keys, values, grad_out, fold_cols):
    height, width, features = queries.shape
    n_lat = lax.axis_size("lat")
    n_lon = lax.axis_size("lon")
    half = n_lon // 2
    i = lax.axis_index("lat")
    j = lax.axis_index("lon")
    at_north = i == 0
    at_south = i == n_lat - 1
    partner_j = (j + half) % n_lon
    r = RADIUS
    f32 = jnp.float32
    bf16 = jnp.bfloat16
    cells = height * width
    edge = r * width
    corner = r * r

    def flat(a, b):
        return a * n_lon + b

    down_pairs = [(flat(a, b), flat(a + 1, b)) for a in range(n_lat - 1) for b in range(n_lon)]
    up_pairs = [(flat(a + 1, b), flat(a, b)) for a in range(n_lat - 1) for b in range(n_lon)]
    pole_pairs = [(flat(a, b), flat(a, (b + half) % n_lon)) for a in (0, n_lat - 1) for b in range(n_lon)]
    right_pairs = [(b, (b + 1) % n_lon) for b in range(n_lon)]
    left_pairs = [(b, (b - 1) % n_lon) for b in range(n_lon)]
    both = ("lat", "lon")

    ext_w = width + 2 * r
    n_cols = n_lon * width
    my_ext_cols = (j * width - r + jnp.arange(ext_w)) % n_cols
    partner_ext_cols = (partner_j * width - r + jnp.arange(ext_w)) % n_cols
    fold_row = jnp.where(at_north, fold_cols[0], fold_cols[1])
    fold_idx = (jnp.take(fold_row, my_ext_cols) - (partner_j * width - r)) % n_cols
    landing = (jnp.take(fold_row, partner_ext_cols) - (j * width - r)) % n_cols
    unfold_idx = jnp.zeros((ext_w,), jnp.int32).at[landing].set(jnp.arange(ext_w, dtype=jnp.int32))

    strip_row = np.concatenate([np.arange(edge) // width, np.arange(corner) // r, np.arange(corner) // r])
    strip_col = np.concatenate(
        [r + np.arange(edge) % width, np.arange(corner) % r, width + r + np.arange(corner) % r]
    )

    def strip_cell(row, col):
        return jnp.where(
            col < r,
            edge + row * r + col,
            jnp.where(col >= width + r, edge + corner + row * r + col - width - r, row * width + col - r),
        )

    pole_src = strip_cell(r - 1 - strip_row, jnp.take(fold_idx, strip_col))
    pole_dst = strip_cell(r - 1 - strip_row, jnp.take(unfold_idx, strip_col))

    def pair(a, b):
        return jnp.stack([a, b])

    kf = keys.reshape(cells, features)
    vf = values.reshape(cells, features)

    def cols(x, a, b):
        return x[:, a:b].reshape(height * (b - a), features)

    from_left = lax.ppermute(pair(cols(keys, width - r, width), cols(values, width - r, width)), "lon", right_pairs)
    from_right = lax.ppermute(pair(cols(keys, 0, r), cols(values, 0, r)), "lon", left_pairs)
    top_mid = pair(kf[:edge], vf[:edge])
    bottom_mid = pair(kf[cells - edge :], vf[cells - edge :])
    pole_mid = lax.ppermute(jnp.where(at_north, top_mid, bottom_mid), both, pole_pairs)
    n_side = height * r
    top_send = jnp.concatenate([top_mid, from_left[:, :corner], from_right[:, :corner]], axis=1)
    bottom_send = jnp.concatenate(
        [bottom_mid, from_left[:, n_side - corner :], from_right[:, n_side - corner :]], axis=1
    )
    from_above = lax.ppermute(bottom_send, both, down_pairs)
    from_below = lax.ppermute(top_send, both, up_pairs)
    pole_corners = lax.ppermute(
        jnp.where(at_north, top_send[:, edge:], bottom_send[:, edge:]), both, pole_pairs
    )
    pole_mid_rows = jnp.take(pole_mid, pole_src[:edge], axis=1)
    pole_corner_rows = jnp.take(pole_corners, pole_src[edge:] - edge, axis=1)

    q2 = queries.reshape(cells, features)
    g2 = grad_out.reshape(cells, features)
    dq, dk_own, dv_own, top_g, bottom_g, left_g, right_g, pole_g_mid_send, pole_g_corner_send = attention_core(
        q2, g2, kf, vf, from_above, from_below, pole_mid_rows, pole_corner_rows, from_left, from_right, width, n_lat
    )

    up_recv = lax.ppermute(top_g, both, up_pairs)
    down_recv = lax.ppermute(bottom_g, both, down_pairs)
    pole_g_corners = lax.ppermute(pole_g_corner_send, both, pole_pairs)
    unfolded_corners = jnp.take(pole_g_corners, pole_dst[edge:] - edge, axis=1)
    zero_mid = jnp.zeros_like(up_recv[:, :edge])
    add_top = jnp.where(
        at_north, jnp.concatenate([zero_mid, unfolded_corners], axis=1), down_recv
    ).astype(f32)
    add_bottom = jnp.where(
        at_south, jnp.concatenate([zero_mid, unfolded_corners], axis=1), up_recv
    ).astype(f32)

    def side_send(g, first):
        pads_top = [(0, 0), (0, n_side - corner), (0, 0)]
        pads_bottom = [(0, 0), (n_side - corner, 0), (0, 0)]
        return (
            g
            + jnp.pad(add_top[:, first : first + corner], pads_top)
            + jnp.pad(add_bottom[:, first : first + corner], pads_bottom)
        ).astype(bf16)

    back_right = lax.ppermute(side_send(left_g, edge), "lon", left_pairs)
    back_left = lax.ppermute(side_send(right_g, edge + corner), "lon", right_pairs)
    pole_g_mid = lax.ppermute(pole_g_mid_send, both, pole_pairs)
    unfolded_mid = jnp.take(pole_g_mid, pole_dst[:edge], axis=1).astype(f32)
    north_mid = jnp.where(at_north, unfolded_mid, 0.0)
    south_mid = jnp.where(at_south, unfolded_mid, 0.0)

    def final_of(c, own):
        block = own.reshape(height, width, features)
        row_pad = [(0, 0), (0, 0)]
        block = (
            block
            + jnp.pad((add_top[c, :edge] + north_mid[c]).reshape(r, width, features), [(0, height - r)] + row_pad)
            + jnp.pad((add_bottom[c, :edge] + south_mid[c]).reshape(r, width, features), [(height - r, 0)] + row_pad)
            + jnp.pad(
                back_left[c].reshape(height, r, features).astype(f32), [(0, 0), (0, width - r), (0, 0)]
            )
            + jnp.pad(
                back_right[c].reshape(height, r, features).astype(f32), [(0, 0), (width - r, 0), (0, 0)]
            )
        )
        return block.astype(bf16)

    return (dq.reshape(height, width, features), final_of(0, dk_own), final_of(1, dv_own))


def solution(mesh):
    placed = (
        P("lat", "lon", None),
        P("lat", "lon", None),
        P("lat", "lon", None),
        P("lat", "lon", None),
        P(),
    )
    return jax.shard_map(
        on_device,
        mesh=mesh,
        in_specs=placed,
        out_specs=(P("lat", "lon", None), P("lat", "lon", None), P("lat", "lon", None)),
        check_vma=False,
    )
```

```python
import jax
import jax.numpy as jnp
import numpy as np
from jax import lax
from jax.experimental import pallas as pl
from jax.experimental.pallas import tpu as pltpu
from jax.sharding import PartitionSpec as P

HEADS = 16
HEAD_DIM = 64
RADIUS = 4

SPAN = 2 * RADIUS + 1
TILE_ROWS = 8
LANES = 128


def attention_kernel(width, n_lat, *refs):
    (q_ref, g_ref, k_own, v_own, above_in, below_in, pole_mid_in, pole_corner_in, left_in, right_in) = refs[:10]
    (dq_ref, dk_own, dv_own, top_out, bot_out, left_out, right_out, pole_mid_out, pole_corner_out) = refs[10:19]
    bias_ref = refs[19]
    lat = lax.axis_index("lat")
    north = lat == 0
    south = lat == n_lat - 1

    class Strip:
        def __init__(self, neighbour, pole):
            self.neighbour, self.pole = neighbour, pole

        def __getitem__(self, index):
            c, cells, lanes = index
            if cells.start >= edge:
                pole = self.pole_corner_ref[c, pl.ds(cells.start - edge, cells.size), lanes]
            else:
                pole = pole_mid_in[c, cells, lanes]
            return jnp.where(self.pole, pole, self.neighbour[c, cells, lanes])

    top_in = Strip(above_in, north)
    bot_in = Strip(below_in, south)
    top_in.pole_corner_ref = pole_corner_in
    bot_in.pole_corner_ref = pole_corner_in
    scale = HEAD_DIM ** (-0.5)
    r = RADIUS
    tq = TILE_ROWS * width
    main = 2 * TILE_ROWS * width
    side = 2 * TILE_ROWS * r
    tk = main + 2 * side
    edge = r * width
    corner = r * r
    pairs = q_ref.shape[1] // LANES

    qi = lax.broadcasted_iota(jnp.int32, (2 * tq, tk), 0).astype(jnp.float32)
    ki = lax.broadcasted_iota(jnp.int32, (2 * tq, tk), 1).astype(jnp.float32)
    qi = jnp.where(qi >= tq, qi - tq, qi)
    qr = jnp.floor((qi + 0.5) * (1.0 / width))
    qc = qi - width * qr
    in_main = ki < main
    in_left = (ki >= main) & (ki < main + side)
    kk = jnp.where(in_main, ki, jnp.where(in_left, ki - main, ki - main - side))
    per_row = jnp.where(in_main, float(width), float(r))
    kr = jnp.floor((kk + 0.5) / per_row)
    kc = kk - per_row * kr + jnp.where(in_main, float(r), jnp.where(in_left, 0.0, float(width + r)))
    dr = kr - qr
    dc = kc - qc
    ok = (dr >= 0) & (dr <= 2 * r) & (dc >= 0) & (dc <= 2 * r)
    bias_ref[...] = jnp.where(ok, 0.0, -jnp.inf).astype(jnp.float32)

    nt = (((1,), (1,)), ((), ()))
    tn = (((0,), (0,)), ((), ()))

    def both_heads(qab, gab, kp, vp):
        s = lax.dot_general(qab, kp, nt, preferred_element_type=jnp.float32) + bias_ref[...]
        m = jnp.max(s, axis=1, keepdims=True)
        e = jnp.exp(s - m)
        total = jnp.sum(e, axis=1, keepdims=True)
        w = e * (1.0 / total)
        dw = lax.dot_general(gab, vp, nt, preferred_element_type=jnp.float32)
        corr = jnp.sum(w * dw, axis=1, keepdims=True)
        ds = (w * (dw - corr)).astype(jnp.bfloat16)
        return ds, w.astype(jnp.bfloat16)

    def gather_keys(own, c, t, lanes):
        rows = side - corner
        if t == 0:
            parts = [
                top_in[c, pl.ds(0, edge), lanes],
                own[pl.ds(0, main - edge), lanes],
                top_in[c, pl.ds(edge, corner), lanes],
                left_in[c, pl.ds(0, rows), lanes],
                top_in[c, pl.ds(edge + corner, corner), lanes],
                right_in[c, pl.ds(0, rows), lanes],
            ]
        else:
            start = left_in.shape[1] - rows
            parts = [
                own[pl.ds(edge, main - edge), lanes],
                bot_in[c, pl.ds(0, edge), lanes],
                left_in[c, pl.ds(start, rows), lanes],
                bot_in[c, pl.ds(edge, corner), lanes],
                right_in[c, pl.ds(start, rows), lanes],
                bot_in[c, pl.ds(edge + corner, corner), lanes],
            ]
        return jnp.concatenate(parts, axis=0)

    def put_strip(out, c, start, piece, t):
        bf = jnp.bfloat16
        piece = piece.astype(bf)
        out[c, pl.ds(start, piece.shape[0]), lanes_now[0]] = piece
        if start < edge:
            pole_ref, pole_start = pole_mid_out, start
        else:
            pole_ref, pole_start = pole_corner_out, start - edge
        index = (c, pl.ds(pole_start, piece.shape[0]), lanes_now[0])
        if t == 0:
            pole_ref[index] = piece
        else:
            pole_ref[index] = jnp.where(south, piece, pole_ref[index])

    lanes_now = [None]

    def scatter_grads(d, own, c, t, lanes):
        rows = side - corner
        n_side = left_out.shape[1]
        lanes_now[0] = lanes
        if t == 0:
            put_strip(top_out, c, 0, d[:edge], t)
            own[pl.ds(0, main - edge), lanes] = d[edge:main]
            put_strip(top_out, c, edge, d[main : main + corner], t)
            left_out[c, pl.ds(0, rows), lanes] = d[main + corner : main + side]
            put_strip(top_out, c, edge + corner, d[main + side : main + side + corner], t)
            right_out[c, pl.ds(0, rows), lanes] = d[main + side + corner :]
        else:
            shared = main - 2 * edge
            own[pl.ds(edge, shared), lanes] += d[:shared]
            own[pl.ds(edge + shared, edge), lanes] = d[shared : main - edge]
            put_strip(bot_out, c, 0, d[main - edge : main], t)
            start = n_side - rows
            overlap = rows - start
            left_out[c, pl.ds(start, overlap), lanes] += d[main : main + overlap]
            left_out[c, pl.ds(rows, n_side - rows), lanes] = d[main + overlap : main + rows]
            put_strip(bot_out, c, edge, d[main + rows : main + side], t)
            right_out[c, pl.ds(start, overlap), lanes] += d[main + side : main + side + overlap]
            right_out[c, pl.ds(rows, n_side - rows), lanes] = d[main + side + overlap : main + side + rows]
            put_strip(bot_out, c, edge + corner, d[main + side + rows :], t)

    def body(p, carry):
        lanes = pl.ds(pl.multiple_of(p * LANES, LANES), LANES)
        for t in range(2):
            qp = q_ref[pl.ds(t * tq, tq), lanes]
            gp = g_ref[pl.ds(t * tq, tq), lanes]
            kp = gather_keys(k_own, 0, t, lanes)
            vp = gather_keys(v_own, 1, t, lanes)
            lo = lax.broadcasted_iota(jnp.int32, qp.shape, 1) < HEAD_DIM
            zero = jnp.zeros_like(qp)
            qs = qp * jnp.asarray(scale, qp.dtype)
            qab = jnp.concatenate([jnp.where(lo, qs, zero), jnp.where(lo, zero, qs)], axis=0)
            gab = jnp.concatenate([jnp.where(lo, gp, zero), jnp.where(lo, zero, gp)], axis=0)
            ds, w = both_heads(qab, gab, kp, vp)
            dq_ab = jnp.dot(ds, kp, preferred_element_type=jnp.float32)
            dq = jnp.where(lo, dq_ab[:tq], dq_ab[tq:]) * scale
            dq_ref[pl.ds(t * tq, tq), lanes] = dq.astype(dq_ref.dtype)
            dk = lax.dot_general(ds, qab, tn, preferred_element_type=jnp.float32)
            dv = lax.dot_general(w, gab, tn, preferred_element_type=jnp.float32)
            scatter_grads(dk, dk_own, 0, t, lanes)
            scatter_grads(dv, dv_own, 1, t, lanes)
        return carry

    lax.fori_loop(0, pairs, body, 0, unroll=True)


def attention_core(q2, g2, k2, v2, above, below, pole_mid, pole_corner, left_in, right_in, width, n_lat):
    cells, features = q2.shape
    r = RADIUS
    tq = TILE_ROWS * width
    tk = 2 * TILE_ROWS * (width + 2 * r)
    tiles = cells // tq
    assert tiles == 2
    flops = 10 * 2 * tq * tk * LANES * (features // LANES) * tiles
    vmem = pl.BlockSpec(memory_space=pltpu.VMEM)
    f32 = jnp.float32
    outs = (
        jax.ShapeDtypeStruct((cells, features), jnp.bfloat16),
        jax.ShapeDtypeStruct((cells, features), f32),
        jax.ShapeDtypeStruct((cells, features), f32),
        jax.ShapeDtypeStruct(above.shape, jnp.bfloat16),
        jax.ShapeDtypeStruct(below.shape, jnp.bfloat16),
        jax.ShapeDtypeStruct(left_in.shape, f32),
        jax.ShapeDtypeStruct(right_in.shape, f32),
        jax.ShapeDtypeStruct(pole_mid.shape, jnp.bfloat16),
        jax.ShapeDtypeStruct(pole_corner.shape, jnp.bfloat16),
    )
    strips = above.size + below.size + pole_mid.size + pole_corner.size
    in_bytes = 2 * (4 * cells * features + strips + left_in.size + right_in.size)
    out_bytes = 10 * cells * features + 2 * strips + 4 * (left_in.size + right_in.size)
    return pl.pallas_call(
        lambda *refs: attention_kernel(width, n_lat, *refs),
        out_shape=outs,
        in_specs=[vmem] * 10,
        out_specs=tuple([vmem] * 9),
        scratch_shapes=[pltpu.VMEM((2 * tq, tk), jnp.float32)],
        cost_estimate=pl.CostEstimate(
            flops=flops,
            transcendentals=2 * tq * tk * HEADS * tiles,
            bytes_accessed=in_bytes + out_bytes,
        ),
        name="neighbourhood_attention_bwd",
    )(q2, g2, k2, v2, above, below, pole_mid, pole_corner, left_in, right_in)


def on_device(queries, keys, values, grad_out, fold_cols):
    height, width, features = queries.shape
    n_lat = lax.axis_size("lat")
    n_lon = lax.axis_size("lon")
    half = n_lon // 2
    i = lax.axis_index("lat")
    j = lax.axis_index("lon")
    at_north = i == 0
    at_south = i == n_lat - 1
    partner_j = (j + half) % n_lon
    r = RADIUS
    f32 = jnp.float32
    bf16 = jnp.bfloat16
    cells = height * width
    edge = r * width
    corner = r * r

    def flat(a, b):
        return a * n_lon + b

    down_pairs = [(flat(a, b), flat(a + 1, b)) for a in range(n_lat - 1) for b in range(n_lon)]
    up_pairs = [(flat(a + 1, b), flat(a, b)) for a in range(n_lat - 1) for b in range(n_lon)]
    pole_pairs = [(flat(a, b), flat(a, (b + half) % n_lon)) for a in (0, n_lat - 1) for b in range(n_lon)]
    right_pairs = [(b, (b + 1) % n_lon) for b in range(n_lon)]
    left_pairs = [(b, (b - 1) % n_lon) for b in range(n_lon)]
    both = ("lat", "lon")

    ext_w = width + 2 * r
    n_cols = n_lon * width
    my_ext_cols = (j * width - r + jnp.arange(ext_w)) % n_cols
    partner_ext_cols = (partner_j * width - r + jnp.arange(ext_w)) % n_cols
    fold_row = jnp.where(at_north, fold_cols[0], fold_cols[1])
    fold_idx = (jnp.take(fold_row, my_ext_cols) - (partner_j * width - r)) % n_cols
    landing = (jnp.take(fold_row, partner_ext_cols) - (j * width - r)) % n_cols
    unfold_idx = jnp.zeros((ext_w,), jnp.int32).at[landing].set(jnp.arange(ext_w, dtype=jnp.int32))

    strip_row = np.concatenate([np.arange(edge) // width, np.arange(corner) // r, np.arange(corner) // r])
    strip_col = np.concatenate(
        [r + np.arange(edge) % width, np.arange(corner) % r, width + r + np.arange(corner) % r]
    )

    def strip_cell(row, col):
        return jnp.where(
            col < r,
            edge + row * r + col,
            jnp.where(col >= width + r, edge + corner + row * r + col - width - r, row * width + col - r),
        )

    pole_src = strip_cell(r - 1 - strip_row, jnp.take(fold_idx, strip_col))
    pole_dst = strip_cell(r - 1 - strip_row, jnp.take(unfold_idx, strip_col))

    def pair(a, b):
        return jnp.stack([a, b])

    kf = keys.reshape(cells, features)
    vf = values.reshape(cells, features)

    def cols(x, a, b):
        return x[:, a:b].reshape(height * (b - a), features)

    from_left = lax.ppermute(pair(cols(keys, width - r, width), cols(values, width - r, width)), "lon", right_pairs)
    from_right = lax.ppermute(pair(cols(keys, 0, r), cols(values, 0, r)), "lon", left_pairs)
    top_mid = pair(kf[:edge], vf[:edge])
    bottom_mid = pair(kf[cells - edge :], vf[cells - edge :])
    pole_mid = lax.ppermute(jnp.where(at_north, top_mid, bottom_mid), both, pole_pairs)
    n_side = height * r
    top_send = jnp.concatenate([top_mid, from_left[:, :corner], from_right[:, :corner]], axis=1)
    bottom_send = jnp.concatenate(
        [bottom_mid, from_left[:, n_side - corner :], from_right[:, n_side - corner :]], axis=1
    )
    from_above = lax.ppermute(bottom_send, both, down_pairs)
    from_below = lax.ppermute(top_send, both, up_pairs)
    pole_corners = lax.ppermute(
        jnp.where(at_north, top_send[:, edge:], bottom_send[:, edge:]), both, pole_pairs
    )
    pole_mid_rows = jnp.take(pole_mid, pole_src[:edge], axis=1)
    pole_corner_rows = jnp.take(pole_corners, pole_src[edge:] - edge, axis=1)

    q2 = queries.reshape(cells, features)
    g2 = grad_out.reshape(cells, features)
    dq, dk_own, dv_own, top_g, bottom_g, left_g, right_g, pole_g_mid_send, pole_g_corner_send = attention_core(
        q2, g2, kf, vf, from_above, from_below, pole_mid_rows, pole_corner_rows, from_left, from_right, width, n_lat
    )

    up_recv = lax.ppermute(top_g, both, up_pairs)
    down_recv = lax.ppermute(bottom_g, both, down_pairs)
    pole_g_corners = lax.ppermute(pole_g_corner_send, both, pole_pairs)
    unfolded_corners = jnp.take(pole_g_corners, pole_dst[edge:] - edge, axis=1)
    zero_mid = jnp.zeros_like(up_recv[:, :edge])
    add_top = jnp.where(
        at_north, jnp.concatenate([zero_mid, unfolded_corners], axis=1), down_recv
    ).astype(f32)
    add_bottom = jnp.where(
        at_south, jnp.concatenate([zero_mid, unfolded_corners], axis=1), up_recv
    ).astype(f32)

    def side_send(g, first):
        pads_top = [(0, 0), (0, n_side - corner), (0, 0)]
        pads_bottom = [(0, 0), (n_side - corner, 0), (0, 0)]
        return (
            g
            + jnp.pad(add_top[:, first : first + corner], pads_top)
            + jnp.pad(add_bottom[:, first : first + corner], pads_bottom)
        ).astype(bf16)

    back_right = lax.ppermute(side_send(left_g, edge), "lon", left_pairs)
    back_left = lax.ppermute(side_send(right_g, edge + corner), "lon", right_pairs)
    pole_g_mid = lax.ppermute(pole_g_mid_send, both, pole_pairs)
    unfolded_mid = jnp.take(pole_g_mid, pole_dst[:edge], axis=1).astype(f32)
    north_mid = jnp.where(at_north, unfolded_mid, 0.0)
    south_mid = jnp.where(at_south, unfolded_mid, 0.0)

    def final_of(c, own):
        block = own.reshape(height, width, features)
        row_pad = [(0, 0), (0, 0)]
        block = (
            block
            + jnp.pad((add_top[c, :edge] + north_mid[c]).reshape(r, width, features), [(0, height - r)] + row_pad)
            + jnp.pad((add_bottom[c, :edge] + south_mid[c]).reshape(r, width, features), [(height - r, 0)] + row_pad)
            + jnp.pad(
                back_left[c].reshape(height, r, features).astype(f32), [(0, 0), (0, width - r), (0, 0)]
            )
            + jnp.pad(
                back_right[c].reshape(height, r, features).astype(f32), [(0, 0), (width - r, 0), (0, 0)]
            )
        )
        return block.astype(bf16)

    return (dq.reshape(height, width, features), final_of(0, dk_own), final_of(1, dv_own))


def solution(mesh):
    placed = (
        P("lat", "lon", None),
        P("lat", "lon", None),
        P("lat", "lon", None),
        P("lat", "lon", None),
        P(),
    )
    return jax.shard_map(
        on_device,
        mesh=mesh,
        in_specs=placed,
        out_specs=(P("lat", "lon", None), P("lat", "lon", None), P("lat", "lon", None)),
        check_vma=False,
    )
```

```python
import jax
import jax.numpy as jnp
import numpy as np
from jax import lax
from jax.experimental import pallas as pl
from jax.experimental.pallas import tpu as pltpu
from jax.sharding import PartitionSpec as P

HEADS = 16
HEAD_DIM = 64
RADIUS = 4

SPAN = 2 * RADIUS + 1
TILE_ROWS = 8
LANES = 128


def attention_kernel(width, n_lat, *refs):
    (q_ref, g_ref, k_own, v_own, above_in, below_in, pole_mid_in, pole_corner_in, left_in, right_in) = refs[:10]
    bias_ref = refs[10]
    (dq_ref, dk_own, dv_own, top_out, bot_out, left_out, right_out, pole_mid_out, pole_corner_out) = refs[11:20]
    lat = lax.axis_index("lat")
    north = lat == 0
    south = lat == n_lat - 1

    class Strip:
        def __init__(self, neighbour, pole):
            self.neighbour, self.pole = neighbour, pole

        def __getitem__(self, index):
            c, cells, lanes = index
            if cells.start >= edge:
                pole = self.pole_corner_ref[c, pl.ds(cells.start - edge, cells.size), lanes]
            else:
                pole = pole_mid_in[c, cells, lanes]
            return jnp.where(self.pole, pole, self.neighbour[c, cells, lanes])

    top_in = Strip(above_in, north)
    bot_in = Strip(below_in, south)
    top_in.pole_corner_ref = pole_corner_in
    bot_in.pole_corner_ref = pole_corner_in
    scale = HEAD_DIM ** (-0.5)
    r = RADIUS
    tq = TILE_ROWS * width
    main = 2 * TILE_ROWS * width
    side = 2 * TILE_ROWS * r
    tk = main + 2 * side
    edge = r * width
    corner = r * r
    pairs = q_ref.shape[1] // LANES

    nt = (((1,), (1,)), ((), ()))
    tn = (((0,), (0,)), ((), ()))

    def both_heads(qab, gab, kp, vp):
        s = lax.dot_general(qab, kp, nt, preferred_element_type=jnp.float32) + bias_ref[...]
        m = jnp.max(s, axis=1, keepdims=True)
        e = jnp.exp(s - m)
        total = jnp.sum(e, axis=1, keepdims=True)
        w = e * (1.0 / total)
        dw = lax.dot_general(gab, vp, nt, preferred_element_type=jnp.float32)
        corr = jnp.sum(w * dw, axis=1, keepdims=True)
        ds = (w * (dw - corr)).astype(jnp.bfloat16)
        return ds, w.astype(jnp.bfloat16)

    def gather_keys(own, c, t, lanes):
        rows = side - corner
        if t == 0:
            parts = [
                top_in[c, pl.ds(0, edge), lanes],
                own[pl.ds(0, main - edge), lanes],
                top_in[c, pl.ds(edge, corner), lanes],
                left_in[c, pl.ds(0, rows), lanes],
                top_in[c, pl.ds(edge + corner, corner), lanes],
                right_in[c, pl.ds(0, rows), lanes],
            ]
        else:
            start = left_in.shape[1] - rows
            parts = [
                own[pl.ds(edge, main - edge), lanes],
                bot_in[c, pl.ds(0, edge), lanes],
                left_in[c, pl.ds(start, rows), lanes],
                bot_in[c, pl.ds(edge, corner), lanes],
                right_in[c, pl.ds(start, rows), lanes],
                bot_in[c, pl.ds(edge + corner, corner), lanes],
            ]
        return jnp.concatenate(parts, axis=0)

    def put_strip(out, c, start, piece, t):
        bf = jnp.bfloat16
        piece = piece.astype(bf)
        out[c, pl.ds(start, piece.shape[0]), lanes_now[0]] = piece
        if start < edge:
            pole_ref, pole_start = pole_mid_out, start
        else:
            pole_ref, pole_start = pole_corner_out, start - edge
        index = (c, pl.ds(pole_start, piece.shape[0]), lanes_now[0])
        if t == 0:
            pole_ref[index] = piece
        else:
            pole_ref[index] = jnp.where(south, piece, pole_ref[index])

    lanes_now = [None]

    def scatter_grads(d, own, c, t, lanes):
        rows = side - corner
        n_side = left_out.shape[1]
        lanes_now[0] = lanes
        if t == 0:
            put_strip(top_out, c, 0, d[:edge], t)
            own[pl.ds(0, main - edge), lanes] = d[edge:main]
            put_strip(top_out, c, edge, d[main : main + corner], t)
            left_out[c, pl.ds(0, rows), lanes] = d[main + corner : main + side]
            put_strip(top_out, c, edge + corner, d[main + side : main + side + corner], t)
            right_out[c, pl.ds(0, rows), lanes] = d[main + side + corner :]
        else:
            shared = main - 2 * edge
            own[pl.ds(edge, shared), lanes] += d[:shared]
            own[pl.ds(edge + shared, edge), lanes] = d[shared : main - edge]
            put_strip(bot_out, c, 0, d[main - edge : main], t)
            start = n_side - rows
            overlap = rows - start
            left_out[c, pl.ds(start, overlap), lanes] += d[main : main + overlap]
            left_out[c, pl.ds(rows, n_side - rows), lanes] = d[main + overlap : main + rows]
            put_strip(bot_out, c, edge, d[main + rows : main + side], t)
            right_out[c, pl.ds(start, overlap), lanes] += d[main + side : main + side + overlap]
            right_out[c, pl.ds(rows, n_side - rows), lanes] = d[main + side + overlap : main + side + rows]
            put_strip(bot_out, c, edge + corner, d[main + side + rows :], t)

    def body(p, carry):
        lanes = pl.ds(pl.multiple_of(p * LANES, LANES), LANES)
        for t in range(2):
            qp = q_ref[pl.ds(t * tq, tq), lanes]
            gp = g_ref[pl.ds(t * tq, tq), lanes]
            kp = gather_keys(k_own, 0, t, lanes)
            vp = gather_keys(v_own, 1, t, lanes)
            lo = lax.broadcasted_iota(jnp.int32, qp.shape, 1) < HEAD_DIM
            zero = jnp.zeros_like(qp)
            qs = qp * jnp.asarray(scale, qp.dtype)
            qab = jnp.concatenate([jnp.where(lo, qs, zero), jnp.where(lo, zero, qs)], axis=0)
            gab = jnp.concatenate([jnp.where(lo, gp, zero), jnp.where(lo, zero, gp)], axis=0)
            ds, w = both_heads(qab, gab, kp, vp)
            dq_ab = jnp.dot(ds, kp, preferred_element_type=jnp.float32)
            dq = jnp.where(lo, dq_ab[:tq], dq_ab[tq:]) * scale
            dq_ref[pl.ds(t * tq, tq), lanes] = dq.astype(dq_ref.dtype)
            dk = lax.dot_general(ds, qab, tn, preferred_element_type=jnp.float32)
            dv = lax.dot_general(w, gab, tn, preferred_element_type=jnp.float32)
            scatter_grads(dk, dk_own, 0, t, lanes)
            scatter_grads(dv, dv_own, 1, t, lanes)
        return carry

    lax.fori_loop(0, pairs, body, 0, unroll=True)


def window_bias(width):
    r = RADIUS
    tq = TILE_ROWS * width
    main = 2 * TILE_ROWS * width
    side = 2 * TILE_ROWS * r
    q = np.arange(2 * tq)[:, None] % tq
    k = np.arange(main + 2 * side)[None, :]
    in_main = k < main
    in_left = (k >= main) & (k < main + side)
    kk = np.where(in_main, k, np.where(in_left, k - main, k - main - side))
    per_row = np.where(in_main, width, r)
    kr = kk // per_row
    kc = kk % per_row + np.where(in_main, r, np.where(in_left, 0, width + r))
    dr = kr - q // width
    dc = kc - q % width
    ok = (dr >= 0) & (dr <= 2 * r) & (dc >= 0) & (dc <= 2 * r)
    return jnp.asarray(np.where(ok, 0.0, -np.inf).astype(np.float32))


def attention_core(q2, g2, k2, v2, above, below, pole_mid, pole_corner, left_in, right_in, width, n_lat):
    cells, features = q2.shape
    r = RADIUS
    tq = TILE_ROWS * width
    tk = 2 * TILE_ROWS * (width + 2 * r)
    tiles = cells // tq
    assert tiles == 2
    flops = 10 * 2 * tq * tk * LANES * (features // LANES) * tiles
    vmem = pl.BlockSpec(memory_space=pltpu.VMEM)
    f32 = jnp.float32
    outs = (
        jax.ShapeDtypeStruct((cells, features), jnp.bfloat16),
        jax.ShapeDtypeStruct((cells, features), f32),
        jax.ShapeDtypeStruct((cells, features), f32),
        jax.ShapeDtypeStruct(above.shape, jnp.bfloat16),
        jax.ShapeDtypeStruct(below.shape, jnp.bfloat16),
        jax.ShapeDtypeStruct(left_in.shape, f32),
        jax.ShapeDtypeStruct(right_in.shape, f32),
        jax.ShapeDtypeStruct(pole_mid.shape, jnp.bfloat16),
        jax.ShapeDtypeStruct(pole_corner.shape, jnp.bfloat16),
    )
    strips = above.size + below.size + pole_mid.size + pole_corner.size
    in_bytes = 2 * (4 * cells * features + strips + left_in.size + right_in.size)
    out_bytes = 10 * cells * features + 2 * strips + 4 * (left_in.size + right_in.size)
    return pl.pallas_call(
        lambda *refs: attention_kernel(width, n_lat, *refs),
        out_shape=outs,
        in_specs=[vmem] * 11,
        out_specs=tuple([vmem] * 9),
        cost_estimate=pl.CostEstimate(
            flops=flops,
            transcendentals=2 * tq * tk * HEADS * tiles,
            bytes_accessed=in_bytes + out_bytes,
        ),
        name="neighbourhood_attention_bwd",
    )(q2, g2, k2, v2, above, below, pole_mid, pole_corner, left_in, right_in, window_bias(width))


def on_device(queries, keys, values, grad_out, fold_cols):
    height, width, features = queries.shape
    n_lat = lax.axis_size("lat")
    n_lon = lax.axis_size("lon")
    half = n_lon // 2
    i = lax.axis_index("lat")
    j = lax.axis_index("lon")
    at_north = i == 0
    at_south = i == n_lat - 1
    partner_j = (j + half) % n_lon
    r = RADIUS
    f32 = jnp.float32
    bf16 = jnp.bfloat16
    cells = height * width
    edge = r * width
    corner = r * r

    def flat(a, b):
        return a * n_lon + b

    down_pairs = [(flat(a, b), flat(a + 1, b)) for a in range(n_lat - 1) for b in range(n_lon)]
    up_pairs = [(flat(a + 1, b), flat(a, b)) for a in range(n_lat - 1) for b in range(n_lon)]
    pole_pairs = [(flat(a, b), flat(a, (b + half) % n_lon)) for a in (0, n_lat - 1) for b in range(n_lon)]
    right_pairs = [(b, (b + 1) % n_lon) for b in range(n_lon)]
    left_pairs = [(b, (b - 1) % n_lon) for b in range(n_lon)]
    both = ("lat", "lon")

    ext_w = width + 2 * r
    n_cols = n_lon * width
    my_ext_cols = (j * width - r + jnp.arange(ext_w)) % n_cols
    partner_ext_cols = (partner_j * width - r + jnp.arange(ext_w)) % n_cols
    fold_row = jnp.where(at_north, fold_cols[0], fold_cols[1])
    fold_idx = (jnp.take(fold_row, my_ext_cols) - (partner_j * width - r)) % n_cols
    landing = (jnp.take(fold_row, partner_ext_cols) - (j * width - r)) % n_cols
    unfold_idx = jnp.zeros((ext_w,), jnp.int32).at[landing].set(jnp.arange(ext_w, dtype=jnp.int32))

    strip_row = np.concatenate([np.arange(edge) // width, np.arange(corner) // r, np.arange(corner) // r])
    strip_col = np.concatenate(
        [r + np.arange(edge) % width, np.arange(corner) % r, width + r + np.arange(corner) % r]
    )

    def strip_cell(row, col):
        return jnp.where(
            col < r,
            edge + row * r + col,
            jnp.where(col >= width + r, edge + corner + row * r + col - width - r, row * width + col - r),
        )

    pole_src = strip_cell(r - 1 - strip_row, jnp.take(fold_idx, strip_col))
    pole_dst = strip_cell(r - 1 - strip_row, jnp.take(unfold_idx, strip_col))

    def pair(a, b):
        return jnp.stack([a, b])

    kf = keys.reshape(cells, features)
    vf = values.reshape(cells, features)

    def cols(x, a, b):
        return x[:, a:b].reshape(height * (b - a), features)

    from_left = lax.ppermute(pair(cols(keys, width - r, width), cols(values, width - r, width)), "lon", right_pairs)
    from_right = lax.ppermute(pair(cols(keys, 0, r), cols(values, 0, r)), "lon", left_pairs)
    top_mid = pair(kf[:edge], vf[:edge])
    bottom_mid = pair(kf[cells - edge :], vf[cells - edge :])
    pole_mid = lax.ppermute(jnp.where(at_north, top_mid, bottom_mid), both, pole_pairs)
    n_side = height * r
    top_send = jnp.concatenate([top_mid, from_left[:, :corner], from_right[:, :corner]], axis=1)
    bottom_send = jnp.concatenate(
        [bottom_mid, from_left[:, n_side - corner :], from_right[:, n_side - corner :]], axis=1
    )
    from_above = lax.ppermute(bottom_send, both, down_pairs)
    from_below = lax.ppermute(top_send, both, up_pairs)
    pole_corners = lax.ppermute(
        jnp.where(at_north, top_send[:, edge:], bottom_send[:, edge:]), both, pole_pairs
    )
    pole_mid_rows = jnp.take(pole_mid, pole_src[:edge], axis=1)
    pole_corner_rows = jnp.take(pole_corners, pole_src[edge:] - edge, axis=1)

    q2 = queries.reshape(cells, features)
    g2 = grad_out.reshape(cells, features)
    dq, dk_own, dv_own, top_g, bottom_g, left_g, right_g, pole_g_mid_send, pole_g_corner_send = attention_core(
        q2, g2, kf, vf, from_above, from_below, pole_mid_rows, pole_corner_rows, from_left, from_right, width, n_lat
    )

    up_recv = lax.ppermute(top_g, both, up_pairs)
    down_recv = lax.ppermute(bottom_g, both, down_pairs)
    pole_g_corners = lax.ppermute(pole_g_corner_send, both, pole_pairs)
    unfolded_corners = jnp.take(pole_g_corners, pole_dst[edge:] - edge, axis=1)
    zero_mid = jnp.zeros_like(up_recv[:, :edge])
    add_top = jnp.where(
        at_north, jnp.concatenate([zero_mid, unfolded_corners], axis=1), down_recv
    ).astype(f32)
    add_bottom = jnp.where(
        at_south, jnp.concatenate([zero_mid, unfolded_corners], axis=1), up_recv
    ).astype(f32)

    def side_send(g, first):
        pads_top = [(0, 0), (0, n_side - corner), (0, 0)]
        pads_bottom = [(0, 0), (n_side - corner, 0), (0, 0)]
        return (
            g
            + jnp.pad(add_top[:, first : first + corner], pads_top)
            + jnp.pad(add_bottom[:, first : first + corner], pads_bottom)
        ).astype(bf16)

    back_right = lax.ppermute(side_send(left_g, edge), "lon", left_pairs)
    back_left = lax.ppermute(side_send(right_g, edge + corner), "lon", right_pairs)
    pole_g_mid = lax.ppermute(pole_g_mid_send, both, pole_pairs)
    unfolded_mid = jnp.take(pole_g_mid, pole_dst[:edge], axis=1).astype(f32)
    north_mid = jnp.where(at_north, unfolded_mid, 0.0)
    south_mid = jnp.where(at_south, unfolded_mid, 0.0)

    def final_of(c, own):
        block = own.reshape(height, width, features)
        row_pad = [(0, 0), (0, 0)]
        block = (
            block
            + jnp.pad((add_top[c, :edge] + north_mid[c]).reshape(r, width, features), [(0, height - r)] + row_pad)
            + jnp.pad((add_bottom[c, :edge] + south_mid[c]).reshape(r, width, features), [(height - r, 0)] + row_pad)
            + jnp.pad(
                back_left[c].reshape(height, r, features).astype(f32), [(0, 0), (0, width - r), (0, 0)]
            )
            + jnp.pad(
                back_right[c].reshape(height, r, features).astype(f32), [(0, 0), (width - r, 0), (0, 0)]
            )
        )
        return block.astype(bf16)

    return (dq.reshape(height, width, features), final_of(0, dk_own), final_of(1, dv_own))


def solution(mesh):
    placed = (
        P("lat", "lon", None),
        P("lat", "lon", None),
        P("lat", "lon", None),
        P("lat", "lon", None),
        P(),
    )
    return jax.shard_map(
        on_device,
        mesh=mesh,
        in_specs=placed,
        out_specs=(P("lat", "lon", None), P("lat", "lon", None), P("lat", "lon", None)),
        check_vma=False,
    )
```
